32 devices in a mesh: leaf: 4 (over y, x), src: 8 (over z, core).
Axes of the slice: x: 2, y: 2, z: 4, core: 2. Of those that a mesh axis runs over, the one named last changes fastest.
Arguments:
- src_cells: int32 [1024], P('src'), may hold values from 0 to 2047
- rec_cells: int32 [512], P('leaf'), may hold values from 0 to 511
- residual: float32 [1024, 512], P('src', 'leaf'), may hold values from -6 to 6
- pattern: int32 [12, 2], P('leaf'), may hold values 0 or 1
- leaf_lower: bfloat16 [2048, 512], P('leaf'), may hold values from -0.1875 to 0.1875
- leaf_upper: bfloat16 [2048, 512], P('leaf'), may hold values from -0.1875 to 0.1875
- leaf_inv: bfloat16 [16, 128, 128], P('leaf'), may hold values from -0.5 to 0.5
- anc_lower: bfloat16 [1024, 512], P('leaf'), may hold values from -0.125 to 0.125
- anc_upper: bfloat16 [2048, 256], P('leaf'), may hold values from -0.375 to 0.375
- sep_inv: bfloat16 [8, 128, 128], P('leaf'), may hold values from -0.5 to 0.5
- sep_lower: bfloat16 [8, 256, 128], P('leaf'), may hold values from -0.25 to 0.25
- sep_upper: bfloat16 [8, 128, 256], P('leaf'), may hold values from -0.375 to 0.375
Outputs:
- forward_field: float32 [1024, 2048], P('src', 'leaf')
- adjoint_field: float32 [1024, 2048], P('src', 'leaf')
- gradient: float32 [2048], P(('leaf', 'src'))
The draws below stay inside these ranges and needn't reach their ends.
Inputs may be any that keep to these rules, and one draw needn't show every extreme that they name: src_cells holds 512 d + c for a source in interior cell c of subdomain d. rec_cells holds a receiver's cell within the subdomain of its block of 128 entries.
All inputs are finite; a program needn't handle non-finite values. No bound on the sum of `pattern` on one device may be relied on, other than what follows from the above.
Results may differ from the reference program's by a relative error of at most 0.0068.
Values may be sent and summed in bfloat16 or wider, within the bound.
No kernel may reach another device: no remote copies, remote signals or barrier semaphores. Data moves between devices by JAX's collectives and lax.ppermute only.
A program may use at most 64 MiB of HBM per device.

```python
import math
import jax
import jax.numpy as jnp
from jax import lax

BLK = 128
LEAF_BLKS = 4
REC_DEV = 128
LEAF_CELLS = 512
LEVELS = 2
SOURCES = 1024
N_LEAF = 4


def place_ends(array, stream_key, least, top_value):
    spot = [jax.random.randint(jax.random.fold_in(stream_key, axis), (), 0, length) for axis, length in enumerate(array.shape)]
    longest = array.shape.index(max(array.shape))
    neighbour = spot[:longest] + [(spot[longest] + 1) % array.shape[longest]] + spot[longest + 1:]
    return array.at[tuple(spot)].set(least).at[tuple(neighbour)].set(top_value)


def steps_of(stream_key, extent, split, least, largest):
    gain = 1.0
    for axis_at, shards_of in split:
        steps = jax.random.uniform(jax.random.fold_in(jax.random.fold_in(stream_key, 6), axis_at), (shards_of,), jnp.float32, least / len(split), largest / len(split))
        gain = gain * jnp.repeat(jnp.exp(steps), extent[axis_at] // shards_of).reshape((-1,) + (1,) * (len(extent) - 1 - axis_at))
    return gain


def centred(rng, shape, scale, most, cuts=(), kind=jnp.bfloat16):
    entries = jax.random.normal(rng, shape, jnp.float32) * scale
    if len(cuts) > 0:
        entries = steps_of(rng, shape, cuts, -0.22, 0.18) * entries
    return jnp.clip(entries, min=-most, max=most).astype(kind)


def setup_inputs(seed: int = 0) -> dict:
    seeds = jax.random.split(jax.random.key(seed), 13)
    src_cells = place_ends(jax.random.randint(seeds[0], (SOURCES,), 0, N_LEAF * LEAF_CELLS), jax.random.fold_in(seeds[0], 1), 0, (N_LEAF * LEAF_CELLS) - 1).astype(jnp.int32)
    rec_cells = place_ends(jax.random.randint(seeds[1], (N_LEAF * REC_DEV,), 0, LEAF_CELLS), jax.random.fold_in(seeds[1], 1), 0, LEAF_CELLS - 1).astype(jnp.int32)
    residual = centred(seeds[2], (SOURCES, N_LEAF * REC_DEV), 1.0, 6.0, ((0, 8), (1, 4)), jnp.float32)
    pattern = place_ends((jax.random.randint(seeds[3], (N_LEAF * (LEVELS + 1), LEVELS), 0, 4) < 3).astype(jnp.int32), jax.random.fold_in(seeds[3], 1), 0, 1)
    leaf_lower = centred(seeds[4], (N_LEAF * LEAF_CELLS, LEAF_CELLS), (2 * LEAF_CELLS) ** -0.5, 0.1875, ((0, 4),))
    leaf_upper = centred(seeds[5], (N_LEAF * LEAF_CELLS, LEAF_CELLS), (2 * LEAF_CELLS) ** -0.5, 0.1875, ((0, 4),))
    leaf_inv = centred(seeds[6], (N_LEAF * LEAF_BLKS, BLK, BLK), BLK ** -0.5, 0.5, ((0, 4),))
    anc_lower = centred(seeds[7], (N_LEAF * LEVELS * BLK, LEAF_CELLS), (LEAF_CELLS * N_LEAF) ** -0.5, 0.125, ((0, 4),))
    anc_upper = centred(seeds[8], (N_LEAF * LEAF_CELLS, LEVELS * BLK), (LEVELS * BLK) ** -0.5, 0.375, ((0, 4),))
    sep_inv = centred(seeds[9], (N_LEAF * LEVELS, BLK, BLK), BLK ** -0.5, 0.5, ((0, 4),))
    sep_lower = centred(seeds[10], (N_LEAF * LEVELS, LEVELS * BLK, BLK), (BLK * N_LEAF) ** -0.5, 0.25, ((0, 4),))
    sep_upper = centred(seeds[11], (N_LEAF * LEVELS, BLK, LEVELS * BLK), (LEVELS * BLK) ** -0.5, 0.375, ((0, 4),))
    return dict(src_cells=src_cells, rec_cells=rec_cells, residual=residual, pattern=pattern, leaf_lower=leaf_lower, leaf_upper=leaf_upper, leaf_inv=leaf_inv, anc_lower=anc_lower, anc_upper=anc_upper, sep_inv=sep_inv, sep_lower=sep_lower, sep_upper=sep_upper)


def rounded(values):
    return lax.optimization_barrier(values.astype(jnp.bfloat16)).astype(jnp.float32)

def product(layout, former, latter):
    return jnp.einsum(layout, former.astype(jnp.float32), latter.astype(jnp.float32))

def level_masks(present, height, block_size, levels):
    stride = 2 ** height
    level_row = present[::stride, height, :] * (jnp.arange(1, levels + 1) > height).astype(jnp.float32)
    return jnp.repeat(level_row, block_size, axis=1)[:, None, :]

def ancestors(solved, height, levels, block_size, nodes, sources):
    pieces = []
    for upper_level in range(1, levels + 1):
        if upper_level > height:
            pieces.append(jnp.repeat(solved[upper_level], 2 ** (upper_level - height), axis=0))
        else:
            pieces.append(jnp.zeros((nodes, sources, block_size), jnp.float32))
    return jnp.concatenate(pieces, axis=2)

def reference(src_cells, rec_cells, residual, pattern, leaf_lower, leaf_upper, leaf_inv, anc_lower, anc_upper, sep_inv, sep_lower, sep_upper):
    leaves = N_LEAF
    block_size = BLK
    cell_count = LEAF_CELLS
    levels = LEVELS
    block_count = LEAF_BLKS
    present = pattern.reshape(leaves, levels + 1, levels).astype(jnp.float32)
    low_leaf = leaf_lower.reshape(leaves, cell_count, cell_count)
    up_leaf = leaf_upper.reshape(leaves, cell_count, cell_count)
    inv_leaf = leaf_inv.reshape(leaves, block_count, block_size, block_size)
    low_anc = anc_lower.reshape(leaves, levels * block_size, cell_count)
    up_anc = anc_upper.reshape(leaves, cell_count, levels * block_size)
    inv_sep = sep_inv.reshape(leaves, levels, block_size, block_size)
    low_sep = sep_lower.reshape(leaves, levels, levels * block_size, block_size)
    up_sep = sep_upper.reshape(leaves, levels, block_size, levels * block_size)
    all_cells = jnp.arange(leaves * cell_count, dtype=jnp.int32)
    forcing = (src_cells[:, None] == all_cells[None, :]).astype(jnp.float32)
    forcing = forcing.reshape(SOURCES, leaves, cell_count).transpose(1, 0, 2)
    local_cells = jnp.arange(cell_count, dtype=jnp.int32)
    receiver_hits = (rec_cells.reshape(leaves, REC_DEV)[:, :, None] == local_cells[None, None, :]).astype(jnp.float32)
    adjoint_rhs = jnp.einsum('spk,pkc->psc', residual.reshape(SOURCES, leaves, REC_DEV), receiver_hits, precision=lax.Precision.HIGHEST)
    base_mask = level_masks(present, 0, block_size, levels)
    solved = []
    for index in range(block_count):
        segment = forcing[:, :, index * block_size:(index + 1) * block_size]
        if index:
            earlier = rounded(jnp.concatenate(solved, axis=2))
            segment = segment - product('psj,pij->psi', earlier, low_leaf[:, index * block_size:(index + 1) * block_size, :index * block_size])
        solved.append(segment)
    y_leaf = jnp.concatenate(solved, axis=2)
    totals = product('psc,pmc->psm', rounded(y_leaf), low_anc) * base_mask
    y_sep = []
    for height in range(1, levels + 1):
        stride = 2 ** height
        summed = totals[0::2] + totals[1::2]
        y_node = -summed[:, :, (height - 1) * block_size:height * block_size]
        totals = summed + product('nsb,nmb->nsm', rounded(y_node), low_sep[::stride, height - 1]) * level_masks(present, height, block_size, levels)
        y_sep.append(y_node)
    u_sep = {}
    for height in range(levels, 0, -1):
        stride = 2 ** height
        above = ancestors(u_sep, height, levels, block_size, leaves >> height, SOURCES)
        above = above * level_masks(present, height, block_size, levels)
        right_side = y_sep[height - 1] - product('nsm,nbm->nsb', rounded(above), up_sep[::stride, height - 1])
        u_sep[height] = product('nsb,ncb->nsc', rounded(right_side), inv_sep[::stride, height - 1])
    above = ancestors(u_sep, 0, levels, block_size, leaves, SOURCES) * base_mask
    remain = y_leaf - product('psm,pcm->psc', rounded(above), up_anc)
    behind = []
    for index in reversed(range(block_count)):
        segment = remain[:, :, index * block_size:(index + 1) * block_size]
        if behind:
            segment = segment - product('psj,pij->psi', rounded(jnp.concatenate(behind, axis=2)), up_leaf[:, index * block_size:(index + 1) * block_size, (index + 1) * block_size:])
        behind.insert(0, product('psb,pcb->psc', rounded(segment), inv_leaf[:, index]))
    u_leaf = jnp.concatenate(behind, axis=2)
    solved = []
    for index in range(block_count):
        segment = adjoint_rhs[:, :, index * block_size:(index + 1) * block_size]
        if index:
            earlier = rounded(jnp.concatenate(solved, axis=2))
            segment = segment - product('psj,pji->psi', earlier, up_leaf[:, :index * block_size, index * block_size:(index + 1) * block_size])
        solved.append(product('psb,pbc->psc', rounded(segment), inv_leaf[:, index]))
    z_leaf = jnp.concatenate(solved, axis=2)
    totals = product('psc,pcm->psm', rounded(z_leaf), up_anc) * base_mask
    z_sep = []
    for height in range(1, levels + 1):
        stride = 2 ** height
        summed = totals[0::2] + totals[1::2]
        right_side = -summed[:, :, (height - 1) * block_size:height * block_size]
        z_node = product('nsb,nbc->nsc', rounded(right_side), inv_sep[::stride, height - 1])
        totals = summed + product('nsb,nbm->nsm', rounded(z_node), up_sep[::stride, height - 1]) * level_masks(present, height, block_size, levels)
        z_sep.append(z_node)
    lam_sep = {}
    for height in range(levels, 0, -1):
        stride = 2 ** height
        above = ancestors(lam_sep, height, levels, block_size, leaves >> height, SOURCES)
        above = above * level_masks(present, height, block_size, levels)
        lam_sep[height] = z_sep[height - 1] - product('nsm,nmb->nsb', rounded(above), low_sep[::stride, height - 1])
    above = ancestors(lam_sep, 0, levels, block_size, leaves, SOURCES) * base_mask
    remain = z_leaf - product('psm,pmc->psc', rounded(above), low_anc)
    behind = []
    for index in reversed(range(block_count)):
        segment = remain[:, :, index * block_size:(index + 1) * block_size]
        if behind:
            segment = segment - product('psj,pjc->psc', rounded(jnp.concatenate(behind, axis=2)), low_leaf[:, (index + 1) * block_size:, index * block_size:(index + 1) * block_size])
        behind.insert(0, segment)
    lam_leaf = jnp.concatenate(behind, axis=2)
    factor = 1.0 / math.sqrt(SOURCES)
    gradient = (lax.optimization_barrier(jnp.sum(u_leaf * lam_leaf, axis=1)) * factor).reshape(leaves * cell_count)
    forward_field = u_leaf.transpose(1, 0, 2).reshape(SOURCES, leaves * cell_count)
    adjoint_field = lam_leaf.transpose(1, 0, 2).reshape(SOURCES, leaves * cell_count)
    return (forward_field, adjoint_field, gradient)
```

```python
import math

import jax
import jax.numpy as jnp
from jax import lax
from jax.sharding import PartitionSpec as P


def across(former, latter):
    return lax.dot_general(
        former, latter, (((1,), (1,)), ((), ())), preferred_element_type=jnp.float32
    )


def plain_dot(former, latter):
    return jnp.dot(former, latter, preferred_element_type=jnp.float32)


def as_half(values):
    return values.astype(jnp.bfloat16)


def lower_solve(right_side, lower, block_size, block_count):
    solved = []
    for index in range(block_count):
        segment = right_side[:, index * block_size : (index + 1) * block_size]
        if index:
            earlier = as_half(jnp.concatenate(solved, axis=1))
            segment = segment - across(
                earlier, lower[index * block_size : (index + 1) * block_size, : index * block_size]
            )
        solved.append(segment)
    return jnp.concatenate(solved, axis=1)


def upper_solve(right_side, upper, inverse, block_size, block_count):
    behind = []
    for index in reversed(range(block_count)):
        segment = right_side[:, index * block_size : (index + 1) * block_size]
        if behind:
            segment = segment - across(
                as_half(jnp.concatenate(behind, axis=1)),
                upper[index * block_size : (index + 1) * block_size, (index + 1) * block_size :],
            )
        behind.insert(0, across(as_half(segment), inverse[index]))
    return jnp.concatenate(behind, axis=1)


def upper_t_solve(right_side, upper, inverse, block_size, block_count):
    solved = []
    for index in range(block_count):
        segment = right_side[:, index * block_size : (index + 1) * block_size]
        if index:
            earlier = as_half(jnp.concatenate(solved, axis=1))
            segment = segment - plain_dot(
                earlier, upper[: index * block_size, index * block_size : (index + 1) * block_size]
            )
        solved.append(plain_dot(as_half(segment), inverse[index]))
    return jnp.concatenate(solved, axis=1)


def lower_t_solve(right_side, lower, block_size, block_count):
    behind = []
    for index in reversed(range(block_count)):
        segment = right_side[:, index * block_size : (index + 1) * block_size]
        if behind:
            segment = segment - plain_dot(
                as_half(jnp.concatenate(behind, axis=1)),
                lower[(index + 1) * block_size :, index * block_size : (index + 1) * block_size],
            )
        behind.insert(0, segment)
    return jnp.concatenate(behind, axis=1)


def shards(
    src_cells,
    rec_cells,
    residual,
    pattern,
    leaf_lower,
    leaf_upper,
    leaf_inv,
    anc_lower,
    anc_upper,
    sep_inv,
    sep_lower,
    sep_upper,
):
    leaves = lax.axis_size("leaf")
    levels = leaves.bit_length() - 1
    device = lax.axis_index("leaf")
    block_size = leaf_inv.shape[1]
    block_count = leaf_inv.shape[0]
    cell_count = leaf_lower.shape[1]
    source_count = src_cells.shape[0]
    factor = 1.0 / math.sqrt(source_count * lax.axis_size("src"))
    present = pattern.astype(jnp.float32)

    def level_mask(height):
        level_row = present[height] * (jnp.arange(1, levels + 1) > height).astype(jnp.float32)
        return jnp.repeat(level_row, block_size)

    def blocks_of(values):
        return [values[:, k * block_size : (k + 1) * block_size] for k in range(values.shape[1] // block_size)]

    columns = lax.broadcasted_iota(jnp.int32, (source_count, cell_count), 1)
    forcing = (src_cells[:, None] - device * cell_count == columns).astype(jnp.float32)
    receiver_hits = (
        rec_cells[:, None] == lax.broadcasted_iota(jnp.int32, (rec_cells.shape[0], cell_count), 1)
    ).astype(jnp.float32)
    adjoint_rhs = jnp.dot(residual, receiver_hits, precision=lax.Precision.HIGHEST)

    base_mask = level_mask(0)
    y_leaf = lower_solve(forcing, leaf_lower, block_size, block_count)
    z_leaf = upper_t_solve(adjoint_rhs, leaf_upper, leaf_inv, block_size, block_count)
    forward_sums = blocks_of(across(as_half(y_leaf), anc_lower) * base_mask)
    adjoint_sums = blocks_of(plain_dot(as_half(z_leaf), anc_upper) * base_mask)

    lower_panels, upper_panels, inverse_panels = [], [], []
    for height in range(1, levels + 1):
        mask = level_mask(height)[height * block_size :]
        lower_panels.append(sep_lower[height - 1, height * block_size :, :] * mask[:, None].astype(jnp.bfloat16))
        upper_panels.append(sep_upper[height - 1, :, height * block_size :] * mask[None, :].astype(jnp.bfloat16))
        inverse_panels.append(sep_inv[height - 1])

    forward_nodes, adjoint_nodes = [], []
    for height in range(1, levels + 1):
        stride = 1 << (height - 1)
        pairs = [(index, index ^ stride) for index in range(leaves)]
        pieces = list(forward_sums) + list(adjoint_sums)
        for upper_level in range(height, levels + 1):
            pieces.append(lower_panels[upper_level - 1].astype(jnp.float32))
            pieces.extend(block.astype(jnp.float32) for block in blocks_of(upper_panels[upper_level - 1]))
            pieces.append(inverse_panels[upper_level - 1].astype(jnp.float32))
        incoming = lax.ppermute(jnp.concatenate(pieces, axis=0), "leaf", pairs)
        received, row = [], 0
        for piece in pieces:
            received.append(incoming[row : row + piece.shape[0]])
            row += piece.shape[0]
        count = len(forward_sums)
        forward_sums = [mine + theirs for mine, theirs in zip(forward_sums, received[:count])]
        adjoint_sums = [mine + theirs for mine, theirs in zip(adjoint_sums, received[count : 2 * count])]
        received = received[2 * count :]
        for upper_level in range(height, levels + 1):
            place = device % (1 << upper_level)
            take = jnp.logical_and(place >= stride, place < 2 * stride)
            width = levels - upper_level
            lower_in = received[0].astype(jnp.bfloat16)
            upper_in = jnp.concatenate([block.astype(jnp.bfloat16) for block in received[1 : 1 + width]] or [upper_panels[upper_level - 1]], axis=1)
            inverse_in = received[1 + width].astype(jnp.bfloat16)
            received = received[2 + width :]
            lower_panels[upper_level - 1] = jnp.where(take, lower_in, lower_panels[upper_level - 1])
            upper_panels[upper_level - 1] = jnp.where(take, upper_in, upper_panels[upper_level - 1])
            inverse_panels[upper_level - 1] = jnp.where(take, inverse_in, inverse_panels[upper_level - 1])
        forward_node = -forward_sums[0]
        adjoint_node = plain_dot(as_half(-adjoint_sums[0]), inverse_panels[height - 1])
        forward_nodes.append(forward_node)
        adjoint_nodes.append(adjoint_node)
        forward_sums, adjoint_sums = forward_sums[1:], adjoint_sums[1:]
        if forward_sums:
            forward_coupling = blocks_of(across(as_half(forward_node), lower_panels[height - 1]))
            adjoint_coupling = blocks_of(plain_dot(as_half(adjoint_node), upper_panels[height - 1]))
            forward_sums = [total + extra for total, extra in zip(forward_sums, forward_coupling)]
            adjoint_sums = [total + extra for total, extra in zip(adjoint_sums, adjoint_coupling)]

    forward_above, adjoint_above = [], []
    for height in range(levels, 0, -1):
        right_side = forward_nodes[height - 1]
        adjoint_value = adjoint_nodes[height - 1]
        if forward_above:
            right_side = right_side - across(
                as_half(jnp.concatenate(forward_above, axis=1)), upper_panels[height - 1]
            )
            adjoint_value = adjoint_value - plain_dot(
                as_half(jnp.concatenate(adjoint_above, axis=1)), lower_panels[height - 1]
            )
        forward_above.insert(0, across(as_half(right_side), inverse_panels[height - 1]))
        adjoint_above.insert(0, adjoint_value)
    forward_above = jnp.concatenate(forward_above, axis=1)
    adjoint_above = jnp.concatenate(adjoint_above, axis=1)

    forward_remain = y_leaf - across(as_half(forward_above * base_mask), anc_upper)
    forward_field = upper_solve(forward_remain, leaf_upper, leaf_inv, block_size, block_count)
    adjoint_remain = z_leaf - plain_dot(as_half(adjoint_above * base_mask), anc_lower)
    adjoint_field = lower_t_solve(adjoint_remain, leaf_lower, block_size, block_count)
    partial_gradient = jnp.sum(forward_field * adjoint_field, axis=0)
    gradient = lax.psum_scatter(partial_gradient, "src", scatter_dimension=0, tiled=True) * factor
    return (forward_field, adjoint_field, gradient)


def solution(mesh):
    in_specs = (
        P("src"),
        P("leaf"),
        P("src", "leaf"),
        P("leaf", None),
        P("leaf", None),
        P("leaf", None),
        P("leaf", None, None),
        P("leaf", None),
        P("leaf", None),
        P("leaf", None, None),
        P("leaf", None, None),
        P("leaf", None, None),
    )
    out_specs = (P("src", "leaf"), P("src", "leaf"), P(("leaf", "src")))
    return jax.shard_map(shards, mesh=mesh, in_specs=in_specs, out_specs=out_specs, check_vma=False)
```

```python
import math

import jax
import jax.numpy as jnp
from jax import lax
from jax.sharding import PartitionSpec as P


def across(former, latter):
    return lax.dot_general(
        former, latter, (((1,), (1,)), ((), ())), preferred_element_type=jnp.float32
    )


def plain_dot(former, latter):
    return jnp.dot(former, latter, preferred_element_type=jnp.float32)


def as_half(values):
    return values.astype(jnp.bfloat16)


def lower_solve(right_side, lower, block_size, block_count):
    solved = []
    for index in range(block_count):
        segment = right_side[:, index * block_size : (index + 1) * block_size]
        if index:
            earlier = as_half(jnp.concatenate(solved, axis=1))
            segment = segment - across(
                earlier, lower[index * block_size : (index + 1) * block_size, : index * block_size]
            )
        solved.append(segment)
    return jnp.concatenate(solved, axis=1)


def upper_solve(right_side, upper, inverse, block_size, block_count):
    behind = []
    for index in reversed(range(block_count)):
        segment = right_side[:, index * block_size : (index + 1) * block_size]
        if behind:
            segment = segment - across(
                as_half(jnp.concatenate(behind, axis=1)),
                upper[index * block_size : (index + 1) * block_size, (index + 1) * block_size :],
            )
        behind.insert(0, across(as_half(segment), inverse[index]))
    return jnp.concatenate(behind, axis=1)


def upper_t_solve(right_side, upper, inverse, block_size, block_count):
    solved = []
    for index in range(block_count):
        segment = right_side[:, index * block_size : (index + 1) * block_size]
        if index:
            earlier = as_half(jnp.concatenate(solved, axis=1))
            segment = segment - plain_dot(
                earlier, upper[: index * block_size, index * block_size : (index + 1) * block_size]
            )
        solved.append(plain_dot(as_half(segment), inverse[index]))
    return jnp.concatenate(solved, axis=1)


def lower_t_solve(right_side, lower, block_size, block_count):
    behind = []
    for index in reversed(range(block_count)):
        segment = right_side[:, index * block_size : (index + 1) * block_size]
        if behind:
            segment = segment - plain_dot(
                as_half(jnp.concatenate(behind, axis=1)),
                lower[(index + 1) * block_size :, index * block_size : (index + 1) * block_size],
            )
        behind.insert(0, segment)
    return jnp.concatenate(behind, axis=1)


def shards(
    src_cells,
    rec_cells,
    residual,
    pattern,
    leaf_lower,
    leaf_upper,
    leaf_inv,
    anc_lower,
    anc_upper,
    sep_inv,
    sep_lower,
    sep_upper,
):
    leaves = lax.axis_size("leaf")
    levels = leaves.bit_length() - 1
    device = lax.axis_index("leaf")
    block_size = leaf_inv.shape[1]
    block_count = leaf_inv.shape[0]
    cell_count = leaf_lower.shape[1]
    source_count = src_cells.shape[0]
    factor = 1.0 / math.sqrt(source_count * lax.axis_size("src"))
    present = pattern.astype(jnp.float32)

    def level_mask(height):
        level_row = present[height] * (jnp.arange(1, levels + 1) > height).astype(jnp.float32)
        return jnp.repeat(level_row, block_size)

    def blocks_of(values):
        return [values[:, k * block_size : (k + 1) * block_size] for k in range(values.shape[1] // block_size)]

    columns = lax.broadcasted_iota(jnp.int32, (source_count, cell_count), 1)
    forcing = (src_cells[:, None] - device * cell_count == columns).astype(jnp.float32)
    receiver_hits = (
        rec_cells[:, None] == lax.broadcasted_iota(jnp.int32, (rec_cells.shape[0], cell_count), 1)
    ).astype(jnp.float32)
    adjoint_rhs = jnp.dot(residual, receiver_hits, precision=lax.Precision.HIGHEST)

    base_mask = level_mask(0)
    y_leaf = lower_solve(forcing, leaf_lower, block_size, block_count)
    z_leaf = upper_t_solve(adjoint_rhs, leaf_upper, leaf_inv, block_size, block_count)
    forward_sums = blocks_of(across(as_half(y_leaf), anc_lower) * base_mask)
    adjoint_sums = blocks_of(plain_dot(as_half(z_leaf), anc_upper) * base_mask)

    lower_panels, upper_panels, inverse_panels = [], [], []
    for height in range(1, levels + 1):
        mask = level_mask(height)[height * block_size :]
        lower_panels.append(sep_lower[height - 1, height * block_size :, :] * mask[:, None].astype(jnp.bfloat16))
        upper_panels.append(sep_upper[height - 1, :, height * block_size :] * mask[None, :].astype(jnp.bfloat16))
        inverse_panels.append(sep_inv[height - 1])

    def exchange(values, pairs):
        pieces = [piece for piece in values]
        incoming = lax.ppermute(jnp.concatenate(pieces, axis=0), "leaf", pairs)
        received, row = [], 0
        for piece in pieces:
            received.append(incoming[row : row + piece.shape[0]])
            row += piece.shape[0]
        return received

    for height in range(1, levels + 1):
        stride = 1 << (height - 1)
        pairs = [(index, index ^ stride) for index in range(leaves)]
        pieces = []
        for upper_level in range(height, levels + 1):
            pieces.append(lower_panels[upper_level - 1])
            pieces.extend(blocks_of(upper_panels[upper_level - 1]))
            pieces.append(inverse_panels[upper_level - 1])
        received = exchange(pieces, pairs)
        for upper_level in range(height, levels + 1):
            place = device % (1 << upper_level)
            take = jnp.logical_and(place >= stride, place < 2 * stride)
            width = levels - upper_level
            lower_in = received[0]
            upper_in = jnp.concatenate(received[1 : 1 + width] or [upper_panels[upper_level - 1]], axis=1)
            inverse_in = received[1 + width]
            received = received[2 + width :]
            lower_panels[upper_level - 1] = jnp.where(take, lower_in, lower_panels[upper_level - 1])
            upper_panels[upper_level - 1] = jnp.where(take, upper_in, upper_panels[upper_level - 1])
            inverse_panels[upper_level - 1] = jnp.where(take, inverse_in, inverse_panels[upper_level - 1])

    forward_nodes, adjoint_nodes = [], []
    for height in range(1, levels + 1):
        stride = 1 << (height - 1)
        pairs = [(index, index ^ stride) for index in range(leaves)]
        forward_sums = [mine + theirs for mine, theirs in zip(forward_sums, exchange(forward_sums, pairs))]
        forward_node = -forward_sums[0]
        forward_nodes.append(forward_node)
        forward_sums = forward_sums[1:]
        if forward_sums:
            forward_coupling = blocks_of(across(as_half(forward_node), lower_panels[height - 1]))
            forward_sums = [total + extra for total, extra in zip(forward_sums, forward_coupling)]
        adjoint_sums = [mine + theirs for mine, theirs in zip(adjoint_sums, exchange(adjoint_sums, pairs))]
        adjoint_node = plain_dot(as_half(-adjoint_sums[0]), inverse_panels[height - 1])
        adjoint_nodes.append(adjoint_node)
        adjoint_sums = adjoint_sums[1:]
        if adjoint_sums:
            adjoint_coupling = blocks_of(plain_dot(as_half(adjoint_node), upper_panels[height - 1]))
            adjoint_sums = [total + extra for total, extra in zip(adjoint_sums, adjoint_coupling)]

    forward_above, adjoint_above = [], []
    for height in range(levels, 0, -1):
        right_side = forward_nodes[height - 1]
        adjoint_value = adjoint_nodes[height - 1]
        if forward_above:
            right_side = right_side - across(
                as_half(jnp.concatenate(forward_above, axis=1)), upper_panels[height - 1]
            )
            adjoint_value = adjoint_value - plain_dot(
                as_half(jnp.concatenate(adjoint_above, axis=1)), lower_panels[height - 1]
            )
        forward_above.insert(0, across(as_half(right_side), inverse_panels[height - 1]))
        adjoint_above.insert(0, adjoint_value)
    forward_above = jnp.concatenate(forward_above, axis=1)
    adjoint_above = jnp.concatenate(adjoint_above, axis=1)

    forward_remain = y_leaf - across(as_half(forward_above * base_mask), anc_upper)
    forward_field = upper_solve(forward_remain, leaf_upper, leaf_inv, block_size, block_count)
    adjoint_remain = z_leaf - plain_dot(as_half(adjoint_above * base_mask), anc_lower)
    adjoint_field = lower_t_solve(adjoint_remain, leaf_lower, block_size, block_count)
    partial_gradient = jnp.sum(forward_field * adjoint_field, axis=0)
    spread = lax.axis_size("src")
    gathered = lax.all_to_all(partial_gradient.reshape(spread, -1), "src", 0, 0, tiled=True)
    gradient = jnp.sum(gathered, axis=0) * factor
    return (forward_field, adjoint_field, gradient)


def solution(mesh):
    in_specs = (
        P("src"),
        P("leaf"),
        P("src", "leaf"),
        P("leaf", None),
        P("leaf", None),
        P("leaf", None),
        P("leaf", None, None),
        P("leaf", None),
        P("leaf", None),
        P("leaf", None, None),
        P("leaf", None, None),
        P("leaf", None, None),
    )
    out_specs = (P("src", "leaf"), P("src", "leaf"), P(("leaf", "src")))
    return jax.shard_map(shards, mesh=mesh, in_specs=in_specs, out_specs=out_specs, check_vma=False)
```

```python
import math

import jax
import jax.numpy as jnp
from jax import lax
from jax.sharding import PartitionSpec as P


def across(former, latter):
    return lax.dot_general(
        former, latter, (((1,), (1,)), ((), ())), preferred_element_type=jnp.float32
    )


def plain_dot(former, latter):
    return jnp.dot(former, latter, preferred_element_type=jnp.float32)


def as_half(values):
    return values.astype(jnp.bfloat16)


def lower_solve(right_side, lower, block_size, block_count):
    solved = []
    for index in range(block_count):
        segment = right_side[:, index * block_size : (index + 1) * block_size]
        if index:
            earlier = as_half(jnp.concatenate(solved, axis=1))
            segment = segment - across(
                earlier, lower[index * block_size : (index + 1) * block_size, : index * block_size]
            )
        solved.append(segment)
    return jnp.concatenate(solved, axis=1)


def upper_solve(right_side, upper, inverse, block_size, block_count):
    behind = []
    for index in reversed(range(block_count)):
        segment = right_side[:, index * block_size : (index + 1) * block_size]
        if behind:
            segment = segment - across(
                as_half(jnp.concatenate(behind, axis=1)),
                upper[index * block_size : (index + 1) * block_size, (index + 1) * block_size :],
            )
        behind.insert(0, across(as_half(segment), inverse[index]))
    return jnp.concatenate(behind, axis=1)


def upper_t_solve(right_side, upper, inverse, block_size, block_count):
    solved = []
    for index in range(block_count):
        segment = right_side[:, index * block_size : (index + 1) * block_size]
        if index:
            earlier = as_half(jnp.concatenate(solved, axis=1))
            segment = segment - plain_dot(
                earlier, upper[: index * block_size, index * block_size : (index + 1) * block_size]
            )
        solved.append(plain_dot(as_half(segment), inverse[index]))
    return jnp.concatenate(solved, axis=1)


def lower_t_solve(right_side, lower, block_size, block_count):
    behind = []
    for index in reversed(range(block_count)):
        segment = right_side[:, index * block_size : (index + 1) * block_size]
        if behind:
            segment = segment - plain_dot(
                as_half(jnp.concatenate(behind, axis=1)),
                lower[(index + 1) * block_size :, index * block_size : (index + 1) * block_size],
            )
        behind.insert(0, segment)
    return jnp.concatenate(behind, axis=1)


def shards(
    src_cells,
    rec_cells,
    residual,
    pattern,
    leaf_lower,
    leaf_upper,
    leaf_inv,
    anc_lower,
    anc_upper,
    sep_inv,
    sep_lower,
    sep_upper,
):
    leaves = lax.axis_size("leaf")
    levels = leaves.bit_length() - 1
    device = lax.axis_index("leaf")
    block_size = leaf_inv.shape[1]
    block_count = leaf_inv.shape[0]
    cell_count = leaf_lower.shape[1]
    source_count = src_cells.shape[0]
    factor = 1.0 / math.sqrt(source_count * lax.axis_size("src"))
    present = pattern.astype(jnp.float32)

    def level_mask(height):
        level_row = present[height] * (jnp.arange(1, levels + 1) > height).astype(jnp.float32)
        return jnp.repeat(level_row, block_size)

    def blocks_of(values):
        return [values[:, k * block_size : (k + 1) * block_size] for k in range(values.shape[1] // block_size)]

    columns = lax.broadcasted_iota(jnp.int32, (source_count, cell_count), 1)
    forcing = (src_cells[:, None] - device * cell_count == columns).astype(jnp.float32)
    receiver_hits = (
        rec_cells[:, None] == lax.broadcasted_iota(jnp.int32, (rec_cells.shape[0], cell_count), 1)
    ).astype(jnp.float32)
    adjoint_rhs = jnp.dot(residual, receiver_hits, precision=lax.Precision.HIGHEST)

    base_mask = level_mask(0)
    y_leaf = lower_solve(forcing, leaf_lower, block_size, block_count)
    z_leaf = upper_t_solve(adjoint_rhs, leaf_upper, leaf_inv, block_size, block_count)
    forward_sums = blocks_of(across(as_half(y_leaf), anc_lower) * base_mask)
    adjoint_sums = blocks_of(plain_dot(as_half(z_leaf), anc_upper) * base_mask)

    lower_panels, upper_panels, inverse_panels, pattern_rows = [], [], [], []
    for height in range(1, levels + 1):
        lower_panels.append(sep_lower[height - 1, height * block_size :, :])
        upper_panels.append(sep_upper[height - 1, :, height * block_size :])
        inverse_panels.append(sep_inv[height - 1])
        row = pattern[height].astype(jnp.bfloat16)[None, :]
        pattern_rows.append(jnp.pad(row, ((0, 7), (0, block_size - levels))))

    def chain_mask(height):
        level_row = pattern_rows[height - 1][0, :levels].astype(jnp.float32)
        level_row = level_row * (jnp.arange(1, levels + 1) > height).astype(jnp.float32)
        return jnp.repeat(level_row, block_size)[height * block_size :]

    def exchange(values, pairs):
        pieces = [piece for piece in values]
        incoming = lax.ppermute(jnp.concatenate(pieces, axis=0), "leaf", pairs)
        received, row = [], 0
        for piece in pieces:
            received.append(incoming[row : row + piece.shape[0]])
            row += piece.shape[0]
        return received

    for height in range(1, levels + 1):
        stride = 1 << (height - 1)
        pairs = [(index, index ^ stride) for index in range(leaves)]
        pieces = []
        for upper_level in range(height, levels + 1):
            pieces.append(lower_panels[upper_level - 1])
            pieces.extend(blocks_of(upper_panels[upper_level - 1]))
            pieces.append(inverse_panels[upper_level - 1])
            pieces.append(pattern_rows[upper_level - 1])
        received = exchange(pieces, pairs)
        for upper_level in range(height, levels + 1):
            place = device % (1 << upper_level)
            take = jnp.logical_and(place >= stride, place < 2 * stride)
            width = levels - upper_level
            lower_in = received[0]
            upper_in = jnp.concatenate(received[1 : 1 + width] or [upper_panels[upper_level - 1]], axis=1)
            inverse_in = received[1 + width]
            pattern_in = received[2 + width]
            received = received[3 + width :]
            pattern_rows[upper_level - 1] = jnp.where(take, pattern_in, pattern_rows[upper_level - 1])
            lower_panels[upper_level - 1] = jnp.where(take, lower_in, lower_panels[upper_level - 1])
            upper_panels[upper_level - 1] = jnp.where(take, upper_in, upper_panels[upper_level - 1])
            inverse_panels[upper_level - 1] = jnp.where(take, inverse_in, inverse_panels[upper_level - 1])

    forward_nodes, adjoint_nodes = [], []
    for height in range(1, levels + 1):
        stride = 1 << (height - 1)
        pairs = [(index, index ^ stride) for index in range(leaves)]
        forward_sums = [mine + theirs for mine, theirs in zip(forward_sums, exchange(forward_sums, pairs))]
        forward_node = -forward_sums[0]
        forward_nodes.append(forward_node)
        forward_sums = forward_sums[1:]
        if forward_sums:
            forward_coupling = blocks_of(
                across(as_half(forward_node), lower_panels[height - 1]) * chain_mask(height)
            )
            forward_sums = [total + extra for total, extra in zip(forward_sums, forward_coupling)]
        adjoint_sums = [mine + theirs for mine, theirs in zip(adjoint_sums, exchange(adjoint_sums, pairs))]
        adjoint_node = plain_dot(as_half(-adjoint_sums[0]), inverse_panels[height - 1])
        adjoint_nodes.append(adjoint_node)
        adjoint_sums = adjoint_sums[1:]
        if adjoint_sums:
            adjoint_coupling = blocks_of(
                plain_dot(as_half(adjoint_node), upper_panels[height - 1]) * chain_mask(height)
            )
            adjoint_sums = [total + extra for total, extra in zip(adjoint_sums, adjoint_coupling)]

    forward_above, adjoint_above = [], []
    for height in range(levels, 0, -1):
        right_side = forward_nodes[height - 1]
        adjoint_value = adjoint_nodes[height - 1]
        if forward_above:
            right_side = right_side - across(
                as_half(jnp.concatenate(forward_above, axis=1) * chain_mask(height)), upper_panels[height - 1]
            )
            adjoint_value = adjoint_value - plain_dot(
                as_half(jnp.concatenate(adjoint_above, axis=1) * chain_mask(height)), lower_panels[height - 1]
            )
        forward_above.insert(0, across(as_half(right_side), inverse_panels[height - 1]))
        adjoint_above.insert(0, adjoint_value)
    forward_above = jnp.concatenate(forward_above, axis=1)
    adjoint_above = jnp.concatenate(adjoint_above, axis=1)

    forward_remain = y_leaf - across(as_half(forward_above * base_mask), anc_upper)
    forward_field = upper_solve(forward_remain, leaf_upper, leaf_inv, block_size, block_count)
    adjoint_remain = z_leaf - plain_dot(as_half(adjoint_above * base_mask), anc_lower)
    adjoint_field = lower_t_solve(adjoint_remain, leaf_lower, block_size, block_count)
    spread = lax.axis_size("src")
    product_field = (forward_field * adjoint_field).reshape(source_count, spread, cell_count // spread)
    partial_gradient = jnp.sum(product_field, axis=0)
    gathered = lax.all_to_all(partial_gradient, "src", 0, 0, tiled=True)
    gradient = jnp.sum(gathered, axis=0) * factor
    return (forward_field, adjoint_field, gradient)


def solution(mesh):
    in_specs = (
        P("src"),
        P("leaf"),
        P("src", "leaf"),
        P("leaf", None),
        P("leaf", None),
        P("leaf", None),
        P("leaf", None, None),
        P("leaf", None),
        P("leaf", None),
        P("leaf", None, None),
        P("leaf", None, None),
        P("leaf", None, None),
    )
    out_specs = (P("src", "leaf"), P("src", "leaf"), P(("leaf", "src")))
    return jax.shard_map(shards, mesh=mesh, in_specs=in_specs, out_specs=out_specs, check_vma=False)
```

```python
import math

import jax
import numpy as np
import jax.numpy as jnp
from jax import lax
from jax.sharding import PartitionSpec as P


def across(former, latter):
    return lax.dot_general(
        former, latter, (((1,), (1,)), ((), ())), preferred_element_type=jnp.float32
    )


def plain_dot(former, latter):
    return jnp.dot(former, latter, preferred_element_type=jnp.float32)


def as_half(values):
    return values.astype(jnp.bfloat16)


def lower_solve(right_side, lower, block_size, block_count):
    solved = []
    for index in range(block_count):
        segment = right_side[:, index * block_size : (index + 1) * block_size]
        if index:
            earlier = as_half(jnp.concatenate(solved, axis=1))
            segment = segment - across(
                earlier, lower[index * block_size : (index + 1) * block_size, : index * block_size]
            )
        solved.append(segment)
    return jnp.concatenate(solved, axis=1)


def upper_solve(right_side, upper, inverse, block_size, block_count):
    behind = []
    for index in reversed(range(block_count)):
        segment = right_side[:, index * block_size : (index + 1) * block_size]
        if behind:
            segment = segment - across(
                as_half(jnp.concatenate(behind, axis=1)),
                upper[index * block_size : (index + 1) * block_size, (index + 1) * block_size :],
            )
        behind.insert(0, across(as_half(segment), inverse[index]))
    return jnp.concatenate(behind, axis=1)


def upper_t_solve(right_side, upper, inverse, block_size, block_count):
    solved = []
    for index in range(block_count):
        segment = right_side[:, index * block_size : (index + 1) * block_size]
        if index:
            earlier = as_half(jnp.concatenate(solved, axis=1))
            segment = segment - plain_dot(
                earlier, upper[: index * block_size, index * block_size : (index + 1) * block_size]
            )
        solved.append(plain_dot(as_half(segment), inverse[index]))
    return jnp.concatenate(solved, axis=1)


def lower_t_solve(right_side, lower, block_size, block_count):
    behind = []
    for index in reversed(range(block_count)):
        segment = right_side[:, index * block_size : (index + 1) * block_size]
        if behind:
            segment = segment - plain_dot(
                as_half(jnp.concatenate(behind, axis=1)),
                lower[(index + 1) * block_size :, index * block_size : (index + 1) * block_size],
            )
        behind.insert(0, segment)
    return jnp.concatenate(behind, axis=1)


def shards(
    src_cells,
    rec_cells,
    residual,
    pattern,
    leaf_lower,
    leaf_upper,
    leaf_inv,
    anc_lower,
    anc_upper,
    sep_inv,
    sep_lower,
    sep_upper,
):
    leaves = lax.axis_size("leaf")
    levels = leaves.bit_length() - 1
    device = lax.axis_index("leaf")
    block_size = leaf_inv.shape[1]
    block_count = leaf_inv.shape[0]
    cell_count = leaf_lower.shape[1]
    source_count = src_cells.shape[0]
    factor = 1.0 / math.sqrt(source_count * lax.axis_size("src"))
    present = pattern.astype(jnp.float32)

    def level_mask(height):
        level_row = present[height] * (jnp.arange(1, levels + 1) > height).astype(jnp.float32)
        return jnp.repeat(level_row, block_size)

    def blocks_of(values):
        return [values[:, k * block_size : (k + 1) * block_size] for k in range(values.shape[1] // block_size)]

    columns = lax.broadcasted_iota(jnp.int32, (source_count, cell_count), 1)
    forcing = (src_cells[:, None] - device * cell_count == columns).astype(jnp.float32)
    receiver_hits = (
        rec_cells[:, None] == lax.broadcasted_iota(jnp.int32, (rec_cells.shape[0], cell_count), 1)
    ).astype(jnp.float32)
    adjoint_rhs = jnp.dot(residual, receiver_hits, precision=lax.Precision.HIGHEST)

    base_mask = level_mask(0)
    y_leaf = lower_solve(forcing, leaf_lower, block_size, block_count)
    z_leaf = upper_t_solve(adjoint_rhs, leaf_upper, leaf_inv, block_size, block_count)
    forward_sums = blocks_of(across(as_half(y_leaf), anc_lower) * base_mask)
    adjoint_sums = blocks_of(plain_dot(as_half(z_leaf), anc_upper) * base_mask)

    lower_panels, upper_panels, inverse_panels, pattern_rows = [], [], [], []
    for height in range(1, levels + 1):
        lower_panels.append(sep_lower[height - 1, height * block_size :, :])
        upper_panels.append(sep_upper[height - 1, :, height * block_size :])
        inverse_panels.append(sep_inv[height - 1])
        row = pattern[height].astype(jnp.bfloat16)[None, :]
        pattern_rows.append(jnp.pad(row, ((0, 7), (0, block_size - levels))))

    def chain_mask(height):
        level_row = pattern_rows[height - 1][0, :levels].astype(jnp.float32)
        level_row = level_row * (jnp.arange(1, levels + 1) > height).astype(jnp.float32)
        return jnp.repeat(level_row, block_size)[height * block_size :]

    def exchange(values, pairs):
        pieces = [piece for piece in values]
        incoming = lax.ppermute(jnp.concatenate(pieces, axis=0), "leaf", pairs)
        received, row = [], 0
        for piece in pieces:
            received.append(incoming[row : row + piece.shape[0]])
            row += piece.shape[0]
        return received

    pieces, piece_levels = [], []
    for height in range(1, levels + 1):
        node_pieces = [lower_panels[height - 1]] + blocks_of(upper_panels[height - 1])
        node_pieces += [inverse_panels[height - 1], pattern_rows[height - 1]]
        pieces += node_pieces
        piece_levels += [height] * len(node_pieces)
    row_levels = np.concatenate([np.full(piece.shape[0], height) for piece, height in zip(pieces, piece_levels)])
    panel_buffer = jnp.concatenate(pieces, axis=0)
    for height in range(1, levels + 1):
        stride = 1 << (height - 1)
        pairs = [(index, index ^ stride) for index in range(leaves)]
        received = lax.ppermute(panel_buffer, "leaf", pairs)
        takes = [jnp.zeros((), jnp.bool_)]
        for upper_level in range(1, levels + 1):
            place = device % (1 << upper_level)
            takes.append(jnp.logical_and(upper_level >= height, jnp.logical_and(place >= stride, place < 2 * stride)))
        take_rows = jnp.stack(takes)[row_levels]
        panel_buffer = jnp.where(take_rows[:, None], received, panel_buffer)
    row = 0
    for height in range(1, levels + 1):
        width = levels - height
        lower_panels[height - 1] = panel_buffer[row : row + width * block_size]
        row += width * block_size
        if width:
            upper_panels[height - 1] = jnp.concatenate(
                [panel_buffer[row + k * block_size : row + (k + 1) * block_size] for k in range(width)], axis=1
            )
        row += width * block_size
        inverse_panels[height - 1] = panel_buffer[row : row + block_size]
        row += block_size
        pattern_rows[height - 1] = panel_buffer[row : row + 8]
        row += 8

    def exchange(values, pairs):
        incoming = lax.ppermute(jnp.concatenate(values, axis=0), "leaf", pairs)
        return [incoming[k * source_count : (k + 1) * source_count] for k in range(len(values))]

    forward_nodes, adjoint_nodes = [], []
    for height in range(1, levels + 1):
        stride = 1 << (height - 1)
        pairs = [(index, index ^ stride) for index in range(leaves)]
        count = len(forward_sums)
        received = exchange(forward_sums + adjoint_sums, pairs)
        forward_sums = [mine + theirs for mine, theirs in zip(forward_sums, received[:count])]
        adjoint_sums = [mine + theirs for mine, theirs in zip(adjoint_sums, received[count:])]
        forward_node = -forward_sums[0]
        forward_nodes.append(forward_node)
        forward_sums = forward_sums[1:]
        adjoint_node = plain_dot(as_half(-adjoint_sums[0]), inverse_panels[height - 1])
        adjoint_nodes.append(adjoint_node)
        adjoint_sums = adjoint_sums[1:]
        if forward_sums:
            forward_coupling = blocks_of(
                across(as_half(forward_node), lower_panels[height - 1]) * chain_mask(height)
            )
            forward_sums = [total + extra for total, extra in zip(forward_sums, forward_coupling)]
            adjoint_coupling = blocks_of(
                plain_dot(as_half(adjoint_node), upper_panels[height - 1]) * chain_mask(height)
            )
            adjoint_sums = [total + extra for total, extra in zip(adjoint_sums, adjoint_coupling)]

    forward_above, adjoint_above = [], []
    for height in range(levels, 0, -1):
        right_side = forward_nodes[height - 1]
        adjoint_value = adjoint_nodes[height - 1]
        if forward_above:
            right_side = right_side - across(
                as_half(jnp.concatenate(forward_above, axis=1) * chain_mask(height)), upper_panels[height - 1]
            )
            adjoint_value = adjoint_value - plain_dot(
                as_half(jnp.concatenate(adjoint_above, axis=1) * chain_mask(height)), lower_panels[height - 1]
            )
        forward_above.insert(0, across(as_half(right_side), inverse_panels[height - 1]))
        adjoint_above.insert(0, adjoint_value)
    forward_above = jnp.concatenate(forward_above, axis=1)
    adjoint_above = jnp.concatenate(adjoint_above, axis=1)

    forward_remain = y_leaf - across(as_half(forward_above * base_mask), anc_upper)
    forward_field = upper_solve(forward_remain, leaf_upper, leaf_inv, block_size, block_count)
    adjoint_remain = z_leaf - plain_dot(as_half(adjoint_above * base_mask), anc_lower)
    adjoint_field = lower_t_solve(adjoint_remain, leaf_lower, block_size, block_count)
    spread = lax.axis_size("src")
    product_field = (forward_field * adjoint_field).reshape(source_count, spread, cell_count // spread)
    partial_gradient = jnp.sum(product_field, axis=0)
    gathered = lax.all_to_all(partial_gradient, "src", 0, 0, tiled=True)
    gradient = jnp.sum(gathered, axis=0) * factor
    return (forward_field, adjoint_field, gradient)


def solution(mesh):
    in_specs = (
        P("src"),
        P("leaf"),
        P("src", "leaf"),
        P("leaf", None),
        P("leaf", None),
        P("leaf", None),
        P("leaf", None, None),
        P("leaf", None),
        P("leaf", None),
        P("leaf", None, None),
        P("leaf", None, None),
        P("leaf", None, None),
    )
    out_specs = (P("src", "leaf"), P("src", "leaf"), P(("leaf", "src")))
    return jax.shard_map(shards, mesh=mesh, in_specs=in_specs, out_specs=out_specs, check_vma=False)
```

```python
import math

import jax
import jax.numpy as jnp
from jax import lax
from jax.sharding import PartitionSpec as P


def across(former, latter):
    return lax.dot_general(
        former, latter, (((1,), (1,)), ((), ())), preferred_element_type=jnp.float32
    )


def plain_dot(former, latter):
    return jnp.dot(former, latter, preferred_element_type=jnp.float32)


def as_half(values):
    return values.astype(jnp.bfloat16)


def lower_solve(right_side, lower, block_size, block_count):
    solved = []
    for index in range(block_count):
        segment = right_side[:, index * block_size : (index + 1) * block_size]
        if index:
            earlier = as_half(jnp.concatenate(solved, axis=1))
            segment = segment - across(
                earlier, lower[index * block_size : (index + 1) * block_size, : index * block_size]
            )
        solved.append(segment)
    return jnp.concatenate(solved, axis=1)


def upper_solve(right_side, upper, inverse, block_size, block_count):
    behind = []
    for index in reversed(range(block_count)):
        segment = right_side[:, index * block_size : (index + 1) * block_size]
        if behind:
            segment = segment - across(
                as_half(jnp.concatenate(behind, axis=1)),
                upper[index * block_size : (index + 1) * block_size, (index + 1) * block_size :],
            )
        behind.insert(0, across(as_half(segment), inverse[index]))
    return jnp.concatenate(behind, axis=1)


def upper_t_solve(right_side, upper, inverse, block_size, block_count):
    solved = []
    for index in range(block_count):
        segment = right_side[:, index * block_size : (index + 1) * block_size]
        if index:
            earlier = as_half(jnp.concatenate(solved, axis=1))
            segment = segment - plain_dot(
                earlier, upper[: index * block_size, index * block_size : (index + 1) * block_size]
            )
        solved.append(plain_dot(as_half(segment), inverse[index]))
    return jnp.concatenate(solved, axis=1)


def lower_t_solve(right_side, lower, block_size, block_count):
    behind = []
    for index in reversed(range(block_count)):
        segment = right_side[:, index * block_size : (index + 1) * block_size]
        if behind:
            segment = segment - plain_dot(
                as_half(jnp.concatenate(behind, axis=1)),
                lower[(index + 1) * block_size :, index * block_size : (index + 1) * block_size],
            )
        behind.insert(0, segment)
    return jnp.concatenate(behind, axis=1)


def shards(
    src_cells,
    rec_cells,
    residual,
    pattern,
    leaf_lower,
    leaf_upper,
    leaf_inv,
    anc_lower,
    anc_upper,
    sep_inv,
    sep_lower,
    sep_upper,
):
    leaves = lax.axis_size("leaf")
    levels = leaves.bit_length() - 1
    device = lax.axis_index("leaf")
    block_size = leaf_inv.shape[1]
    block_count = leaf_inv.shape[0]
    cell_count = leaf_lower.shape[1]
    source_count = src_cells.shape[0]
    factor = 1.0 / math.sqrt(source_count * lax.axis_size("src"))
    present = pattern.astype(jnp.float32)

    def level_mask(height):
        level_row = present[height] * (jnp.arange(1, levels + 1) > height).astype(jnp.float32)
        return jnp.repeat(level_row, block_size)

    def blocks_of(values):
        return [values[:, k * block_size : (k + 1) * block_size] for k in range(values.shape[1] // block_size)]

    columns = lax.broadcasted_iota(jnp.int32, (source_count, cell_count), 1)
    forcing = (src_cells[:, None] - device * cell_count == columns).astype(jnp.float32)
    receiver_hits = (
        rec_cells[:, None] == lax.broadcasted_iota(jnp.int32, (rec_cells.shape[0], cell_count), 1)
    ).astype(jnp.float32)
    adjoint_rhs = jnp.dot(residual, receiver_hits, precision=lax.Precision.HIGHEST)

    base_mask = level_mask(0)
    y_leaf = lower_solve(forcing, leaf_lower, block_size, block_count)
    z_leaf = upper_t_solve(adjoint_rhs, leaf_upper, leaf_inv, block_size, block_count)
    forward_sums = blocks_of(across(as_half(y_leaf), anc_lower) * base_mask)
    adjoint_sums = blocks_of(plain_dot(as_half(z_leaf), anc_upper) * base_mask)

    forward_sums, sep_lower, sep_upper, sep_inv, pattern = lax.optimization_barrier(
        (forward_sums, sep_lower, sep_upper, sep_inv, pattern)
    )
    lower_panels, upper_panels, inverse_panels, pattern_rows = [], [], [], []
    for height in range(1, levels + 1):
        lower_panels.append(sep_lower[height - 1, height * block_size :, :])
        upper_panels.append(sep_upper[height - 1, :, height * block_size :])
        inverse_panels.append(sep_inv[height - 1])
        row = pattern[height].astype(jnp.bfloat16)[None, :]
        pattern_rows.append(jnp.pad(row, ((0, 7), (0, block_size - levels))))

    def chain_mask(height):
        level_row = pattern_rows[height - 1][0, :levels].astype(jnp.float32)
        level_row = level_row * (jnp.arange(1, levels + 1) > height).astype(jnp.float32)
        return jnp.repeat(level_row, block_size)[height * block_size :]

    def exchange(values, pairs):
        pieces = [piece for piece in values]
        incoming = lax.ppermute(jnp.concatenate(pieces, axis=0), "leaf", pairs)
        received, row = [], 0
        for piece in pieces:
            received.append(incoming[row : row + piece.shape[0]])
            row += piece.shape[0]
        return received

    for height in range(1, levels + 1):
        stride = 1 << (height - 1)
        pairs = [(index, index ^ stride) for index in range(leaves)]
        pieces = []
        for upper_level in range(height, levels + 1):
            pieces.append(lower_panels[upper_level - 1])
            pieces.extend(blocks_of(upper_panels[upper_level - 1]))
            pieces.append(inverse_panels[upper_level - 1])
            pieces.append(pattern_rows[upper_level - 1])
        received = exchange(pieces, pairs)
        for upper_level in range(height, levels + 1):
            place = device % (1 << upper_level)
            take = jnp.logical_and(place >= stride, place < 2 * stride)
            width = levels - upper_level
            lower_in = received[0]
            upper_in = jnp.concatenate(received[1 : 1 + width] or [upper_panels[upper_level - 1]], axis=1)
            inverse_in = received[1 + width]
            pattern_in = received[2 + width]
            received = received[3 + width :]
            pattern_rows[upper_level - 1] = jnp.where(take, pattern_in, pattern_rows[upper_level - 1])
            lower_panels[upper_level - 1] = jnp.where(take, lower_in, lower_panels[upper_level - 1])
            upper_panels[upper_level - 1] = jnp.where(take, upper_in, upper_panels[upper_level - 1])
            inverse_panels[upper_level - 1] = jnp.where(take, inverse_in, inverse_panels[upper_level - 1])

    forward_nodes, adjoint_nodes = [], []
    for height in range(1, levels + 1):
        stride = 1 << (height - 1)
        pairs = [(index, index ^ stride) for index in range(leaves)]
        forward_sums = [mine + theirs for mine, theirs in zip(forward_sums, exchange(forward_sums, pairs))]
        forward_node = -forward_sums[0]
        forward_nodes.append(forward_node)
        forward_sums = forward_sums[1:]
        if forward_sums:
            forward_coupling = blocks_of(
                across(as_half(forward_node), lower_panels[height - 1]) * chain_mask(height)
            )
            forward_sums = [total + extra for total, extra in zip(forward_sums, forward_coupling)]
        adjoint_sums = [mine + theirs for mine, theirs in zip(adjoint_sums, exchange(adjoint_sums, pairs))]
        adjoint_node = plain_dot(as_half(-adjoint_sums[0]), inverse_panels[height - 1])
        adjoint_nodes.append(adjoint_node)
        adjoint_sums = adjoint_sums[1:]
        if adjoint_sums:
            adjoint_coupling = blocks_of(
                plain_dot(as_half(adjoint_node), upper_panels[height - 1]) * chain_mask(height)
            )
            adjoint_sums = [total + extra for total, extra in zip(adjoint_sums, adjoint_coupling)]

    forward_above, adjoint_above = [], []
    for height in range(levels, 0, -1):
        right_side = forward_nodes[height - 1]
        adjoint_value = adjoint_nodes[height - 1]
        if forward_above:
            right_side = right_side - across(
                as_half(jnp.concatenate(forward_above, axis=1) * chain_mask(height)), upper_panels[height - 1]
            )
            adjoint_value = adjoint_value - plain_dot(
                as_half(jnp.concatenate(adjoint_above, axis=1) * chain_mask(height)), lower_panels[height - 1]
            )
        forward_above.insert(0, across(as_half(right_side), inverse_panels[height - 1]))
        adjoint_above.insert(0, adjoint_value)
    forward_above = jnp.concatenate(forward_above, axis=1)
    adjoint_above = jnp.concatenate(adjoint_above, axis=1)

    forward_remain = y_leaf - across(as_half(forward_above * base_mask), anc_upper)
    forward_field = upper_solve(forward_remain, leaf_upper, leaf_inv, block_size, block_count)
    adjoint_remain = z_leaf - plain_dot(as_half(adjoint_above * base_mask), anc_lower)
    adjoint_field = lower_t_solve(adjoint_remain, leaf_lower, block_size, block_count)
    spread = lax.axis_size("src")
    product_field = (forward_field * adjoint_field).reshape(source_count, spread, cell_count // spread)
    partial_gradient = jnp.sum(product_field, axis=0)
    gathered = lax.all_to_all(partial_gradient, "src", 0, 0, tiled=True)
    gradient = jnp.sum(gathered, axis=0) * factor
    return (forward_field, adjoint_field, gradient)


def solution(mesh):
    in_specs = (
        P("src"),
        P("leaf"),
        P("src", "leaf"),
        P("leaf", None),
        P("leaf", None),
        P("leaf", None),
        P("leaf", None, None),
        P("leaf", None),
        P("leaf", None),
        P("leaf", None, None),
        P("leaf", None, None),
        P("leaf", None, None),
    )
    out_specs = (P("src", "leaf"), P("src", "leaf"), P(("leaf", "src")))
    return jax.shard_map(shards, mesh=mesh, in_specs=in_specs, out_specs=out_specs, check_vma=False)
```

```python
import math

import jax
import jax.numpy as jnp
from jax import lax
from jax.experimental import pallas as pl
from jax.sharding import PartitionSpec as P


def across(former, latter):
    return lax.dot_general(
        former, latter, (((1,), (1,)), ((), ())), preferred_element_type=jnp.float32
    )


def plain_dot(former, latter):
    return jnp.dot(former, latter, preferred_element_type=jnp.float32)


def as_half(values):
    return values.astype(jnp.bfloat16)


def transposed_dot(former, latter):
    return lax.dot_general(
        former, latter, (((1,), (1,)), ((), ())), preferred_element_type=jnp.float32
    )


def back_kernel(
    y_ref, fa_ref, z_ref, aa_ref, mask_ref, anc_up_ref, anc_lo_ref, up_ref, lo_ref, inv_ref,
    forward_out, adjoint_out, gradient_out,
):
    block_size = inv_ref.shape[1]
    block_count = inv_ref.shape[0]
    mask = mask_ref[...]
    forward_remain = y_ref[...] - transposed_dot(as_half(fa_ref[...] * mask), anc_up_ref[...])
    adjoint_remain = z_ref[...] - plain_dot(as_half(aa_ref[...] * mask), anc_lo_ref[...])
    forward_blocks = [None] * block_count
    adjoint_blocks = [None] * block_count
    for index in reversed(range(block_count)):
        here = slice(index * block_size, (index + 1) * block_size)
        segment = forward_remain[:, here]
        if index < block_count - 1:
            later = jnp.concatenate([as_half(block) for block in forward_blocks[index + 1 :]], axis=1)
            segment = segment - transposed_dot(later, up_ref[here, (index + 1) * block_size :])
        forward_blocks[index] = transposed_dot(as_half(segment), inv_ref[index])
        forward_out[:, here] = forward_blocks[index]
        segment = adjoint_remain[:, here]
        if index < block_count - 1:
            later = jnp.concatenate([as_half(block) for block in adjoint_blocks[index + 1 :]], axis=1)
            segment = segment - plain_dot(later, lo_ref[(index + 1) * block_size :, here])
        adjoint_blocks[index] = segment
        adjoint_out[:, here] = segment
        gradient_out[:, here] = jnp.sum(forward_blocks[index] * segment, axis=0, keepdims=True)


def lower_solve(right_side, lower, block_size, block_count):
    solved = []
    for index in range(block_count):
        segment = right_side[:, index * block_size : (index + 1) * block_size]
        if index:
            earlier = as_half(jnp.concatenate(solved, axis=1))
            segment = segment - across(
                earlier, lower[index * block_size : (index + 1) * block_size, : index * block_size]
            )
        solved.append(segment)
    return jnp.concatenate(solved, axis=1)


def upper_solve(right_side, upper, inverse, block_size, block_count):
    behind = []
    for index in reversed(range(block_count)):
        segment = right_side[:, index * block_size : (index + 1) * block_size]
        if behind:
            segment = segment - across(
                as_half(jnp.concatenate(behind, axis=1)),
                upper[index * block_size : (index + 1) * block_size, (index + 1) * block_size :],
            )
        behind.insert(0, across(as_half(segment), inverse[index]))
    return jnp.concatenate(behind, axis=1)


def upper_t_solve(right_side, upper, inverse, block_size, block_count):
    solved = []
    for index in range(block_count):
        segment = right_side[:, index * block_size : (index + 1) * block_size]
        if index:
            earlier = as_half(jnp.concatenate(solved, axis=1))
            segment = segment - plain_dot(
                earlier, upper[: index * block_size, index * block_size : (index + 1) * block_size]
            )
        solved.append(plain_dot(as_half(segment), inverse[index]))
    return jnp.concatenate(solved, axis=1)


def lower_t_solve(right_side, lower, block_size, block_count):
    behind = []
    for index in reversed(range(block_count)):
        segment = right_side[:, index * block_size : (index + 1) * block_size]
        if behind:
            segment = segment - plain_dot(
                as_half(jnp.concatenate(behind, axis=1)),
                lower[(index + 1) * block_size :, index * block_size : (index + 1) * block_size],
            )
        behind.insert(0, segment)
    return jnp.concatenate(behind, axis=1)


def shards(
    src_cells,
    rec_cells,
    residual,
    pattern,
    leaf_lower,
    leaf_upper,
    leaf_inv,
    anc_lower,
    anc_upper,
    sep_inv,
    sep_lower,
    sep_upper,
):
    leaves = lax.axis_size("leaf")
    levels = leaves.bit_length() - 1
    device = lax.axis_index("leaf")
    block_size = leaf_inv.shape[1]
    block_count = leaf_inv.shape[0]
    cell_count = leaf_lower.shape[1]
    source_count = src_cells.shape[0]
    factor = 1.0 / math.sqrt(source_count * lax.axis_size("src"))
    present = pattern.astype(jnp.float32)

    def level_mask(height):
        level_row = present[height] * (jnp.arange(1, levels + 1) > height).astype(jnp.float32)
        return jnp.repeat(level_row, block_size)

    def blocks_of(values):
        return [values[:, k * block_size : (k + 1) * block_size] for k in range(values.shape[1] // block_size)]

    columns = lax.broadcasted_iota(jnp.int32, (source_count, cell_count), 1)
    forcing = (src_cells[:, None] - device * cell_count == columns).astype(jnp.float32)
    receiver_hits = (
        rec_cells[:, None] == lax.broadcasted_iota(jnp.int32, (rec_cells.shape[0], cell_count), 1)
    ).astype(jnp.float32)
    adjoint_rhs = jnp.dot(residual, receiver_hits, precision=lax.Precision.HIGHEST)

    base_mask = level_mask(0)
    y_leaf = lower_solve(forcing, leaf_lower, block_size, block_count)
    z_leaf = upper_t_solve(adjoint_rhs, leaf_upper, leaf_inv, block_size, block_count)
    forward_sums = blocks_of(across(as_half(y_leaf), anc_lower) * base_mask)
    adjoint_sums = blocks_of(plain_dot(as_half(z_leaf), anc_upper) * base_mask)

    lower_panels, upper_panels, inverse_panels, pattern_rows = [], [], [], []
    for height in range(1, levels + 1):
        lower_panels.append(sep_lower[height - 1, height * block_size :, :])
        upper_panels.append(sep_upper[height - 1, :, height * block_size :])
        inverse_panels.append(sep_inv[height - 1])
        row = pattern[height].astype(jnp.bfloat16)[None, :]
        pattern_rows.append(jnp.pad(row, ((0, 7), (0, block_size - levels))))

    def chain_mask(height):
        level_row = pattern_rows[height - 1][0, :levels].astype(jnp.float32)
        level_row = level_row * (jnp.arange(1, levels + 1) > height).astype(jnp.float32)
        return jnp.repeat(level_row, block_size)[height * block_size :]

    def exchange(values, pairs):
        pieces = [piece for piece in values]
        incoming = lax.ppermute(jnp.concatenate(pieces, axis=0), "leaf", pairs)
        received, row = [], 0
        for piece in pieces:
            received.append(incoming[row : row + piece.shape[0]])
            row += piece.shape[0]
        return received

    for height in range(1, levels + 1):
        stride = 1 << (height - 1)
        pairs = [(index, index ^ stride) for index in range(leaves)]
        pieces = []
        for upper_level in range(height, levels + 1):
            pieces.append(lower_panels[upper_level - 1])
            pieces.extend(blocks_of(upper_panels[upper_level - 1]))
            pieces.append(inverse_panels[upper_level - 1])
            pieces.append(pattern_rows[upper_level - 1])
        received = exchange(pieces, pairs)
        for upper_level in range(height, levels + 1):
            place = device % (1 << upper_level)
            take = jnp.logical_and(place >= stride, place < 2 * stride)
            width = levels - upper_level
            lower_in = received[0]
            upper_in = jnp.concatenate(received[1 : 1 + width] or [upper_panels[upper_level - 1]], axis=1)
            inverse_in = received[1 + width]
            pattern_in = received[2 + width]
            received = received[3 + width :]
            pattern_rows[upper_level - 1] = jnp.where(take, pattern_in, pattern_rows[upper_level - 1])
            lower_panels[upper_level - 1] = jnp.where(take, lower_in, lower_panels[upper_level - 1])
            upper_panels[upper_level - 1] = jnp.where(take, upper_in, upper_panels[upper_level - 1])
            inverse_panels[upper_level - 1] = jnp.where(take, inverse_in, inverse_panels[upper_level - 1])

    forward_nodes, adjoint_nodes = [], []
    for height in range(1, levels + 1):
        stride = 1 << (height - 1)
        pairs = [(index, index ^ stride) for index in range(leaves)]
        forward_sums = [mine + theirs for mine, theirs in zip(forward_sums, exchange(forward_sums, pairs))]
        forward_node = -forward_sums[0]
        forward_nodes.append(forward_node)
        forward_sums = forward_sums[1:]
        if forward_sums:
            forward_coupling = blocks_of(
                across(as_half(forward_node), lower_panels[height - 1]) * chain_mask(height)
            )
            forward_sums = [total + extra for total, extra in zip(forward_sums, forward_coupling)]
        adjoint_sums = [mine + theirs for mine, theirs in zip(adjoint_sums, exchange(adjoint_sums, pairs))]
        adjoint_node = plain_dot(as_half(-adjoint_sums[0]), inverse_panels[height - 1])
        adjoint_nodes.append(adjoint_node)
        adjoint_sums = adjoint_sums[1:]
        if adjoint_sums:
            adjoint_coupling = blocks_of(
                plain_dot(as_half(adjoint_node), upper_panels[height - 1]) * chain_mask(height)
            )
            adjoint_sums = [total + extra for total, extra in zip(adjoint_sums, adjoint_coupling)]

    forward_above, adjoint_above = [], []
    for height in range(levels, 0, -1):
        right_side = forward_nodes[height - 1]
        adjoint_value = adjoint_nodes[height - 1]
        if forward_above:
            right_side = right_side - across(
                as_half(jnp.concatenate(forward_above, axis=1) * chain_mask(height)), upper_panels[height - 1]
            )
            adjoint_value = adjoint_value - plain_dot(
                as_half(jnp.concatenate(adjoint_above, axis=1) * chain_mask(height)), lower_panels[height - 1]
            )
        forward_above.insert(0, across(as_half(right_side), inverse_panels[height - 1]))
        adjoint_above.insert(0, adjoint_value)
    forward_above = jnp.concatenate(forward_above, axis=1)
    adjoint_above = jnp.concatenate(adjoint_above, axis=1)

    spread = lax.axis_size("src")
    forward_field, adjoint_field, partial_gradient = pl.pallas_call(
        back_kernel,
        out_shape=(
            jax.ShapeDtypeStruct((source_count, cell_count), jnp.float32),
            jax.ShapeDtypeStruct((source_count, cell_count), jnp.float32),
            jax.ShapeDtypeStruct((1, cell_count), jnp.float32),
        ),
    )(
        y_leaf, forward_above, z_leaf, adjoint_above, base_mask[None, :],
        anc_upper, anc_lower, leaf_upper, leaf_lower, leaf_inv,
    )
    partial_gradient = partial_gradient.reshape(spread, cell_count // spread)
    gathered = lax.all_to_all(partial_gradient, "src", 0, 0, tiled=True)
    gradient = jnp.sum(gathered, axis=0) * factor
    return (forward_field, adjoint_field, gradient)


def solution(mesh):
    in_specs = (
        P("src"),
        P("leaf"),
        P("src", "leaf"),
        P("leaf", None),
        P("leaf", None),
        P("leaf", None),
        P("leaf", None, None),
        P("leaf", None),
        P("leaf", None),
        P("leaf", None, None),
        P("leaf", None, None),
        P("leaf", None, None),
    )
    out_specs = (P("src", "leaf"), P("src", "leaf"), P(("leaf", "src")))
    return jax.shard_map(shards, mesh=mesh, in_specs=in_specs, out_specs=out_specs, check_vma=False)
```

```python
import math

import jax
import jax.numpy as jnp
from jax import lax
from jax.sharding import PartitionSpec as P


def across(former, latter):
    return lax.dot_general(
        former, latter, (((1,), (1,)), ((), ())), preferred_element_type=jnp.float32
    )


def plain_dot(former, latter):
    return jnp.dot(former, latter, preferred_element_type=jnp.float32)


def as_half(values):
    return values.astype(jnp.bfloat16)


def lower_solve(right_side, lower, block_size, block_count):
    solved = []
    for index in range(block_count):
        segment = right_side[:, index * block_size : (index + 1) * block_size]
        if index:
            earlier = as_half(jnp.concatenate(solved, axis=1))
            segment = segment - across(
                earlier, lower[index * block_size : (index + 1) * block_size, : index * block_size]
            )
        solved.append(segment)
    return jnp.concatenate(solved, axis=1)


def upper_solve(right_side, upper, inverse, block_size, block_count):
    behind = []
    for index in reversed(range(block_count)):
        segment = right_side[:, index * block_size : (index + 1) * block_size]
        if behind:
            segment = segment - across(
                as_half(jnp.concatenate(behind, axis=1)),
                upper[index * block_size : (index + 1) * block_size, (index + 1) * block_size :],
            )
        behind.insert(0, across(as_half(segment), inverse[index]))
    return jnp.concatenate(behind, axis=1)


def upper_t_solve(right_side, upper, inverse, block_size, block_count):
    solved = []
    for index in range(block_count):
        segment = right_side[:, index * block_size : (index + 1) * block_size]
        if index:
            earlier = as_half(jnp.concatenate(solved, axis=1))
            segment = segment - plain_dot(
                earlier, upper[: index * block_size, index * block_size : (index + 1) * block_size]
            )
        solved.append(plain_dot(as_half(segment), inverse[index]))
    return jnp.concatenate(solved, axis=1)


def lower_t_solve(right_side, lower, block_size, block_count):
    behind = []
    for index in reversed(range(block_count)):
        segment = right_side[:, index * block_size : (index + 1) * block_size]
        if behind:
            segment = segment - plain_dot(
                as_half(jnp.concatenate(behind, axis=1)),
                lower[(index + 1) * block_size :, index * block_size : (index + 1) * block_size],
            )
        behind.insert(0, segment)
    return jnp.concatenate(behind, axis=1)


def shards(
    src_cells,
    rec_cells,
    residual,
    pattern,
    leaf_lower,
    leaf_upper,
    leaf_inv,
    anc_lower,
    anc_upper,
    sep_inv,
    sep_lower,
    sep_upper,
):
    leaves = lax.axis_size("leaf")
    levels = leaves.bit_length() - 1
    device = lax.axis_index("leaf")
    block_size = leaf_inv.shape[1]
    block_count = leaf_inv.shape[0]
    cell_count = leaf_lower.shape[1]
    source_count = src_cells.shape[0]
    factor = 1.0 / math.sqrt(source_count * lax.axis_size("src"))
    present = pattern.astype(jnp.float32)

    def level_mask(height):
        level_row = present[height] * (jnp.arange(1, levels + 1) > height).astype(jnp.float32)
        return jnp.repeat(level_row, block_size)

    def blocks_of(values):
        return [values[:, k * block_size : (k + 1) * block_size] for k in range(values.shape[1] // block_size)]

    columns = lax.broadcasted_iota(jnp.int32, (source_count, cell_count), 1)
    forcing = (src_cells[:, None] - device * cell_count == columns).astype(jnp.float32)
    receiver_hits = (
        rec_cells[:, None] == lax.broadcasted_iota(jnp.int32, (rec_cells.shape[0], cell_count), 1)
    ).astype(jnp.float32)
    adjoint_rhs = jnp.dot(residual, receiver_hits, precision=lax.Precision.HIGHEST)

    base_mask = level_mask(0)
    y_leaf = lower_solve(forcing, leaf_lower, block_size, block_count)
    z_leaf = upper_t_solve(adjoint_rhs, leaf_upper, leaf_inv, block_size, block_count)
    forward_sums = blocks_of(across(as_half(y_leaf), anc_lower) * base_mask)
    adjoint_sums = blocks_of(plain_dot(as_half(z_leaf), anc_upper) * base_mask)

    lower_panels, upper_panels, inverse_panels, pattern_rows = [], [], [], []
    for height in range(1, levels + 1):
        lower_panels.append(sep_lower[height - 1, height * block_size :, :])
        upper_panels.append(sep_upper[height - 1, :, height * block_size :])
        inverse_panels.append(sep_inv[height - 1])
        row = pattern[height].astype(jnp.bfloat16)[None, :]
        pattern_rows.append(jnp.pad(row, ((0, 7), (0, block_size - levels))))

    def chain_mask(height):
        level_row = pattern_rows[height - 1][0, :levels].astype(jnp.float32)
        level_row = level_row * (jnp.arange(1, levels + 1) > height).astype(jnp.float32)
        return jnp.repeat(level_row, block_size)[height * block_size :]

    def exchange(values, pairs):
        pieces = [piece for piece in values]
        incoming = lax.ppermute(jnp.concatenate(pieces, axis=0), "leaf", pairs)
        received, row = [], 0
        for piece in pieces:
            received.append(incoming[row : row + piece.shape[0]])
            row += piece.shape[0]
        return received

    level_pieces, level_rows = [], [0]
    for height in range(1, levels + 1):
        node_pieces = [lower_panels[height - 1]] + blocks_of(upper_panels[height - 1])
        node_pieces += [inverse_panels[height - 1], pattern_rows[height - 1]]
        level_pieces.append(node_pieces)
        level_rows.append(level_rows[-1] + sum(piece.shape[0] for piece in node_pieces))
    panel_buffer = jnp.concatenate([piece for node_pieces in level_pieces for piece in node_pieces], axis=0)
    received = {}
    for offset in range(1, leaves):
        first = level_rows[offset.bit_length() - 1]
        pairs = [(index, index ^ offset) for index in range(leaves)]
        received[offset] = (first, lax.ppermute(panel_buffer[first:], "leaf", pairs))
    for height in range(1, levels + 1):
        rows = slice(level_rows[height - 1], level_rows[height])
        value = panel_buffer[rows]
        place = device % (1 << height)
        for offset in range(1, 1 << height):
            first, incoming = received[offset]
            piece = incoming[level_rows[height - 1] - first : level_rows[height] - first]
            value = jnp.where(place == offset, piece, value)
        row, width = 0, levels - height
        lower_panels[height - 1] = value[row : row + width * block_size]
        row += width * block_size
        if width:
            upper_panels[height - 1] = jnp.concatenate(
                [value[row + k * block_size : row + (k + 1) * block_size] for k in range(width)], axis=1
            )
        row += width * block_size
        inverse_panels[height - 1] = value[row : row + block_size]
        pattern_rows[height - 1] = value[row + block_size : row + block_size + 8]

    forward_nodes, adjoint_nodes = [], []
    for height in range(1, levels + 1):
        stride = 1 << (height - 1)
        pairs = [(index, index ^ stride) for index in range(leaves)]
        forward_sums = [mine + theirs for mine, theirs in zip(forward_sums, exchange(forward_sums, pairs))]
        forward_node = -forward_sums[0]
        forward_nodes.append(forward_node)
        forward_sums = forward_sums[1:]
        if forward_sums:
            forward_coupling = blocks_of(
                across(as_half(forward_node), lower_panels[height - 1]) * chain_mask(height)
            )
            forward_sums = [total + extra for total, extra in zip(forward_sums, forward_coupling)]
        adjoint_sums = [mine + theirs for mine, theirs in zip(adjoint_sums, exchange(adjoint_sums, pairs))]
        adjoint_node = plain_dot(as_half(-adjoint_sums[0]), inverse_panels[height - 1])
        adjoint_nodes.append(adjoint_node)
        adjoint_sums = adjoint_sums[1:]
        if adjoint_sums:
            adjoint_coupling = blocks_of(
                plain_dot(as_half(adjoint_node), upper_panels[height - 1]) * chain_mask(height)
            )
            adjoint_sums = [total + extra for total, extra in zip(adjoint_sums, adjoint_coupling)]

    forward_above, adjoint_above = [], []
    for height in range(levels, 0, -1):
        right_side = forward_nodes[height - 1]
        adjoint_value = adjoint_nodes[height - 1]
        if forward_above:
            right_side = right_side - across(
                as_half(jnp.concatenate(forward_above, axis=1) * chain_mask(height)), upper_panels[height - 1]
            )
            adjoint_value = adjoint_value - plain_dot(
                as_half(jnp.concatenate(adjoint_above, axis=1) * chain_mask(height)), lower_panels[height - 1]
            )
        forward_above.insert(0, across(as_half(right_side), inverse_panels[height - 1]))
        adjoint_above.insert(0, adjoint_value)
    forward_above = jnp.concatenate(forward_above, axis=1)
    adjoint_above = jnp.concatenate(adjoint_above, axis=1)

    forward_remain = y_leaf - across(as_half(forward_above * base_mask), anc_upper)
    forward_field = upper_solve(forward_remain, leaf_upper, leaf_inv, block_size, block_count)
    adjoint_remain = z_leaf - plain_dot(as_half(adjoint_above * base_mask), anc_lower)
    adjoint_field = lower_t_solve(adjoint_remain, leaf_lower, block_size, block_count)
    spread = lax.axis_size("src")
    product_field = (forward_field * adjoint_field).reshape(source_count, spread, cell_count // spread)
    partial_gradient = jnp.sum(product_field, axis=0)
    gathered = lax.all_to_all(partial_gradient, "src", 0, 0, tiled=True)
    gradient = jnp.sum(gathered, axis=0) * factor
    return (forward_field, adjoint_field, gradient)


def solution(mesh):
    in_specs = (
        P("src"),
        P("leaf"),
        P("src", "leaf"),
        P("leaf", None),
        P("leaf", None),
        P("leaf", None),
        P("leaf", None, None),
        P("leaf", None),
        P("leaf", None),
        P("leaf", None, None),
        P("leaf", None, None),
        P("leaf", None, None),
    )
    out_specs = (P("src", "leaf"), P("src", "leaf"), P(("leaf", "src")))
    return jax.shard_map(shards, mesh=mesh, in_specs=in_specs, out_specs=out_specs, check_vma=False)
```

```python
import math

import jax
import jax.numpy as jnp
from jax import lax
from jax.sharding import PartitionSpec as P


def across(former, latter):
    return lax.dot_general(
        former, latter, (((1,), (1,)), ((), ())), preferred_element_type=jnp.float32
    )


def plain_dot(former, latter):
    return jnp.dot(former, latter, preferred_element_type=jnp.float32)


def as_half(values):
    return values.astype(jnp.bfloat16)


def lower_solve(right_side, lower, block_size, block_count):
    solved = []
    for index in range(block_count):
        segment = right_side[:, index * block_size : (index + 1) * block_size]
        if index:
            earlier = as_half(jnp.concatenate(solved, axis=1))
            segment = segment - across(
                earlier, lower[index * block_size : (index + 1) * block_size, : index * block_size]
            )
        solved.append(segment)
    return jnp.concatenate(solved, axis=1)


def upper_solve(right_side, upper, inverse, block_size, block_count):
    behind = []
    for index in reversed(range(block_count)):
        segment = right_side[:, index * block_size : (index + 1) * block_size]
        if behind:
            segment = segment - across(
                as_half(jnp.concatenate(behind, axis=1)),
                upper[index * block_size : (index + 1) * block_size, (index + 1) * block_size :],
            )
        behind.insert(0, across(as_half(segment), inverse[index]))
    return jnp.concatenate(behind, axis=1)


def upper_t_solve(right_side, upper, inverse, block_size, block_count):
    solved = []
    for index in range(block_count):
        segment = right_side[:, index * block_size : (index + 1) * block_size]
        if index:
            earlier = as_half(jnp.concatenate(solved, axis=1))
            segment = segment - plain_dot(
                earlier, upper[: index * block_size, index * block_size : (index + 1) * block_size]
            )
        solved.append(plain_dot(as_half(segment), inverse[index]))
    return jnp.concatenate(solved, axis=1)


def lower_t_solve(right_side, lower, block_size, block_count):
    behind = []
    for index in reversed(range(block_count)):
        segment = right_side[:, index * block_size : (index + 1) * block_size]
        if behind:
            segment = segment - plain_dot(
                as_half(jnp.concatenate(behind, axis=1)),
                lower[(index + 1) * block_size :, index * block_size : (index + 1) * block_size],
            )
        behind.insert(0, segment)
    return jnp.concatenate(behind, axis=1)


def shards(
    src_cells,
    rec_cells,
    residual,
    pattern,
    leaf_lower,
    leaf_upper,
    leaf_inv,
    anc_lower,
    anc_upper,
    sep_inv,
    sep_lower,
    sep_upper,
):
    leaves = lax.axis_size("leaf")
    levels = leaves.bit_length() - 1
    device = lax.axis_index("leaf")
    block_size = leaf_inv.shape[1]
    block_count = leaf_inv.shape[0]
    cell_count = leaf_lower.shape[1]
    source_count = src_cells.shape[0]
    factor = 1.0 / math.sqrt(source_count * lax.axis_size("src"))
    present = pattern.astype(jnp.float32)

    def level_mask(height):
        level_row = present[height] * (jnp.arange(1, levels + 1) > height).astype(jnp.float32)
        return jnp.repeat(level_row, block_size)

    def blocks_of(values):
        return [values[:, k * block_size : (k + 1) * block_size] for k in range(values.shape[1] // block_size)]

    columns = lax.broadcasted_iota(jnp.int32, (source_count, cell_count), 1)
    forcing = (src_cells[:, None] - device * cell_count == columns).astype(jnp.float32)
    receiver_hits = (
        rec_cells[:, None] == lax.broadcasted_iota(jnp.int32, (rec_cells.shape[0], cell_count), 1)
    ).astype(jnp.float32)
    adjoint_rhs = jnp.dot(residual, receiver_hits, precision=lax.Precision.HIGHEST)

    base_mask = level_mask(0)
    y_leaf = lower_solve(forcing, leaf_lower, block_size, block_count)
    z_leaf = upper_t_solve(adjoint_rhs, leaf_upper, leaf_inv, block_size, block_count)
    forward_sums = blocks_of(across(as_half(y_leaf), anc_lower) * base_mask)
    adjoint_sums = blocks_of(plain_dot(as_half(z_leaf), anc_upper) * base_mask)

    lower_panels, upper_panels, inverse_panels, pattern_rows = [], [], [], []
    for height in range(1, levels + 1):
        lower_panels.append(sep_lower[height - 1, height * block_size :, :])
        upper_panels.append(sep_upper[height - 1, :, height * block_size :])
        inverse_panels.append(sep_inv[height - 1])
        row = pattern[height].astype(jnp.bfloat16)[None, :]
        pattern_rows.append(jnp.pad(row, ((0, 7), (0, block_size - levels))))

    def chain_mask(height):
        level_row = pattern_rows[height - 1][0, :levels].astype(jnp.float32)
        level_row = level_row * (jnp.arange(1, levels + 1) > height).astype(jnp.float32)
        return jnp.repeat(level_row, block_size)[height * block_size :]

    def exchange(values, pairs):
        pieces = [piece for piece in values]
        incoming = lax.ppermute(jnp.concatenate(pieces, axis=0), "leaf", pairs)
        received, row = [], 0
        for piece in pieces:
            received.append(incoming[row : row + piece.shape[0]])
            row += piece.shape[0]
        return received

    for height in range(1, levels + 1):
        stride = 1 << (height - 1)
        pairs = [(index, index ^ stride) for index in range(leaves)]
        pieces = []
        for upper_level in range(height, levels + 1):
            pieces.append(lower_panels[upper_level - 1])
            pieces.extend(blocks_of(upper_panels[upper_level - 1]))
            pieces.append(inverse_panels[upper_level - 1])
            pieces.append(pattern_rows[upper_level - 1])
        received = exchange(pieces, pairs)
        for upper_level in range(height, levels + 1):
            place = device % (1 << upper_level)
            take = jnp.logical_and(place >= stride, place < 2 * stride)
            width = levels - upper_level
            lower_in = received[0]
            upper_in = jnp.concatenate(received[1 : 1 + width] or [upper_panels[upper_level - 1]], axis=1)
            inverse_in = received[1 + width]
            pattern_in = received[2 + width]
            received = received[3 + width :]
            pattern_rows[upper_level - 1] = jnp.where(take, pattern_in, pattern_rows[upper_level - 1])
            lower_panels[upper_level - 1] = jnp.where(take, lower_in, lower_panels[upper_level - 1])
            upper_panels[upper_level - 1] = jnp.where(take, upper_in, upper_panels[upper_level - 1])
            inverse_panels[upper_level - 1] = jnp.where(take, inverse_in, inverse_panels[upper_level - 1])

    forward_nodes, adjoint_nodes = [], []
    for height in range(1, levels + 1):
        stride = 1 << (height - 1)
        pairs = [(index, index ^ stride) for index in range(leaves)]
        forward_sums = [mine + theirs for mine, theirs in zip(forward_sums, exchange(forward_sums, pairs))]
        forward_node = -forward_sums[0]
        forward_nodes.append(forward_node)
        forward_sums = forward_sums[1:]
        if forward_sums:
            forward_coupling = blocks_of(
                across(as_half(forward_node), lower_panels[height - 1]) * chain_mask(height)
            )
            forward_sums = [total + extra for total, extra in zip(forward_sums, forward_coupling)]
        adjoint_sums = [mine + theirs for mine, theirs in zip(adjoint_sums, exchange(adjoint_sums, pairs))]
        adjoint_node = plain_dot(as_half(-adjoint_sums[0]), inverse_panels[height - 1])
        adjoint_nodes.append(adjoint_node)
        adjoint_sums = adjoint_sums[1:]
        if adjoint_sums:
            adjoint_coupling = blocks_of(
                plain_dot(as_half(adjoint_node), upper_panels[height - 1]) * chain_mask(height)
            )
            adjoint_sums = [total + extra for total, extra in zip(adjoint_sums, adjoint_coupling)]

    forward_above, adjoint_above = [], []
    for height in range(levels, 0, -1):
        right_side = forward_nodes[height - 1]
        adjoint_value = adjoint_nodes[height - 1]
        if forward_above:
            right_side = right_side - across(
                as_half(jnp.concatenate(forward_above, axis=1) * chain_mask(height)), upper_panels[height - 1]
            )
            adjoint_value = adjoint_value - plain_dot(
                as_half(jnp.concatenate(adjoint_above, axis=1) * chain_mask(height)), lower_panels[height - 1]
            )
        forward_above.insert(0, across(as_half(right_side), inverse_panels[height - 1]))
        adjoint_above.insert(0, adjoint_value)
    forward_above = jnp.concatenate(forward_above, axis=1)
    adjoint_above = jnp.concatenate(adjoint_above, axis=1)

    forward_remain = y_leaf - across(as_half(forward_above * base_mask), anc_upper)
    forward_field = upper_solve(forward_remain, leaf_upper, leaf_inv, block_size, block_count)
    adjoint_remain = z_leaf - plain_dot(as_half(adjoint_above * base_mask), anc_lower)
    adjoint_field = lower_t_solve(adjoint_remain, leaf_lower, block_size, block_count)
    spread = lax.axis_size("src")
    product_field = (forward_field * adjoint_field).reshape(source_count, spread, cell_count // spread)
    partial_gradient = jnp.sum(product_field, axis=0)
    place = lax.axis_index("src")
    bit = spread // 2
    while bit:
        half = partial_gradient.shape[0] // 2
        upper = (place & bit) != 0
        outgoing = jnp.where(upper, partial_gradient[:half], partial_gradient[half:])
        kept = jnp.where(upper, partial_gradient[half:], partial_gradient[:half])
        pairs = [(index, index ^ bit) for index in range(spread)]
        partial_gradient = kept + lax.ppermute(outgoing, "src", pairs)
        bit //= 2
    gradient = partial_gradient.reshape(-1) * factor
    return (forward_field, adjoint_field, gradient)


def solution(mesh):
    in_specs = (
        P("src"),
        P("leaf"),
        P("src", "leaf"),
        P("leaf", None),
        P("leaf", None),
        P("leaf", None),
        P("leaf", None, None),
        P("leaf", None),
        P("leaf", None),
        P("leaf", None, None),
        P("leaf", None, None),
        P("leaf", None, None),
    )
    out_specs = (P("src", "leaf"), P("src", "leaf"), P(("leaf", "src")))
    return jax.shard_map(shards, mesh=mesh, in_specs=in_specs, out_specs=out_specs, check_vma=False)
```

```python
import math

import jax
import jax.numpy as jnp
from jax import lax
from jax.sharding import PartitionSpec as P


def across(former, latter):
    return lax.dot_general(
        former, latter, (((1,), (1,)), ((), ())), preferred_element_type=jnp.float32
    )


def plain_dot(former, latter):
    return jnp.dot(former, latter, preferred_element_type=jnp.float32)


def as_half(values):
    return values.astype(jnp.bfloat16)


def lower_solve(right_side, lower, block_size, block_count):
    solved = []
    for index in range(block_count):
        segment = right_side[:, index * block_size : (index + 1) * block_size]
        if index:
            earlier = as_half(jnp.concatenate(solved, axis=1))
            segment = segment - across(
                earlier, lower[index * block_size : (index + 1) * block_size, : index * block_size]
            )
        solved.append(segment)
    return jnp.concatenate(solved, axis=1)


def upper_solve(right_side, upper, inverse, block_size, block_count):
    behind = []
    for index in reversed(range(block_count)):
        segment = right_side[:, index * block_size : (index + 1) * block_size]
        if behind:
            segment = segment - across(
                as_half(jnp.concatenate(behind, axis=1)),
                upper[index * block_size : (index + 1) * block_size, (index + 1) * block_size :],
            )
        behind.insert(0, across(as_half(segment), inverse[index]))
    return jnp.concatenate(behind, axis=1)


def upper_t_solve(right_side, upper, inverse, block_size, block_count):
    solved = []
    for index in range(block_count):
        segment = right_side[:, index * block_size : (index + 1) * block_size]
        if index:
            earlier = as_half(jnp.concatenate(solved, axis=1))
            segment = segment - plain_dot(
                earlier, upper[: index * block_size, index * block_size : (index + 1) * block_size]
            )
        solved.append(plain_dot(as_half(segment), inverse[index]))
    return jnp.concatenate(solved, axis=1)


def lower_t_solve(right_side, lower, block_size, block_count):
    behind = []
    for index in reversed(range(block_count)):
        segment = right_side[:, index * block_size : (index + 1) * block_size]
        if behind:
            segment = segment - plain_dot(
                as_half(jnp.concatenate(behind, axis=1)),
                lower[(index + 1) * block_size :, index * block_size : (index + 1) * block_size],
            )
        behind.insert(0, segment)
    return jnp.concatenate(behind, axis=1)


def shards(
    src_cells,
    rec_cells,
    residual,
    pattern,
    leaf_lower,
    leaf_upper,
    leaf_inv,
    anc_lower,
    anc_upper,
    sep_inv,
    sep_lower,
    sep_upper,
):
    leaves = lax.axis_size("leaf")
    levels = leaves.bit_length() - 1
    device = lax.axis_index("leaf")
    block_size = leaf_inv.shape[1]
    block_count = leaf_inv.shape[0]
    cell_count = leaf_lower.shape[1]
    source_count = src_cells.shape[0]
    factor = 1.0 / math.sqrt(source_count * lax.axis_size("src"))
    present = pattern.astype(jnp.float32)

    def level_mask(height):
        level_row = present[height] * (jnp.arange(1, levels + 1) > height).astype(jnp.float32)
        return jnp.repeat(level_row, block_size)

    def blocks_of(values):
        return [values[:, k * block_size : (k + 1) * block_size] for k in range(values.shape[1] // block_size)]

    columns = lax.broadcasted_iota(jnp.int32, (source_count, cell_count), 1)
    forcing = (src_cells[:, None] - device * cell_count == columns).astype(jnp.float32)
    receiver_hits = (
        rec_cells[:, None] == lax.broadcasted_iota(jnp.int32, (rec_cells.shape[0], cell_count), 1)
    ).astype(jnp.float32)
    adjoint_rhs = jnp.dot(residual, receiver_hits, precision=lax.Precision.HIGHEST)

    base_mask = level_mask(0)
    y_leaf = lower_solve(forcing, leaf_lower, block_size, block_count)
    z_leaf = upper_t_solve(adjoint_rhs, leaf_upper, leaf_inv, block_size, block_count)
    forward_sums = blocks_of(across(as_half(y_leaf), anc_lower) * base_mask)
    adjoint_sums = blocks_of(plain_dot(as_half(z_leaf), anc_upper) * base_mask)

    lower_panels, upper_panels, inverse_panels, pattern_rows = [], [], [], []
    for height in range(1, levels + 1):
        lower_panels.append(sep_lower[height - 1, height * block_size :, :])
        upper_panels.append(sep_upper[height - 1, :, height * block_size :])
        inverse_panels.append(sep_inv[height - 1])
        row = pattern[height].astype(jnp.bfloat16)[None, :]
        pattern_rows.append(jnp.pad(row, ((0, 7), (0, block_size - levels))))

    def chain_mask(height):
        level_row = pattern_rows[height - 1][0, :levels].astype(jnp.float32)
        level_row = level_row * (jnp.arange(1, levels + 1) > height).astype(jnp.float32)
        return jnp.repeat(level_row, block_size)[height * block_size :]

    def exchange(values, pairs):
        pieces = [piece for piece in values]
        incoming = lax.ppermute(jnp.concatenate(pieces, axis=0), "leaf", pairs)
        received, row = [], 0
        for piece in pieces:
            received.append(incoming[row : row + piece.shape[0]])
            row += piece.shape[0]
        return received

    for height in range(1, levels + 1):
        stride = 1 << (height - 1)
        pairs = [(index, index ^ stride) for index in range(leaves)]
        pieces = []
        for upper_level in range(height, levels + 1):
            pieces.append(lower_panels[upper_level - 1])
            pieces.extend(blocks_of(upper_panels[upper_level - 1]))
            pieces.append(inverse_panels[upper_level - 1])
            pieces.append(pattern_rows[upper_level - 1])
        received = exchange(pieces, pairs)
        for upper_level in range(height, levels + 1):
            place = device % (1 << upper_level)
            take = jnp.logical_and(place >= stride, place < 2 * stride)
            width = levels - upper_level
            lower_in = received[0]
            upper_in = jnp.concatenate(received[1 : 1 + width] or [upper_panels[upper_level - 1]], axis=1)
            inverse_in = received[1 + width]
            pattern_in = received[2 + width]
            received = received[3 + width :]
            pattern_rows[upper_level - 1] = jnp.where(take, pattern_in, pattern_rows[upper_level - 1])
            lower_panels[upper_level - 1] = jnp.where(take, lower_in, lower_panels[upper_level - 1])
            upper_panels[upper_level - 1] = jnp.where(take, upper_in, upper_panels[upper_level - 1])
            inverse_panels[upper_level - 1] = jnp.where(take, inverse_in, inverse_panels[upper_level - 1])

    forward_nodes, adjoint_nodes = [], []
    for height in range(1, levels + 1):
        stride = 1 << (height - 1)
        pairs = [(index, index ^ stride) for index in range(leaves)]
        forward_sums = [mine + theirs for mine, theirs in zip(forward_sums, exchange(forward_sums, pairs))]
        forward_node = -forward_sums[0]
        forward_nodes.append(forward_node)
        forward_sums = forward_sums[1:]
        if forward_sums:
            forward_coupling = blocks_of(
                across(as_half(forward_node), lower_panels[height - 1]) * chain_mask(height)
            )
            forward_sums = [total + extra for total, extra in zip(forward_sums, forward_coupling)]
        adjoint_sums, forward_sums, forward_node = lax.optimization_barrier((adjoint_sums, forward_sums, forward_node))
        forward_nodes[-1] = forward_node
        adjoint_sums = [mine + theirs for mine, theirs in zip(adjoint_sums, exchange(adjoint_sums, pairs))]
        adjoint_node = plain_dot(as_half(-adjoint_sums[0]), inverse_panels[height - 1])
        adjoint_nodes.append(adjoint_node)
        adjoint_sums = adjoint_sums[1:]
        if adjoint_sums:
            adjoint_coupling = blocks_of(
                plain_dot(as_half(adjoint_node), upper_panels[height - 1]) * chain_mask(height)
            )
            adjoint_sums = [total + extra for total, extra in zip(adjoint_sums, adjoint_coupling)]

    forward_above, adjoint_above = [], []
    for height in range(levels, 0, -1):
        right_side = forward_nodes[height - 1]
        adjoint_value = adjoint_nodes[height - 1]
        if forward_above:
            right_side = right_side - across(
                as_half(jnp.concatenate(forward_above, axis=1) * chain_mask(height)), upper_panels[height - 1]
            )
            adjoint_value = adjoint_value - plain_dot(
                as_half(jnp.concatenate(adjoint_above, axis=1) * chain_mask(height)), lower_panels[height - 1]
            )
        forward_above.insert(0, across(as_half(right_side), inverse_panels[height - 1]))
        adjoint_above.insert(0, adjoint_value)
    forward_above = jnp.concatenate(forward_above, axis=1)
    adjoint_above = jnp.concatenate(adjoint_above, axis=1)

    forward_remain = y_leaf - across(as_half(forward_above * base_mask), anc_upper)
    forward_field = upper_solve(forward_remain, leaf_upper, leaf_inv, block_size, block_count)
    adjoint_remain = z_leaf - plain_dot(as_half(adjoint_above * base_mask), anc_lower)
    adjoint_field = lower_t_solve(adjoint_remain, leaf_lower, block_size, block_count)
    spread = lax.axis_size("src")
    product_field = (forward_field * adjoint_field).reshape(source_count, spread, cell_count // spread)
    partial_gradient = jnp.sum(product_field, axis=0)
    place = lax.axis_index("src")
    bit = spread // 2
    while bit:
        half = partial_gradient.shape[0] // 2
        upper = (place & bit) != 0
        outgoing = jnp.where(upper, partial_gradient[:half], partial_gradient[half:])
        kept = jnp.where(upper, partial_gradient[half:], partial_gradient[:half])
        pairs = [(index, index ^ bit) for index in range(spread)]
        partial_gradient = kept + lax.ppermute(outgoing, "src", pairs)
        bit //= 2
    gradient = partial_gradient.reshape(-1) * factor
    return (forward_field, adjoint_field, gradient)


def solution(mesh):
    in_specs = (
        P("src"),
        P("leaf"),
        P("src", "leaf"),
        P("leaf", None),
        P("leaf", None),
        P("leaf", None),
        P("leaf", None, None),
        P("leaf", None),
        P("leaf", None),
        P("leaf", None, None),
        P("leaf", None, None),
        P("leaf", None, None),
    )
    out_specs = (P("src", "leaf"), P("src", "leaf"), P(("leaf", "src")))
    return jax.shard_map(shards, mesh=mesh, in_specs=in_specs, out_specs=out_specs, check_vma=False)
```

```python
import math

import jax
import jax.numpy as jnp
from jax import lax
from jax.sharding import PartitionSpec as P


def across(former, latter):
    return lax.dot_general(
        former, latter, (((1,), (1,)), ((), ())), preferred_element_type=jnp.float32
    )


def plain_dot(former, latter):
    return jnp.dot(former, latter, preferred_element_type=jnp.float32)


def as_half(values):
    return values.astype(jnp.bfloat16)


def lower_solve(right_side, lower, block_size, block_count):
    solved = []
    for index in range(block_count):
        segment = right_side[:, index * block_size : (index + 1) * block_size]
        if index:
            earlier = as_half(jnp.concatenate(solved, axis=1))
            segment = segment - across(
                earlier, lower[index * block_size : (index + 1) * block_size, : index * block_size]
            )
        solved.append(segment)
    return jnp.concatenate(solved, axis=1)


def upper_solve(right_side, upper, inverse, block_size, block_count):
    behind = []
    for index in reversed(range(block_count)):
        segment = right_side[:, index * block_size : (index + 1) * block_size]
        if behind:
            segment = segment - across(
                as_half(jnp.concatenate(behind, axis=1)),
                upper[index * block_size : (index + 1) * block_size, (index + 1) * block_size :],
            )
        behind.insert(0, across(as_half(segment), inverse[index]))
    return jnp.concatenate(behind, axis=1)


def upper_t_solve(right_side, upper, inverse, block_size, block_count):
    solved = []
    for index in range(block_count):
        segment = right_side[:, index * block_size : (index + 1) * block_size]
        if index:
            earlier = as_half(jnp.concatenate(solved, axis=1))
            segment = segment - plain_dot(
                earlier, upper[: index * block_size, index * block_size : (index + 1) * block_size]
            )
        solved.append(plain_dot(as_half(segment), inverse[index]))
    return jnp.concatenate(solved, axis=1)


def lower_t_solve(right_side, lower, block_size, block_count):
    behind = []
    for index in reversed(range(block_count)):
        segment = right_side[:, index * block_size : (index + 1) * block_size]
        if behind:
            segment = segment - plain_dot(
                as_half(jnp.concatenate(behind, axis=1)),
                lower[(index + 1) * block_size :, index * block_size : (index + 1) * block_size],
            )
        behind.insert(0, segment)
    return jnp.concatenate(behind, axis=1)


def shards(
    src_cells,
    rec_cells,
    residual,
    pattern,
    leaf_lower,
    leaf_upper,
    leaf_inv,
    anc_lower,
    anc_upper,
    sep_inv,
    sep_lower,
    sep_upper,
):
    leaves = lax.axis_size("leaf")
    levels = leaves.bit_length() - 1
    device = lax.axis_index("leaf")
    block_size = leaf_inv.shape[1]
    block_count = leaf_inv.shape[0]
    cell_count = leaf_lower.shape[1]
    source_count = src_cells.shape[0]
    factor = 1.0 / math.sqrt(source_count * lax.axis_size("src"))
    present = pattern.astype(jnp.float32)

    def level_mask(height):
        level_row = present[height] * (jnp.arange(1, levels + 1) > height).astype(jnp.float32)
        return jnp.repeat(level_row, block_size)

    def blocks_of(values):
        return [values[:, k * block_size : (k + 1) * block_size] for k in range(values.shape[1] // block_size)]

    columns = lax.broadcasted_iota(jnp.int32, (source_count, cell_count), 1)
    forcing = (src_cells[:, None] - device * cell_count == columns).astype(jnp.float32)
    receiver_hits = (
        rec_cells[:, None] == lax.broadcasted_iota(jnp.int32, (rec_cells.shape[0], cell_count), 1)
    ).astype(jnp.float32)
    adjoint_rhs = jnp.dot(residual, receiver_hits, precision=lax.Precision.HIGHEST)

    base_mask = level_mask(0)
    y_leaf = lower_solve(forcing, leaf_lower, block_size, block_count)
    z_leaf = upper_t_solve(adjoint_rhs, leaf_upper, leaf_inv, block_size, block_count)
    forward_sums = blocks_of(across(as_half(y_leaf), anc_lower) * base_mask)
    adjoint_sums = blocks_of(plain_dot(as_half(z_leaf), anc_upper) * base_mask)

    panel_arrays = [sep_lower, sep_upper, sep_inv, pattern]
    for height in range(1, levels + 1):
        stride = 1 << (height - 1)
        pairs = [(index, index ^ stride) for index in range(leaves)]
        takes = []
        for upper_level in range(1, levels + 1):
            place = device % (1 << upper_level)
            takes.append(jnp.logical_and(upper_level >= height, jnp.logical_and(place >= stride, place < 2 * stride)))
        takes = jnp.stack(takes)
        pattern_takes = jnp.concatenate([jnp.zeros((1,), jnp.bool_), takes])
        received = [lax.ppermute(array, "leaf", pairs) for array in panel_arrays]
        panel_arrays = [
            jnp.where(takes[:, None, None], received[0], panel_arrays[0]),
            jnp.where(takes[:, None, None], received[1], panel_arrays[1]),
            jnp.where(takes[:, None, None], received[2], panel_arrays[2]),
            jnp.where(pattern_takes[:, None], received[3], panel_arrays[3]),
        ]
    chain_lower, chain_upper, chain_inverse, chain_pattern = panel_arrays
    lower_panels = [chain_lower[height - 1, height * block_size :, :] for height in range(1, levels + 1)]
    upper_panels = [chain_upper[height - 1, :, height * block_size :] for height in range(1, levels + 1)]
    inverse_panels = [chain_inverse[height - 1] for height in range(1, levels + 1)]

    def chain_mask(height):
        level_row = chain_pattern[height].astype(jnp.float32)
        level_row = level_row * (jnp.arange(1, levels + 1) > height).astype(jnp.float32)
        return jnp.repeat(level_row, block_size)[height * block_size :]

    def exchange(values, pairs):
        incoming = lax.ppermute(jnp.concatenate(values, axis=0), "leaf", pairs)
        return [incoming[k * source_count : (k + 1) * source_count] for k in range(len(values))]

    forward_nodes, adjoint_nodes = [], []
    for height in range(1, levels + 1):
        stride = 1 << (height - 1)
        pairs = [(index, index ^ stride) for index in range(leaves)]
        forward_sums = [mine + theirs for mine, theirs in zip(forward_sums, exchange(forward_sums, pairs))]
        forward_node = -forward_sums[0]
        forward_nodes.append(forward_node)
        forward_sums = forward_sums[1:]
        if forward_sums:
            forward_coupling = blocks_of(
                across(as_half(forward_node), lower_panels[height - 1]) * chain_mask(height)
            )
            forward_sums = [total + extra for total, extra in zip(forward_sums, forward_coupling)]
        adjoint_sums = [mine + theirs for mine, theirs in zip(adjoint_sums, exchange(adjoint_sums, pairs))]
        adjoint_node = plain_dot(as_half(-adjoint_sums[0]), inverse_panels[height - 1])
        adjoint_nodes.append(adjoint_node)
        adjoint_sums = adjoint_sums[1:]
        if adjoint_sums:
            adjoint_coupling = blocks_of(
                plain_dot(as_half(adjoint_node), upper_panels[height - 1]) * chain_mask(height)
            )
            adjoint_sums = [total + extra for total, extra in zip(adjoint_sums, adjoint_coupling)]

    forward_above, adjoint_above = [], []
    for height in range(levels, 0, -1):
        right_side = forward_nodes[height - 1]
        adjoint_value = adjoint_nodes[height - 1]
        if forward_above:
            right_side = right_side - across(
                as_half(jnp.concatenate(forward_above, axis=1) * chain_mask(height)), upper_panels[height - 1]
            )
            adjoint_value = adjoint_value - plain_dot(
                as_half(jnp.concatenate(adjoint_above, axis=1) * chain_mask(height)), lower_panels[height - 1]
            )
        forward_above.insert(0, across(as_half(right_side), inverse_panels[height - 1]))
        adjoint_above.insert(0, adjoint_value)
    forward_above = jnp.concatenate(forward_above, axis=1)
    adjoint_above = jnp.concatenate(adjoint_above, axis=1)

    forward_remain = y_leaf - across(as_half(forward_above * base_mask), anc_upper)
    forward_field = upper_solve(forward_remain, leaf_upper, leaf_inv, block_size, block_count)
    adjoint_remain = z_leaf - plain_dot(as_half(adjoint_above * base_mask), anc_lower)
    adjoint_field = lower_t_solve(adjoint_remain, leaf_lower, block_size, block_count)
    spread = lax.axis_size("src")
    product_field = (forward_field * adjoint_field).reshape(source_count, spread, cell_count // spread)
    partial_gradient = jnp.sum(product_field, axis=0)
    place = lax.axis_index("src")
    bit = spread // 2
    while bit:
        half = partial_gradient.shape[0] // 2
        upper = (place & bit) != 0
        outgoing = jnp.where(upper, partial_gradient[:half], partial_gradient[half:])
        kept = jnp.where(upper, partial_gradient[half:], partial_gradient[:half])
        pairs = [(index, index ^ bit) for index in range(spread)]
        partial_gradient = kept + lax.ppermute(outgoing, "src", pairs)
        bit //= 2
    gradient = partial_gradient.reshape(-1) * factor
    return (forward_field, adjoint_field, gradient)


def solution(mesh):
    in_specs = (
        P("src"),
        P("leaf"),
        P("src", "leaf"),
        P("leaf", None),
        P("leaf", None),
        P("leaf", None),
        P("leaf", None, None),
        P("leaf", None),
        P("leaf", None),
        P("leaf", None, None),
        P("leaf", None, None),
        P("leaf", None, None),
    )
    out_specs = (P("src", "leaf"), P("src", "leaf"), P(("leaf", "src")))
    return jax.shard_map(shards, mesh=mesh, in_specs=in_specs, out_specs=out_specs, check_vma=False)
```

```python
import math

import jax
import jax.numpy as jnp
from jax import lax
from jax.sharding import PartitionSpec as P


def across(former, latter):
    return lax.dot_general(
        former, latter, (((1,), (1,)), ((), ())), preferred_element_type=jnp.float32
    )


def plain_dot(former, latter):
    return jnp.dot(former, latter, preferred_element_type=jnp.float32)


def as_half(values):
    return values.astype(jnp.bfloat16)


def lower_solve(right_side, lower, block_size, block_count):
    solved = []
    for index in range(block_count):
        segment = right_side[:, index * block_size : (index + 1) * block_size]
        if index:
            earlier = as_half(jnp.concatenate(solved, axis=1))
            segment = segment - across(
                earlier, lower[index * block_size : (index + 1) * block_size, : index * block_size]
            )
        solved.append(segment)
    return jnp.concatenate(solved, axis=1)


def upper_solve(right_side, upper, inverse, block_size, block_count):
    behind = []
    for index in reversed(range(block_count)):
        segment = right_side[:, index * block_size : (index + 1) * block_size]
        if behind:
            segment = segment - across(
                as_half(jnp.concatenate(behind, axis=1)),
                upper[index * block_size : (index + 1) * block_size, (index + 1) * block_size :],
            )
        behind.insert(0, across(as_half(segment), inverse[index]))
    return jnp.concatenate(behind, axis=1)


def upper_t_solve(right_side, upper, inverse, block_size, block_count):
    solved = []
    for index in range(block_count):
        segment = right_side[:, index * block_size : (index + 1) * block_size]
        if index:
            earlier = as_half(jnp.concatenate(solved, axis=1))
            segment = segment - plain_dot(
                earlier, upper[: index * block_size, index * block_size : (index + 1) * block_size]
            )
        solved.append(plain_dot(as_half(segment), inverse[index]))
    return jnp.concatenate(solved, axis=1)


def lower_t_solve(right_side, lower, block_size, block_count):
    behind = []
    for index in reversed(range(block_count)):
        segment = right_side[:, index * block_size : (index + 1) * block_size]
        if behind:
            segment = segment - plain_dot(
                as_half(jnp.concatenate(behind, axis=1)),
                lower[(index + 1) * block_size :, index * block_size : (index + 1) * block_size],
            )
        behind.insert(0, segment)
    return jnp.concatenate(behind, axis=1)


def shards(
    src_cells,
    rec_cells,
    residual,
    pattern,
    leaf_lower,
    leaf_upper,
    leaf_inv,
    anc_lower,
    anc_upper,
    sep_inv,
    sep_lower,
    sep_upper,
):
    leaves = lax.axis_size("leaf")
    levels = leaves.bit_length() - 1
    device = lax.axis_index("leaf")
    block_size = leaf_inv.shape[1]
    block_count = leaf_inv.shape[0]
    cell_count = leaf_lower.shape[1]
    source_count = src_cells.shape[0]
    factor = 1.0 / math.sqrt(source_count * lax.axis_size("src"))
    present = pattern.astype(jnp.float32)

    def level_mask(height):
        level_row = present[height] * (jnp.arange(1, levels + 1) > height).astype(jnp.float32)
        return jnp.repeat(level_row, block_size)

    def blocks_of(values):
        return [values[:, k * block_size : (k + 1) * block_size] for k in range(values.shape[1] // block_size)]

    columns = lax.broadcasted_iota(jnp.int32, (source_count, cell_count), 1)
    forcing = (src_cells[:, None] - device * cell_count == columns).astype(jnp.float32)
    receiver_hits = (
        rec_cells[:, None] == lax.broadcasted_iota(jnp.int32, (rec_cells.shape[0], cell_count), 1)
    ).astype(jnp.float32)
    adjoint_rhs = jnp.dot(residual, receiver_hits, precision=lax.Precision.HIGHEST)

    base_mask = level_mask(0)
    y_leaf = lower_solve(forcing, leaf_lower, block_size, block_count)
    z_leaf = upper_t_solve(adjoint_rhs, leaf_upper, leaf_inv, block_size, block_count)
    forward_sums = blocks_of(across(as_half(y_leaf), anc_lower) * base_mask)
    adjoint_sums = blocks_of(plain_dot(as_half(z_leaf), anc_upper) * base_mask)

    lower_panels, upper_panels, inverse_panels, pattern_rows = [], [], [], []
    for height in range(1, levels + 1):
        lower_panels.append(sep_lower[height - 1, height * block_size :, :])
        upper_panels.append(sep_upper[height - 1, :, height * block_size :])
        inverse_panels.append(sep_inv[height - 1])
        row = pattern[height].astype(jnp.bfloat16)[None, :]
        pattern_rows.append(jnp.pad(row, ((0, 7), (0, block_size - levels))))

    def chain_mask(height):
        level_row = pattern_rows[height - 1][0, :levels].astype(jnp.float32)
        level_row = level_row * (jnp.arange(1, levels + 1) > height).astype(jnp.float32)
        return jnp.repeat(level_row, block_size)[height * block_size :]

    def exchange(values, pairs):
        pieces = [piece for piece in values]
        incoming = lax.ppermute(jnp.concatenate(pieces, axis=0), "leaf", pairs)
        received, row = [], 0
        for piece in pieces:
            received.append(incoming[row : row + piece.shape[0]])
            row += piece.shape[0]
        return received

    forward_nodes, adjoint_nodes = [], []
    for height in range(1, levels + 1):
        stride = 1 << (height - 1)
        pairs = [(index, index ^ stride) for index in range(leaves)]
        panel_pieces = []
        for upper_level in range(height, levels + 1):
            panel_pieces.append(lower_panels[upper_level - 1])
            panel_pieces.extend(blocks_of(upper_panels[upper_level - 1]))
            panel_pieces.append(inverse_panels[upper_level - 1])
            panel_pieces.append(pattern_rows[upper_level - 1])
        wide_pieces = [piece.astype(jnp.float32) for piece in panel_pieces]
        count = len(forward_sums)
        if height == 1:
            forward_in = exchange(forward_sums + wide_pieces, pairs)
            adjoint_in = exchange(adjoint_sums, pairs)
            received = forward_in[count:]
        else:
            forward_in = exchange(forward_sums, pairs)
            adjoint_in = exchange(adjoint_sums + wide_pieces, pairs)
            received = adjoint_in[count:]
        received = [piece.astype(jnp.bfloat16) for piece in received]
        for upper_level in range(height, levels + 1):
            place = device % (1 << upper_level)
            take = jnp.logical_and(place >= stride, place < 2 * stride)
            width = levels - upper_level
            lower_in = received[0]
            upper_in = jnp.concatenate(received[1 : 1 + width] or [upper_panels[upper_level - 1]], axis=1)
            inverse_in = received[1 + width]
            pattern_in = received[2 + width]
            received = received[3 + width :]
            pattern_rows[upper_level - 1] = jnp.where(take, pattern_in, pattern_rows[upper_level - 1])
            lower_panels[upper_level - 1] = jnp.where(take, lower_in, lower_panels[upper_level - 1])
            upper_panels[upper_level - 1] = jnp.where(take, upper_in, upper_panels[upper_level - 1])
            inverse_panels[upper_level - 1] = jnp.where(take, inverse_in, inverse_panels[upper_level - 1])
        forward_sums = [mine + theirs for mine, theirs in zip(forward_sums, forward_in[:count])]
        adjoint_sums = [mine + theirs for mine, theirs in zip(adjoint_sums, adjoint_in[:count])]
        forward_node = -forward_sums[0]
        forward_nodes.append(forward_node)
        forward_sums = forward_sums[1:]
        adjoint_node = plain_dot(as_half(-adjoint_sums[0]), inverse_panels[height - 1])
        adjoint_nodes.append(adjoint_node)
        adjoint_sums = adjoint_sums[1:]
        if forward_sums:
            forward_coupling = blocks_of(
                across(as_half(forward_node), lower_panels[height - 1]) * chain_mask(height)
            )
            forward_sums = [total + extra for total, extra in zip(forward_sums, forward_coupling)]
            adjoint_coupling = blocks_of(
                plain_dot(as_half(adjoint_node), upper_panels[height - 1]) * chain_mask(height)
            )
            adjoint_sums = [total + extra for total, extra in zip(adjoint_sums, adjoint_coupling)]

    forward_above, adjoint_above = [], []
    for height in range(levels, 0, -1):
        right_side = forward_nodes[height - 1]
        adjoint_value = adjoint_nodes[height - 1]
        if forward_above:
            right_side = right_side - across(
                as_half(jnp.concatenate(forward_above, axis=1) * chain_mask(height)), upper_panels[height - 1]
            )
            adjoint_value = adjoint_value - plain_dot(
                as_half(jnp.concatenate(adjoint_above, axis=1) * chain_mask(height)), lower_panels[height - 1]
            )
        forward_above.insert(0, across(as_half(right_side), inverse_panels[height - 1]))
        adjoint_above.insert(0, adjoint_value)
    forward_above = jnp.concatenate(forward_above, axis=1)
    adjoint_above = jnp.concatenate(adjoint_above, axis=1)

    forward_remain = y_leaf - across(as_half(forward_above * base_mask), anc_upper)
    forward_field = upper_solve(forward_remain, leaf_upper, leaf_inv, block_size, block_count)
    adjoint_remain = z_leaf - plain_dot(as_half(adjoint_above * base_mask), anc_lower)
    adjoint_field = lower_t_solve(adjoint_remain, leaf_lower, block_size, block_count)
    spread = lax.axis_size("src")
    product_field = (forward_field * adjoint_field).reshape(source_count, spread, cell_count // spread)
    partial_gradient = jnp.sum(product_field, axis=0)
    place = lax.axis_index("src")
    bit = spread // 2
    while bit:
        half = partial_gradient.shape[0] // 2
        upper = (place & bit) != 0
        outgoing = jnp.where(upper, partial_gradient[:half], partial_gradient[half:])
        kept = jnp.where(upper, partial_gradient[half:], partial_gradient[:half])
        pairs = [(index, index ^ bit) for index in range(spread)]
        partial_gradient = kept + lax.ppermute(outgoing, "src", pairs)
        bit //= 2
    gradient = partial_gradient.reshape(-1) * factor
    return (forward_field, adjoint_field, gradient)


def solution(mesh):
    in_specs = (
        P("src"),
        P("leaf"),
        P("src", "leaf"),
        P("leaf", None),
        P("leaf", None),
        P("leaf", None),
        P("leaf", None, None),
        P("leaf", None),
        P("leaf", None),
        P("leaf", None, None),
        P("leaf", None, None),
        P("leaf", None, None),
    )
    out_specs = (P("src", "leaf"), P("src", "leaf"), P(("leaf", "src")))
    return jax.shard_map(shards, mesh=mesh, in_specs=in_specs, out_specs=out_specs, check_vma=False)
```

```python
import math

import jax
import jax.numpy as jnp
from jax import lax
from jax.sharding import PartitionSpec as P


def across(former, latter):
    return lax.dot_general(
        former, latter, (((1,), (1,)), ((), ())), preferred_element_type=jnp.float32
    )


def plain_dot(former, latter):
    return jnp.dot(former, latter, preferred_element_type=jnp.float32)


def as_half(values):
    return values.astype(jnp.bfloat16)


def lower_solve(right_side, lower, block_size, block_count):
    solved = []
    for index in range(block_count):
        segment = right_side[:, index * block_size : (index + 1) * block_size]
        if index:
            earlier = as_half(jnp.concatenate(solved, axis=1))
            segment = segment - across(
                earlier, lower[index * block_size : (index + 1) * block_size, : index * block_size]
            )
        solved.append(segment)
    return jnp.concatenate(solved, axis=1)


def upper_solve(right_side, upper, inverse, block_size, block_count):
    behind = []
    for index in reversed(range(block_count)):
        segment = right_side[:, index * block_size : (index + 1) * block_size]
        if behind:
            segment = segment - across(
                as_half(jnp.concatenate(behind, axis=1)),
                upper[index * block_size : (index + 1) * block_size, (index + 1) * block_size :],
            )
        behind.insert(0, across(as_half(segment), inverse[index]))
    return jnp.concatenate(behind, axis=1)


def upper_t_solve(right_side, upper, inverse, block_size, block_count):
    solved = []
    for index in range(block_count):
        segment = right_side[:, index * block_size : (index + 1) * block_size]
        if index:
            earlier = as_half(jnp.concatenate(solved, axis=1))
            segment = segment - plain_dot(
                earlier, upper[: index * block_size, index * block_size : (index + 1) * block_size]
            )
        solved.append(plain_dot(as_half(segment), inverse[index]))
    return jnp.concatenate(solved, axis=1)


def lower_t_solve(right_side, lower, block_size, block_count):
    behind = []
    for index in reversed(range(block_count)):
        segment = right_side[:, index * block_size : (index + 1) * block_size]
        if behind:
            segment = segment - plain_dot(
                as_half(jnp.concatenate(behind, axis=1)),
                lower[(index + 1) * block_size :, index * block_size : (index + 1) * block_size],
            )
        behind.insert(0, segment)
    return jnp.concatenate(behind, axis=1)


def shards(
    src_cells,
    rec_cells,
    residual,
    pattern,
    leaf_lower,
    leaf_upper,
    leaf_inv,
    anc_lower,
    anc_upper,
    sep_inv,
    sep_lower,
    sep_upper,
):
    leaves = lax.axis_size("leaf")
    levels = leaves.bit_length() - 1
    device = lax.axis_index("leaf")
    block_size = leaf_inv.shape[1]
    block_count = leaf_inv.shape[0]
    cell_count = leaf_lower.shape[1]
    source_count = src_cells.shape[0]
    factor = 1.0 / math.sqrt(source_count * lax.axis_size("src"))
    present = pattern.astype(jnp.float32)

    def level_mask(height):
        level_row = present[height] * (jnp.arange(1, levels + 1) > height).astype(jnp.float32)
        return jnp.repeat(level_row, block_size)

    def blocks_of(values):
        return [values[:, k * block_size : (k + 1) * block_size] for k in range(values.shape[1] // block_size)]

    columns = lax.broadcasted_iota(jnp.int32, (source_count, cell_count), 1)
    forcing = (src_cells[:, None] - device * cell_count == columns).astype(jnp.float32)
    receiver_hits = (
        rec_cells[:, None] == lax.broadcasted_iota(jnp.int32, (rec_cells.shape[0], cell_count), 1)
    ).astype(jnp.float32)
    adjoint_rhs = jnp.dot(residual, receiver_hits, precision=lax.Precision.HIGHEST)

    base_mask = level_mask(0)
    y_leaf = lower_solve(forcing, leaf_lower, block_size, block_count)
    z_leaf = upper_t_solve(adjoint_rhs, leaf_upper, leaf_inv, block_size, block_count)
    forward_sums = blocks_of(across(as_half(y_leaf), anc_lower) * base_mask)
    adjoint_sums = blocks_of(plain_dot(as_half(z_leaf), anc_upper) * base_mask)

    lower_panels, upper_panels, inverse_panels, pattern_rows = [], [], [], []
    for height in range(1, levels + 1):
        lower_panels.append(sep_lower[height - 1, height * block_size :, :])
        upper_panels.append(sep_upper[height - 1, :, height * block_size :])
        inverse_panels.append(sep_inv[height - 1])
        row = pattern[height].astype(jnp.bfloat16)[None, :]
        pattern_rows.append(jnp.pad(row, ((0, 7), (0, block_size - levels))))

    def chain_mask(height):
        level_row = pattern_rows[height - 1][0, :levels].astype(jnp.float32)
        level_row = level_row * (jnp.arange(1, levels + 1) > height).astype(jnp.float32)
        return jnp.repeat(level_row, block_size)[height * block_size :]

    def exchange(values, pairs):
        pieces = [piece for piece in values]
        incoming = lax.ppermute(jnp.concatenate(pieces, axis=0), "leaf", pairs)
        received, row = [], 0
        for piece in pieces:
            received.append(incoming[row : row + piece.shape[0]])
            row += piece.shape[0]
        return received

    for height in range(1, levels + 1):
        stride = 1 << (height - 1)
        pairs = [(index, index ^ stride) for index in range(leaves)]
        pieces = []
        for upper_level in range(height, levels + 1):
            lower = lower_panels[upper_level - 1]
            pieces.extend(lower[k * block_size : (k + 1) * block_size] for k in range(lower.shape[0] // block_size))
            pieces.extend(blocks_of(upper_panels[upper_level - 1]))
            pieces.append(inverse_panels[upper_level - 1])
        stacked = lax.ppermute(jnp.stack(pieces), "leaf", pairs)
        received = [stacked[k] for k in range(len(pieces))]
        for upper_level in range(height, levels + 1):
            place = device % (1 << upper_level)
            take = jnp.logical_and(place >= stride, place < 2 * stride)
            width = levels - upper_level
            lower_in = jnp.concatenate(received[:width] or [lower_panels[upper_level - 1]], axis=0)
            upper_in = jnp.concatenate(received[width : 2 * width] or [upper_panels[upper_level - 1]], axis=1)
            inverse_in = received[2 * width]
            received = received[2 * width + 1 :]
            lower_panels[upper_level - 1] = jnp.where(take, lower_in, lower_panels[upper_level - 1])
            upper_panels[upper_level - 1] = jnp.where(take, upper_in, upper_panels[upper_level - 1])
            inverse_panels[upper_level - 1] = jnp.where(take, inverse_in, inverse_panels[upper_level - 1])

    forward_nodes, adjoint_nodes = [], []
    for height in range(1, levels + 1):
        stride = 1 << (height - 1)
        pairs = [(index, index ^ stride) for index in range(leaves)]
        count = len(forward_sums)
        wide_rows = [pattern_rows[upper_level - 1].astype(jnp.float32) for upper_level in range(height, levels + 1)]
        received = exchange(forward_sums + wide_rows, pairs)
        for upper_level, pattern_in in zip(range(height, levels + 1), received[count:]):
            place = device % (1 << upper_level)
            take = jnp.logical_and(place >= stride, place < 2 * stride)
            pattern_rows[upper_level - 1] = jnp.where(
                take, pattern_in.astype(jnp.bfloat16), pattern_rows[upper_level - 1]
            )
        forward_sums = [mine + theirs for mine, theirs in zip(forward_sums, received[:count])]
        forward_node = -forward_sums[0]
        forward_nodes.append(forward_node)
        forward_sums = forward_sums[1:]
        if forward_sums:
            forward_coupling = blocks_of(
                across(as_half(forward_node), lower_panels[height - 1]) * chain_mask(height)
            )
            forward_sums = [total + extra for total, extra in zip(forward_sums, forward_coupling)]
        adjoint_sums = [mine + theirs for mine, theirs in zip(adjoint_sums, exchange(adjoint_sums, pairs))]
        adjoint_node = plain_dot(as_half(-adjoint_sums[0]), inverse_panels[height - 1])
        adjoint_nodes.append(adjoint_node)
        adjoint_sums = adjoint_sums[1:]
        if adjoint_sums:
            adjoint_coupling = blocks_of(
                plain_dot(as_half(adjoint_node), upper_panels[height - 1]) * chain_mask(height)
            )
            adjoint_sums = [total + extra for total, extra in zip(adjoint_sums, adjoint_coupling)]

    forward_above, adjoint_above = [], []
    for height in range(levels, 0, -1):
        right_side = forward_nodes[height - 1]
        adjoint_value = adjoint_nodes[height - 1]
        if forward_above:
            right_side = right_side - across(
                as_half(jnp.concatenate(forward_above, axis=1) * chain_mask(height)), upper_panels[height - 1]
            )
            adjoint_value = adjoint_value - plain_dot(
                as_half(jnp.concatenate(adjoint_above, axis=1) * chain_mask(height)), lower_panels[height - 1]
            )
        forward_above.insert(0, across(as_half(right_side), inverse_panels[height - 1]))
        adjoint_above.insert(0, adjoint_value)
    forward_above = jnp.concatenate(forward_above, axis=1)
    adjoint_above = jnp.concatenate(adjoint_above, axis=1)

    forward_remain = y_leaf - across(as_half(forward_above * base_mask), anc_upper)
    forward_field = upper_solve(forward_remain, leaf_upper, leaf_inv, block_size, block_count)
    adjoint_remain = z_leaf - plain_dot(as_half(adjoint_above * base_mask), anc_lower)
    adjoint_field = lower_t_solve(adjoint_remain, leaf_lower, block_size, block_count)
    spread = lax.axis_size("src")
    product_field = (forward_field * adjoint_field).reshape(source_count, spread, cell_count // spread)
    partial_gradient = jnp.sum(product_field, axis=0)
    place = lax.axis_index("src")
    bit = spread // 2
    while bit:
        half = partial_gradient.shape[0] // 2
        upper = (place & bit) != 0
        outgoing = jnp.where(upper, partial_gradient[:half], partial_gradient[half:])
        kept = jnp.where(upper, partial_gradient[half:], partial_gradient[:half])
        pairs = [(index, index ^ bit) for index in range(spread)]
        partial_gradient = kept + lax.ppermute(outgoing, "src", pairs)
        bit //= 2
    gradient = partial_gradient.reshape(-1) * factor
    return (forward_field, adjoint_field, gradient)


def solution(mesh):
    in_specs = (
        P("src"),
        P("leaf"),
        P("src", "leaf"),
        P("leaf", None),
        P("leaf", None),
        P("leaf", None),
        P("leaf", None, None),
        P("leaf", None),
        P("leaf", None),
        P("leaf", None, None),
        P("leaf", None, None),
        P("leaf", None, None),
    )
    out_specs = (P("src", "leaf"), P("src", "leaf"), P(("leaf", "src")))
    return jax.shard_map(shards, mesh=mesh, in_specs=in_specs, out_specs=out_specs, check_vma=False)
```

```python
import math

import jax
import numpy as np
import jax.numpy as jnp
from jax import lax
from jax.sharding import PartitionSpec as P


def across(former, latter):
    return lax.dot_general(
        former, latter, (((1,), (1,)), ((), ())), preferred_element_type=jnp.float32
    )


def plain_dot(former, latter):
    return jnp.dot(former, latter, preferred_element_type=jnp.float32)


def as_half(values):
    return values.astype(jnp.bfloat16)


def lower_solve(right_side, lower, block_size, block_count):
    solved = []
    for index in range(block_count):
        segment = right_side[:, index * block_size : (index + 1) * block_size]
        if index:
            earlier = as_half(jnp.concatenate(solved, axis=1))
            segment = segment - across(
                earlier, lower[index * block_size : (index + 1) * block_size, : index * block_size]
            )
        solved.append(segment)
    return jnp.concatenate(solved, axis=1)


def upper_solve(right_side, upper, inverse, block_size, block_count):
    behind = []
    for index in reversed(range(block_count)):
        segment = right_side[:, index * block_size : (index + 1) * block_size]
        if behind:
            segment = segment - across(
                as_half(jnp.concatenate(behind, axis=1)),
                upper[index * block_size : (index + 1) * block_size, (index + 1) * block_size :],
            )
        behind.insert(0, across(as_half(segment), inverse[index]))
    return jnp.concatenate(behind, axis=1)


def upper_t_solve(right_side, upper, inverse, block_size, block_count):
    solved = []
    for index in range(block_count):
        segment = right_side[:, index * block_size : (index + 1) * block_size]
        if index:
            earlier = as_half(jnp.concatenate(solved, axis=1))
            segment = segment - plain_dot(
                earlier, upper[: index * block_size, index * block_size : (index + 1) * block_size]
            )
        solved.append(plain_dot(as_half(segment), inverse[index]))
    return jnp.concatenate(solved, axis=1)


def lower_t_solve(right_side, lower, block_size, block_count):
    behind = []
    for index in reversed(range(block_count)):
        segment = right_side[:, index * block_size : (index + 1) * block_size]
        if behind:
            segment = segment - plain_dot(
                as_half(jnp.concatenate(behind, axis=1)),
                lower[(index + 1) * block_size :, index * block_size : (index + 1) * block_size],
            )
        behind.insert(0, segment)
    return jnp.concatenate(behind, axis=1)


def shards(
    src_cells,
    rec_cells,
    residual,
    pattern,
    leaf_lower,
    leaf_upper,
    leaf_inv,
    anc_lower,
    anc_upper,
    sep_inv,
    sep_lower,
    sep_upper,
):
    leaves = lax.axis_size("leaf")
    levels = leaves.bit_length() - 1
    device = lax.axis_index("leaf")
    block_size = leaf_inv.shape[1]
    block_count = leaf_inv.shape[0]
    cell_count = leaf_lower.shape[1]
    source_count = src_cells.shape[0]
    factor = 1.0 / math.sqrt(source_count * lax.axis_size("src"))
    present = pattern.astype(jnp.float32)

    def level_mask(height):
        level_row = present[height] * (jnp.arange(1, levels + 1) > height).astype(jnp.float32)
        return jnp.repeat(level_row, block_size)

    def blocks_of(values):
        return [values[:, k * block_size : (k + 1) * block_size] for k in range(values.shape[1] // block_size)]

    columns = lax.broadcasted_iota(jnp.int32, (source_count, cell_count), 1)
    forcing = (src_cells[:, None] - device * cell_count == columns).astype(jnp.float32)
    receiver_hits = (
        rec_cells[:, None] == lax.broadcasted_iota(jnp.int32, (rec_cells.shape[0], cell_count), 1)
    ).astype(jnp.float32)
    adjoint_rhs = jnp.dot(residual, receiver_hits, precision=lax.Precision.HIGHEST)

    base_mask = level_mask(0)
    y_leaf = lower_solve(forcing, leaf_lower, block_size, block_count)
    z_leaf = upper_t_solve(adjoint_rhs, leaf_upper, leaf_inv, block_size, block_count)
    forward_sums = blocks_of(across(as_half(y_leaf), anc_lower) * base_mask)
    adjoint_sums = blocks_of(plain_dot(as_half(z_leaf), anc_upper) * base_mask)

    lower_panels, upper_panels, inverse_panels, pattern_rows = [], [], [], []
    for height in range(1, levels + 1):
        lower_panels.append(sep_lower[height - 1, height * block_size :, :])
        upper_panels.append(sep_upper[height - 1, :, height * block_size :])
        inverse_panels.append(sep_inv[height - 1])
        row = pattern[height].astype(jnp.bfloat16)[None, :]
        pattern_rows.append(jnp.pad(row, ((0, 7), (0, block_size - levels))))

    def chain_mask(height):
        level_row = pattern_rows[height - 1][0, :levels].astype(jnp.float32)
        level_row = level_row * (jnp.arange(1, levels + 1) > height).astype(jnp.float32)
        return jnp.repeat(level_row, block_size)[height * block_size :]

    def exchange(values, pairs):
        pieces = [piece for piece in values]
        incoming = lax.ppermute(jnp.concatenate(pieces, axis=0), "leaf", pairs)
        received, row = [], 0
        for piece in pieces:
            received.append(incoming[row : row + piece.shape[0]])
            row += piece.shape[0]
        return received

    pieces, piece_levels = [], []
    for height in range(1, levels + 1):
        node_pieces = [lower_panels[height - 1]] + blocks_of(upper_panels[height - 1])
        node_pieces += [inverse_panels[height - 1], pattern_rows[height - 1]]
        pieces += node_pieces
        piece_levels += [height] * len(node_pieces)
    row_levels = np.concatenate([np.full(piece.shape[0], height) for piece, height in zip(pieces, piece_levels)])
    panel_buffer = jnp.concatenate(pieces, axis=0)
    for height in range(1, levels + 1):
        stride = 1 << (height - 1)
        pairs = [(index, index ^ stride) for index in range(leaves)]
        received = lax.ppermute(panel_buffer, "leaf", pairs)
        takes = [jnp.zeros((), jnp.bool_)]
        for upper_level in range(1, levels + 1):
            place = device % (1 << upper_level)
            takes.append(jnp.logical_and(upper_level >= height, jnp.logical_and(place >= stride, place < 2 * stride)))
        take_rows = jnp.stack(takes)[row_levels]
        panel_buffer = jnp.where(take_rows[:, None], received, panel_buffer)
    row = 0
    for height in range(1, levels + 1):
        width = levels - height
        lower_panels[height - 1] = panel_buffer[row : row + width * block_size]
        row += width * block_size
        if width:
            upper_panels[height - 1] = jnp.concatenate(
                [panel_buffer[row + k * block_size : row + (k + 1) * block_size] for k in range(width)], axis=1
            )
        row += width * block_size
        inverse_panels[height - 1] = panel_buffer[row : row + block_size]
        row += block_size
        pattern_rows[height - 1] = panel_buffer[row : row + 8]
        row += 8

    forward_nodes, adjoint_nodes = [], []
    for height in range(1, levels + 1):
        stride = 1 << (height - 1)
        pairs = [(index, index ^ stride) for index in range(leaves)]
        forward_sums = [mine + theirs for mine, theirs in zip(forward_sums, exchange(forward_sums, pairs))]
        forward_node = -forward_sums[0]
        forward_nodes.append(forward_node)
        forward_sums = forward_sums[1:]
        if forward_sums:
            forward_coupling = blocks_of(
                across(as_half(forward_node), lower_panels[height - 1]) * chain_mask(height)
            )
            forward_sums = [total + extra for total, extra in zip(forward_sums, forward_coupling)]
        adjoint_sums = [mine + theirs for mine, theirs in zip(adjoint_sums, exchange(adjoint_sums, pairs))]
        adjoint_node = plain_dot(as_half(-adjoint_sums[0]), inverse_panels[height - 1])
        adjoint_nodes.append(adjoint_node)
        adjoint_sums = adjoint_sums[1:]
        if adjoint_sums:
            adjoint_coupling = blocks_of(
                plain_dot(as_half(adjoint_node), upper_panels[height - 1]) * chain_mask(height)
            )
            adjoint_sums = [total + extra for total, extra in zip(adjoint_sums, adjoint_coupling)]

    forward_above, adjoint_above = [], []
    for height in range(levels, 0, -1):
        right_side = forward_nodes[height - 1]
        adjoint_value = adjoint_nodes[height - 1]
        if forward_above:
            right_side = right_side - across(
                as_half(jnp.concatenate(forward_above, axis=1) * chain_mask(height)), upper_panels[height - 1]
            )
            adjoint_value = adjoint_value - plain_dot(
                as_half(jnp.concatenate(adjoint_above, axis=1) * chain_mask(height)), lower_panels[height - 1]
            )
        forward_above.insert(0, across(as_half(right_side), inverse_panels[height - 1]))
        adjoint_above.insert(0, adjoint_value)
    forward_above = jnp.concatenate(forward_above, axis=1)
    adjoint_above = jnp.concatenate(adjoint_above, axis=1)

    forward_remain = y_leaf - across(as_half(forward_above * base_mask), anc_upper)
    forward_field = upper_solve(forward_remain, leaf_upper, leaf_inv, block_size, block_count)
    adjoint_remain = z_leaf - plain_dot(as_half(adjoint_above * base_mask), anc_lower)
    adjoint_field = lower_t_solve(adjoint_remain, leaf_lower, block_size, block_count)
    spread = lax.axis_size("src")
    product_field = (forward_field * adjoint_field).reshape(source_count, spread, cell_count // spread)
    partial_gradient = jnp.sum(product_field, axis=0)
    place = lax.axis_index("src")
    bit = spread // 2
    while bit:
        half = partial_gradient.shape[0] // 2
        upper = (place & bit) != 0
        outgoing = jnp.where(upper, partial_gradient[:half], partial_gradient[half:])
        kept = jnp.where(upper, partial_gradient[half:], partial_gradient[:half])
        pairs = [(index, index ^ bit) for index in range(spread)]
        partial_gradient = kept + lax.ppermute(outgoing, "src", pairs)
        bit //= 2
    gradient = partial_gradient.reshape(-1) * factor
    return (forward_field, adjoint_field, gradient)


def solution(mesh):
    in_specs = (
        P("src"),
        P("leaf"),
        P("src", "leaf"),
        P("leaf", None),
        P("leaf", None),
        P("leaf", None),
        P("leaf", None, None),
        P("leaf", None),
        P("leaf", None),
        P("leaf", None, None),
        P("leaf", None, None),
        P("leaf", None, None),
    )
    out_specs = (P("src", "leaf"), P("src", "leaf"), P(("leaf", "src")))
    return jax.shard_map(shards, mesh=mesh, in_specs=in_specs, out_specs=out_specs, check_vma=False)
```

```python
import math

import jax
import jax.numpy as jnp
from jax import lax
from jax.sharding import PartitionSpec as P


def across(former, latter):
    return lax.dot_general(
        former, latter, (((1,), (1,)), ((), ())), preferred_element_type=jnp.float32
    )


def plain_dot(former, latter):
    return jnp.dot(former, latter, preferred_element_type=jnp.float32)


def as_half(values):
    return values.astype(jnp.bfloat16)


def lower_solve(right_side, lower, block_size, block_count):
    solved = []
    for index in range(block_count):
        segment = right_side[:, index * block_size : (index + 1) * block_size]
        if index:
            earlier = as_half(jnp.concatenate(solved, axis=1))
            segment = segment - across(
                earlier, lower[index * block_size : (index + 1) * block_size, : index * block_size]
            )
        solved.append(segment)
    return jnp.concatenate(solved, axis=1)


def upper_solve(right_side, upper, inverse, block_size, block_count):
    behind = []
    for index in reversed(range(block_count)):
        segment = right_side[:, index * block_size : (index + 1) * block_size]
        if behind:
            segment = segment - across(
                as_half(jnp.concatenate(behind, axis=1)),
                upper[index * block_size : (index + 1) * block_size, (index + 1) * block_size :],
            )
        behind.insert(0, across(as_half(segment), inverse[index]))
    return jnp.concatenate(behind, axis=1)


def upper_t_solve(right_side, upper, inverse, block_size, block_count):
    solved = []
    for index in range(block_count):
        segment = right_side[:, index * block_size : (index + 1) * block_size]
        if index:
            earlier = as_half(jnp.concatenate(solved, axis=1))
            segment = segment - plain_dot(
                earlier, upper[: index * block_size, index * block_size : (index + 1) * block_size]
            )
        solved.append(plain_dot(as_half(segment), inverse[index]))
    return jnp.concatenate(solved, axis=1)


def lower_t_solve(right_side, lower, block_size, block_count):
    behind = []
    for index in reversed(range(block_count)):
        segment = right_side[:, index * block_size : (index + 1) * block_size]
        if behind:
            segment = segment - plain_dot(
                as_half(jnp.concatenate(behind, axis=1)),
                lower[(index + 1) * block_size :, index * block_size : (index + 1) * block_size],
            )
        behind.insert(0, segment)
    return jnp.concatenate(behind, axis=1)


def shards(
    src_cells,
    rec_cells,
    residual,
    pattern,
    leaf_lower,
    leaf_upper,
    leaf_inv,
    anc_lower,
    anc_upper,
    sep_inv,
    sep_lower,
    sep_upper,
):
    leaves = lax.axis_size("leaf")
    levels = leaves.bit_length() - 1
    device = lax.axis_index("leaf")
    block_size = leaf_inv.shape[1]
    block_count = leaf_inv.shape[0]
    cell_count = leaf_lower.shape[1]
    source_count = src_cells.shape[0]
    factor = 1.0 / math.sqrt(source_count * lax.axis_size("src"))
    present = pattern.astype(jnp.float32)

    def level_mask(height):
        level_row = present[height] * (jnp.arange(1, levels + 1) > height).astype(jnp.float32)
        return jnp.repeat(level_row, block_size)

    def blocks_of(values):
        return [values[:, k * block_size : (k + 1) * block_size] for k in range(values.shape[1] // block_size)]

    columns = lax.broadcasted_iota(jnp.int32, (source_count, cell_count), 1)
    forcing = (src_cells[:, None] - device * cell_count == columns).astype(jnp.float32)
    receiver_hits = (
        rec_cells[:, None] == lax.broadcasted_iota(jnp.int32, (rec_cells.shape[0], cell_count), 1)
    ).astype(jnp.float32)
    adjoint_rhs = jnp.dot(residual, receiver_hits, precision=lax.Precision.HIGHEST)

    base_mask = level_mask(0)
    y_leaf = lower_solve(forcing, leaf_lower, block_size, block_count)
    z_leaf = upper_t_solve(adjoint_rhs, leaf_upper, leaf_inv, block_size, block_count)
    forward_sums = blocks_of(across(as_half(y_leaf), anc_lower) * base_mask)
    adjoint_sums = blocks_of(plain_dot(as_half(z_leaf), anc_upper) * base_mask)

    lower_panels, upper_panels, inverse_panels = [], [], []
    for height in range(1, levels + 1):
        mask = level_mask(height)[height * block_size :]
        lower_panels.append(sep_lower[height - 1, height * block_size :, :] * mask[:, None].astype(jnp.bfloat16))
        upper_panels.append(sep_upper[height - 1, :, height * block_size :] * mask[None, :].astype(jnp.bfloat16))
        inverse_panels.append(sep_inv[height - 1])

    def exchange(values, pairs):
        pieces = [piece for piece in values]
        incoming = lax.ppermute(jnp.concatenate(pieces, axis=0), "leaf", pairs)
        received, row = [], 0
        for piece in pieces:
            received.append(incoming[row : row + piece.shape[0]])
            row += piece.shape[0]
        return received

    for height in range(1, levels + 1):
        stride = 1 << (height - 1)
        pairs = [(index, index ^ stride) for index in range(leaves)]
        pieces = []
        for upper_level in range(height, levels + 1):
            pieces.append(lower_panels[upper_level - 1])
            pieces.extend(blocks_of(upper_panels[upper_level - 1]))
            pieces.append(inverse_panels[upper_level - 1])
        received = exchange(pieces, pairs)
        for upper_level in range(height, levels + 1):
            place = device % (1 << upper_level)
            take = jnp.logical_and(place >= stride, place < 2 * stride)
            width = levels - upper_level
            lower_in = received[0]
            upper_in = jnp.concatenate(received[1 : 1 + width] or [upper_panels[upper_level - 1]], axis=1)
            inverse_in = received[1 + width]
            received = received[2 + width :]
            lower_panels[upper_level - 1] = jnp.where(take, lower_in, lower_panels[upper_level - 1])
            upper_panels[upper_level - 1] = jnp.where(take, upper_in, upper_panels[upper_level - 1])
            inverse_panels[upper_level - 1] = jnp.where(take, inverse_in, inverse_panels[upper_level - 1])

    forward_nodes, adjoint_nodes = [], []
    for height in range(1, levels + 1):
        stride = 1 << (height - 1)
        pairs = [(index, index ^ stride) for index in range(leaves)]
        forward_sums = [mine + theirs for mine, theirs in zip(forward_sums, exchange(forward_sums, pairs))]
        forward_node = -forward_sums[0]
        forward_nodes.append(forward_node)
        forward_sums = forward_sums[1:]
        if forward_sums:
            forward_coupling = blocks_of(across(as_half(forward_node), lower_panels[height - 1]))
            forward_sums = [total + extra for total, extra in zip(forward_sums, forward_coupling)]
        adjoint_sums = [mine + theirs for mine, theirs in zip(adjoint_sums, exchange(adjoint_sums, pairs))]
        adjoint_node = plain_dot(as_half(-adjoint_sums[0]), inverse_panels[height - 1])
        adjoint_nodes.append(adjoint_node)
        adjoint_sums = adjoint_sums[1:]
        if adjoint_sums:
            adjoint_coupling = blocks_of(plain_dot(as_half(adjoint_node), upper_panels[height - 1]))
            adjoint_sums = [total + extra for total, extra in zip(adjoint_sums, adjoint_coupling)]

    forward_above, adjoint_above = [], []
    for height in range(levels, 0, -1):
        right_side = forward_nodes[height - 1]
        adjoint_value = adjoint_nodes[height - 1]
        if forward_above:
            right_side = right_side - across(
                as_half(jnp.concatenate(forward_above, axis=1)), upper_panels[height - 1]
            )
            adjoint_value = adjoint_value - plain_dot(
                as_half(jnp.concatenate(adjoint_above, axis=1)), lower_panels[height - 1]
            )
        forward_above.insert(0, across(as_half(right_side), inverse_panels[height - 1]))
        adjoint_above.insert(0, adjoint_value)
    forward_above = jnp.concatenate(forward_above, axis=1)
    adjoint_above = jnp.concatenate(adjoint_above, axis=1)

    forward_remain = y_leaf - across(as_half(forward_above * base_mask), anc_upper)
    forward_field = upper_solve(forward_remain, leaf_upper, leaf_inv, block_size, block_count)
    adjoint_remain = z_leaf - plain_dot(as_half(adjoint_above * base_mask), anc_lower)
    adjoint_field = lower_t_solve(adjoint_remain, leaf_lower, block_size, block_count)
    spread = lax.axis_size("src")
    product_field = (forward_field * adjoint_field).reshape(source_count, spread, cell_count // spread)
    partial_gradient = jnp.sum(product_field, axis=0)
    place = lax.axis_index("src")
    bit = spread // 2
    while bit:
        half = partial_gradient.shape[0] // 2
        upper = (place & bit) != 0
        outgoing = jnp.where(upper, partial_gradient[:half], partial_gradient[half:])
        kept = jnp.where(upper, partial_gradient[half:], partial_gradient[:half])
        pairs = [(index, index ^ bit) for index in range(spread)]
        partial_gradient = kept + lax.ppermute(outgoing, "src", pairs)
        bit //= 2
    gradient = partial_gradient.reshape(-1) * factor
    return (forward_field, adjoint_field, gradient)


def solution(mesh):
    in_specs = (
        P("src"),
        P("leaf"),
        P("src", "leaf"),
        P("leaf", None),
        P("leaf", None),
        P("leaf", None),
        P("leaf", None, None),
        P("leaf", None),
        P("leaf", None),
        P("leaf", None, None),
        P("leaf", None, None),
        P("leaf", None, None),
    )
    out_specs = (P("src", "leaf"), P("src", "leaf"), P(("leaf", "src")))
    return jax.shard_map(shards, mesh=mesh, in_specs=in_specs, out_specs=out_specs, check_vma=False)
```

```python
import math

import jax
import jax.numpy as jnp
from jax import lax
from jax.sharding import PartitionSpec as P


def across(former, latter):
    return lax.dot_general(
        former, latter, (((1,), (1,)), ((), ())), preferred_element_type=jnp.float32
    )


def plain_dot(former, latter):
    return jnp.dot(former, latter, preferred_element_type=jnp.float32)


def as_half(values):
    return values.astype(jnp.bfloat16)


def lower_solve(right_side, lower, block_size, block_count):
    solved = []
    for index in range(block_count):
        segment = right_side[:, index * block_size : (index + 1) * block_size]
        if index:
            earlier = as_half(jnp.concatenate(solved, axis=1))
            segment = segment - across(
                earlier, lower[index * block_size : (index + 1) * block_size, : index * block_size]
            )
        solved.append(segment)
    return jnp.concatenate(solved, axis=1)


def upper_solve(right_side, upper, inverse, block_size, block_count):
    behind = []
    for index in reversed(range(block_count)):
        segment = right_side[:, index * block_size : (index + 1) * block_size]
        if behind:
            segment = segment - across(
                as_half(jnp.concatenate(behind, axis=1)),
                upper[index * block_size : (index + 1) * block_size, (index + 1) * block_size :],
            )
        behind.insert(0, across(as_half(segment), inverse[index]))
    return jnp.concatenate(behind, axis=1)


def upper_t_solve(right_side, upper, inverse, block_size, block_count):
    solved = []
    for index in range(block_count):
        segment = right_side[:, index * block_size : (index + 1) * block_size]
        if index:
            earlier = as_half(jnp.concatenate(solved, axis=1))
            segment = segment - plain_dot(
                earlier, upper[: index * block_size, index * block_size : (index + 1) * block_size]
            )
        solved.append(plain_dot(as_half(segment), inverse[index]))
    return jnp.concatenate(solved, axis=1)


def lower_t_solve(right_side, lower, block_size, block_count):
    behind = []
    for index in reversed(range(block_count)):
        segment = right_side[:, index * block_size : (index + 1) * block_size]
        if behind:
            segment = segment - plain_dot(
                as_half(jnp.concatenate(behind, axis=1)),
                lower[(index + 1) * block_size :, index * block_size : (index + 1) * block_size],
            )
        behind.insert(0, segment)
    return jnp.concatenate(behind, axis=1)


def shards(
    src_cells,
    rec_cells,
    residual,
    pattern,
    leaf_lower,
    leaf_upper,
    leaf_inv,
    anc_lower,
    anc_upper,
    sep_inv,
    sep_lower,
    sep_upper,
):
    leaves = lax.axis_size("leaf")
    levels = leaves.bit_length() - 1
    device = lax.axis_index("leaf")
    block_size = leaf_inv.shape[1]
    block_count = leaf_inv.shape[0]
    cell_count = leaf_lower.shape[1]
    source_count = src_cells.shape[0]
    factor = 1.0 / math.sqrt(source_count * lax.axis_size("src"))
    def level_mask(height):
        level_row = jnp.logical_and(pattern[height] != 0, jnp.arange(1, levels + 1) > height)
        return jnp.repeat(level_row, block_size)

    def masked(values, keep):
        return jnp.where(keep, values, jnp.zeros_like(values))

    def blocks_of(values):
        return [values[:, k * block_size : (k + 1) * block_size] for k in range(values.shape[1] // block_size)]

    columns = lax.broadcasted_iota(jnp.int32, (source_count, cell_count), 1)
    forcing = (src_cells[:, None] - device * cell_count == columns).astype(jnp.float32)
    receiver_hits = (
        rec_cells[:, None] == lax.broadcasted_iota(jnp.int32, (rec_cells.shape[0], cell_count), 1)
    ).astype(jnp.float32)
    adjoint_rhs = jnp.dot(residual, receiver_hits, precision=lax.Precision.HIGHEST)

    base_mask = level_mask(0)
    y_leaf = lower_solve(forcing, leaf_lower, block_size, block_count)
    z_leaf = upper_t_solve(adjoint_rhs, leaf_upper, leaf_inv, block_size, block_count)
    forward_sums = blocks_of(masked(across(as_half(y_leaf), anc_lower), base_mask))
    adjoint_sums = blocks_of(masked(plain_dot(as_half(z_leaf), anc_upper), base_mask))

    lower_panels, upper_panels, inverse_panels = [], [], []
    for height in range(1, levels + 1):
        mask = level_mask(height)[height * block_size :]
        lower_panels.append(masked(sep_lower[height - 1, height * block_size :, :], mask[:, None]))
        upper_panels.append(masked(sep_upper[height - 1, :, height * block_size :], mask[None, :]))
        inverse_panels.append(sep_inv[height - 1])

    def exchange(values, pairs):
        pieces = [piece for piece in values]
        incoming = lax.ppermute(jnp.concatenate(pieces, axis=0), "leaf", pairs)
        received, row = [], 0
        for piece in pieces:
            received.append(incoming[row : row + piece.shape[0]])
            row += piece.shape[0]
        return received

    for height in range(1, levels + 1):
        stride = 1 << (height - 1)
        pairs = [(index, index ^ stride) for index in range(leaves)]
        pieces = []
        for upper_level in range(height, levels + 1):
            pieces.append(lower_panels[upper_level - 1])
            pieces.extend(blocks_of(upper_panels[upper_level - 1]))
            pieces.append(inverse_panels[upper_level - 1])
        received = exchange(pieces, pairs)
        for upper_level in range(height, levels + 1):
            place = device % (1 << upper_level)
            take = jnp.logical_and(place >= stride, place < 2 * stride)
            width = levels - upper_level
            lower_in = received[0]
            upper_in = jnp.concatenate(received[1 : 1 + width] or [upper_panels[upper_level - 1]], axis=1)
            inverse_in = received[1 + width]
            received = received[2 + width :]
            lower_panels[upper_level - 1] = jnp.where(take, lower_in, lower_panels[upper_level - 1])
            upper_panels[upper_level - 1] = jnp.where(take, upper_in, upper_panels[upper_level - 1])
            inverse_panels[upper_level - 1] = jnp.where(take, inverse_in, inverse_panels[upper_level - 1])

    forward_nodes, adjoint_nodes = [], []
    for height in range(1, levels + 1):
        stride = 1 << (height - 1)
        pairs = [(index, index ^ stride) for index in range(leaves)]
        forward_sums = [mine + theirs for mine, theirs in zip(forward_sums, exchange(forward_sums, pairs))]
        forward_node = -forward_sums[0]
        forward_nodes.append(forward_node)
        forward_sums = forward_sums[1:]
        if forward_sums:
            forward_coupling = blocks_of(across(as_half(forward_node), lower_panels[height - 1]))
            forward_sums = [total + extra for total, extra in zip(forward_sums, forward_coupling)]
        adjoint_sums = [mine + theirs for mine, theirs in zip(adjoint_sums, exchange(adjoint_sums, pairs))]
        adjoint_node = plain_dot(as_half(-adjoint_sums[0]), inverse_panels[height - 1])
        adjoint_nodes.append(adjoint_node)
        adjoint_sums = adjoint_sums[1:]
        if adjoint_sums:
            adjoint_coupling = blocks_of(plain_dot(as_half(adjoint_node), upper_panels[height - 1]))
            adjoint_sums = [total + extra for total, extra in zip(adjoint_sums, adjoint_coupling)]

    forward_above, adjoint_above = [], []
    for height in range(levels, 0, -1):
        right_side = forward_nodes[height - 1]
        adjoint_value = adjoint_nodes[height - 1]
        if forward_above:
            right_side = right_side - across(
                as_half(jnp.concatenate(forward_above, axis=1)), upper_panels[height - 1]
            )
            adjoint_value = adjoint_value - plain_dot(
                as_half(jnp.concatenate(adjoint_above, axis=1)), lower_panels[height - 1]
            )
        forward_above.insert(0, across(as_half(right_side), inverse_panels[height - 1]))
        adjoint_above.insert(0, adjoint_value)
    forward_above = jnp.concatenate(forward_above, axis=1)
    adjoint_above = jnp.concatenate(adjoint_above, axis=1)

    forward_remain = y_leaf - across(as_half(masked(forward_above, base_mask)), anc_upper)
    forward_field = upper_solve(forward_remain, leaf_upper, leaf_inv, block_size, block_count)
    adjoint_remain = z_leaf - plain_dot(as_half(masked(adjoint_above, base_mask)), anc_lower)
    adjoint_field = lower_t_solve(adjoint_remain, leaf_lower, block_size, block_count)
    spread = lax.axis_size("src")
    product_field = (forward_field * adjoint_field).reshape(source_count, spread, cell_count // spread)
    partial_gradient = jnp.sum(product_field, axis=0)
    place = lax.axis_index("src")
    bit = spread // 2
    while bit:
        half = partial_gradient.shape[0] // 2
        upper = (place & bit) != 0
        outgoing = jnp.where(upper, partial_gradient[:half], partial_gradient[half:])
        kept = jnp.where(upper, partial_gradient[half:], partial_gradient[:half])
        pairs = [(index, index ^ bit) for index in range(spread)]
        partial_gradient = kept + lax.ppermute(outgoing, "src", pairs)
        bit //= 2
    gradient = partial_gradient.reshape(-1) * factor
    return (forward_field, adjoint_field, gradient)


def solution(mesh):
    in_specs = (
        P("src"),
        P("leaf"),
        P("src", "leaf"),
        P("leaf", None),
        P("leaf", None),
        P("leaf", None),
        P("leaf", None, None),
        P("leaf", None),
        P("leaf", None),
        P("leaf", None, None),
        P("leaf", None, None),
        P("leaf", None, None),
    )
    out_specs = (P("src", "leaf"), P("src", "leaf"), P(("leaf", "src")))
    return jax.shard_map(shards, mesh=mesh, in_specs=in_specs, out_specs=out_specs, check_vma=False)
```

```python
import math

import jax
import jax.numpy as jnp
from jax import lax
from jax.sharding import PartitionSpec as P


def across(former, latter):
    return lax.dot_general(
        former, latter, (((1,), (1,)), ((), ())), preferred_element_type=jnp.float32
    )


def plain_dot(former, latter):
    return jnp.dot(former, latter, preferred_element_type=jnp.float32)


def as_half(values):
    return values.astype(jnp.bfloat16)


def lower_solve(right_side, lower, block_size, block_count):
    solved = []
    for index in range(block_count):
        segment = right_side[:, index * block_size : (index + 1) * block_size]
        if index:
            earlier = as_half(jnp.concatenate(solved, axis=1))
            segment = segment - across(
                earlier, lower[index * block_size : (index + 1) * block_size, : index * block_size]
            )
        solved.append(segment)
    return jnp.concatenate(solved, axis=1)


def upper_solve(right_side, upper, inverse, block_size, block_count):
    behind = []
    for index in reversed(range(block_count)):
        segment = right_side[:, index * block_size : (index + 1) * block_size]
        if behind:
            segment = segment - across(
                as_half(jnp.concatenate(behind, axis=1)),
                upper[index * block_size : (index + 1) * block_size, (index + 1) * block_size :],
            )
        behind.insert(0, across(as_half(segment), inverse[index]))
    return jnp.concatenate(behind, axis=1)


def upper_t_solve(right_side, upper, inverse, block_size, block_count):
    solved = []
    for index in range(block_count):
        segment = right_side[:, index * block_size : (index + 1) * block_size]
        if index:
            earlier = as_half(jnp.concatenate(solved, axis=1))
            segment = segment - plain_dot(
                earlier, upper[: index * block_size, index * block_size : (index + 1) * block_size]
            )
        solved.append(plain_dot(as_half(segment), inverse[index]))
    return jnp.concatenate(solved, axis=1)


def lower_t_solve(right_side, lower, block_size, block_count):
    behind = []
    for index in reversed(range(block_count)):
        segment = right_side[:, index * block_size : (index + 1) * block_size]
        if behind:
            segment = segment - plain_dot(
                as_half(jnp.concatenate(behind, axis=1)),
                lower[(index + 1) * block_size :, index * block_size : (index + 1) * block_size],
            )
        behind.insert(0, segment)
    return jnp.concatenate(behind, axis=1)


def shards(
    src_cells,
    rec_cells,
    residual,
    pattern,
    leaf_lower,
    leaf_upper,
    leaf_inv,
    anc_lower,
    anc_upper,
    sep_inv,
    sep_lower,
    sep_upper,
):
    leaves = lax.axis_size("leaf")
    levels = leaves.bit_length() - 1
    device = lax.axis_index("leaf")
    block_size = leaf_inv.shape[1]
    block_count = leaf_inv.shape[0]
    cell_count = leaf_lower.shape[1]
    source_count = src_cells.shape[0]
    factor = 1.0 / math.sqrt(source_count * lax.axis_size("src"))
    def level_mask(height):
        level_row = jnp.logical_and(pattern[height] != 0, jnp.arange(1, levels + 1) > height)
        return jnp.repeat(level_row, block_size)

    def masked(values, keep):
        return jnp.where(keep, values, jnp.zeros_like(values))

    def blocks_of(values):
        return [values[:, k * block_size : (k + 1) * block_size] for k in range(values.shape[1] // block_size)]

    columns = lax.broadcasted_iota(jnp.int32, (source_count, cell_count), 1)
    forcing = (src_cells[:, None] - device * cell_count == columns).astype(jnp.float32)
    receiver_hits = (
        rec_cells[:, None] == lax.broadcasted_iota(jnp.int32, (rec_cells.shape[0], cell_count), 1)
    ).astype(jnp.float32)
    adjoint_rhs = jnp.dot(residual, receiver_hits, precision=lax.Precision.HIGHEST)

    base_mask = level_mask(0)
    y_leaf = lower_solve(forcing, leaf_lower, block_size, block_count)
    z_leaf = upper_t_solve(adjoint_rhs, leaf_upper, leaf_inv, block_size, block_count)
    forward_sums = blocks_of(masked(across(as_half(y_leaf), anc_lower), base_mask))
    adjoint_sums = blocks_of(masked(plain_dot(as_half(z_leaf), anc_upper), base_mask))

    lower_panels, upper_panels, inverse_panels = [], [], []
    for height in range(1, levels + 1):
        mask = level_mask(height)[height * block_size :]
        lower_panels.append(masked(sep_lower[height - 1, height * block_size :, :], mask[:, None]))
        upper_panels.append(masked(sep_upper[height - 1, :, height * block_size :], mask[None, :]))
        inverse_panels.append(sep_inv[height - 1])

    def exchange(values, pairs):
        pieces = [piece for piece in values]
        joined = pieces[0] if len(pieces) == 1 else jnp.concatenate(pieces, axis=0)
        incoming = lax.ppermute(joined, "leaf", pairs)
        received, row = [], 0
        for piece in pieces:
            received.append(incoming[row : row + piece.shape[0]])
            row += piece.shape[0]
        return received

    def level_pieces(height):
        pieces = [lower_panels[height - 1]] + blocks_of(upper_panels[height - 1]) + [inverse_panels[height - 1]]
        return [piece for piece in pieces if piece.shape[0]]

    arrivals = {}
    for offset in range(1, leaves):
        lowest = offset.bit_length()
        pairs = [(index, index ^ offset) for index in range(leaves)]
        received = exchange([piece for height in range(lowest, levels + 1) for piece in level_pieces(height)], pairs)
        for height in range(lowest, levels + 1):
            count = len(level_pieces(height))
            arrivals[offset, height] = received[:count]
            received = received[count:]
    for height in range(1, levels + 1):
        place = device % (1 << height)
        width = levels - height
        for offset in range(1, 1 << height):
            arrived = arrivals[offset, height]
            take = place == offset
            if width:
                lower_in = arrived[0]
                upper_in = jnp.concatenate(arrived[1 : 1 + width], axis=1)
                lower_panels[height - 1] = jnp.where(take, lower_in, lower_panels[height - 1])
                upper_panels[height - 1] = jnp.where(take, upper_in, upper_panels[height - 1])
            inverse_panels[height - 1] = jnp.where(take, arrived[-1], inverse_panels[height - 1])

    forward_nodes, adjoint_nodes = [], []
    for height in range(1, levels + 1):
        stride = 1 << (height - 1)
        pairs = [(index, index ^ stride) for index in range(leaves)]
        forward_sums = [mine + theirs for mine, theirs in zip(forward_sums, exchange(forward_sums, pairs))]
        forward_node = -forward_sums[0]
        forward_nodes.append(forward_node)
        forward_sums = forward_sums[1:]
        if forward_sums:
            forward_coupling = blocks_of(across(as_half(forward_node), lower_panels[height - 1]))
            forward_sums = [total + extra for total, extra in zip(forward_sums, forward_coupling)]
        adjoint_sums = [mine + theirs for mine, theirs in zip(adjoint_sums, exchange(adjoint_sums, pairs))]
        adjoint_node = plain_dot(as_half(-adjoint_sums[0]), inverse_panels[height - 1])
        adjoint_nodes.append(adjoint_node)
        adjoint_sums = adjoint_sums[1:]
        if adjoint_sums:
            adjoint_coupling = blocks_of(plain_dot(as_half(adjoint_node), upper_panels[height - 1]))
            adjoint_sums = [total + extra for total, extra in zip(adjoint_sums, adjoint_coupling)]

    forward_above, adjoint_above = [], []
    for height in range(levels, 0, -1):
        right_side = forward_nodes[height - 1]
        adjoint_value = adjoint_nodes[height - 1]
        if forward_above:
            right_side = right_side - across(
                as_half(jnp.concatenate(forward_above, axis=1)), upper_panels[height - 1]
            )
            adjoint_value = adjoint_value - plain_dot(
                as_half(jnp.concatenate(adjoint_above, axis=1)), lower_panels[height - 1]
            )
        forward_above.insert(0, across(as_half(right_side), inverse_panels[height - 1]))
        adjoint_above.insert(0, adjoint_value)
    forward_above = jnp.concatenate(forward_above, axis=1)
    adjoint_above = jnp.concatenate(adjoint_above, axis=1)

    forward_remain = y_leaf - across(as_half(masked(forward_above, base_mask)), anc_upper)
    forward_field = upper_solve(forward_remain, leaf_upper, leaf_inv, block_size, block_count)
    adjoint_remain = z_leaf - plain_dot(as_half(masked(adjoint_above, base_mask)), anc_lower)
    adjoint_field = lower_t_solve(adjoint_remain, leaf_lower, block_size, block_count)
    spread = lax.axis_size("src")
    product_field = (forward_field * adjoint_field).reshape(source_count, spread, cell_count // spread)
    partial_gradient = jnp.sum(product_field, axis=0)
    place = lax.axis_index("src")
    bit = spread // 2
    while bit:
        half = partial_gradient.shape[0] // 2
        upper = (place & bit) != 0
        outgoing = jnp.where(upper, partial_gradient[:half], partial_gradient[half:])
        kept = jnp.where(upper, partial_gradient[half:], partial_gradient[:half])
        pairs = [(index, index ^ bit) for index in range(spread)]
        partial_gradient = kept + lax.ppermute(outgoing, "src", pairs)
        bit //= 2
    gradient = partial_gradient.reshape(-1) * factor
    return (forward_field, adjoint_field, gradient)


def solution(mesh):
    in_specs = (
        P("src"),
        P("leaf"),
        P("src", "leaf"),
        P("leaf", None),
        P("leaf", None),
        P("leaf", None),
        P("leaf", None, None),
        P("leaf", None),
        P("leaf", None),
        P("leaf", None, None),
        P("leaf", None, None),
        P("leaf", None, None),
    )
    out_specs = (P("src", "leaf"), P("src", "leaf"), P(("leaf", "src")))
    return jax.shard_map(shards, mesh=mesh, in_specs=in_specs, out_specs=out_specs, check_vma=False)
```

```python
import math

import jax
import jax.numpy as jnp
from jax import lax
from jax.sharding import PartitionSpec as P


def across(former, latter):
    return lax.dot_general(
        former, latter, (((1,), (1,)), ((), ())), preferred_element_type=jnp.float32
    )


def plain_dot(former, latter):
    return jnp.dot(former, latter, preferred_element_type=jnp.float32)


def as_half(values):
    return values.astype(jnp.bfloat16)


def lower_solve(right_side, lower, block_size, block_count):
    solved = []
    for index in range(block_count):
        segment = right_side[:, index * block_size : (index + 1) * block_size]
        if index:
            earlier = as_half(jnp.concatenate(solved, axis=1))
            segment = segment - across(
                earlier, lower[index * block_size : (index + 1) * block_size, : index * block_size]
            )
        solved.append(segment)
    return jnp.concatenate(solved, axis=1)


def upper_solve(right_side, upper, inverse, block_size, block_count):
    behind = []
    for index in reversed(range(block_count)):
        segment = right_side[:, index * block_size : (index + 1) * block_size]
        if behind:
            segment = segment - across(
                as_half(jnp.concatenate(behind, axis=1)),
                upper[index * block_size : (index + 1) * block_size, (index + 1) * block_size :],
            )
        behind.insert(0, across(as_half(segment), inverse[index]))
    return jnp.concatenate(behind, axis=1)


def upper_t_solve(right_side, upper, inverse, block_size, block_count):
    solved = []
    for index in range(block_count):
        segment = right_side[:, index * block_size : (index + 1) * block_size]
        if index:
            earlier = as_half(jnp.concatenate(solved, axis=1))
            segment = segment - plain_dot(
                earlier, upper[: index * block_size, index * block_size : (index + 1) * block_size]
            )
        solved.append(plain_dot(as_half(segment), inverse[index]))
    return jnp.concatenate(solved, axis=1)


def lower_t_solve(right_side, lower, block_size, block_count):
    behind = []
    for index in reversed(range(block_count)):
        segment = right_side[:, index * block_size : (index + 1) * block_size]
        if behind:
            segment = segment - plain_dot(
                as_half(jnp.concatenate(behind, axis=1)),
                lower[(index + 1) * block_size :, index * block_size : (index + 1) * block_size],
            )
        behind.insert(0, segment)
    return jnp.concatenate(behind, axis=1)


def shards(
    src_cells,
    rec_cells,
    residual,
    pattern,
    leaf_lower,
    leaf_upper,
    leaf_inv,
    anc_lower,
    anc_upper,
    sep_inv,
    sep_lower,
    sep_upper,
):
    leaves = lax.axis_size("leaf")
    levels = leaves.bit_length() - 1
    device = lax.axis_index("leaf")
    block_size = leaf_inv.shape[1]
    block_count = leaf_inv.shape[0]
    cell_count = leaf_lower.shape[1]
    source_count = src_cells.shape[0]
    factor = 1.0 / math.sqrt(source_count * lax.axis_size("src"))
    def level_mask(height):
        level_row = jnp.logical_and(pattern[height] != 0, jnp.arange(1, levels + 1) > height)
        return jnp.repeat(level_row, block_size)

    def masked(values, keep):
        return jnp.where(keep, values, jnp.zeros_like(values))

    def blocks_of(values):
        return [values[:, k * block_size : (k + 1) * block_size] for k in range(values.shape[1] // block_size)]

    columns = lax.broadcasted_iota(jnp.int32, (source_count, cell_count), 1)
    forcing = (src_cells[:, None] - device * cell_count == columns).astype(jnp.float32)
    receiver_hits = (
        rec_cells[:, None] == lax.broadcasted_iota(jnp.int32, (rec_cells.shape[0], cell_count), 1)
    ).astype(jnp.float32)
    adjoint_rhs = jnp.dot(residual, receiver_hits, precision=lax.Precision.HIGHEST)

    base_mask = level_mask(0)
    y_leaf = lower_solve(forcing, leaf_lower, block_size, block_count)
    forward_sums = blocks_of(masked(across(as_half(y_leaf), anc_lower), base_mask))
    forward_sums, adjoint_rhs = lax.optimization_barrier((forward_sums, adjoint_rhs))
    z_leaf = upper_t_solve(adjoint_rhs, leaf_upper, leaf_inv, block_size, block_count)
    adjoint_sums = blocks_of(masked(plain_dot(as_half(z_leaf), anc_upper), base_mask))

    lower_panels, upper_panels, inverse_panels = [], [], []
    for height in range(1, levels + 1):
        mask = level_mask(height)[height * block_size :]
        lower_panels.append(masked(sep_lower[height - 1, height * block_size :, :], mask[:, None]))
        upper_panels.append(masked(sep_upper[height - 1, :, height * block_size :], mask[None, :]))
        inverse_panels.append(sep_inv[height - 1])

    def exchange(values, pairs):
        pieces = [piece for piece in values]
        incoming = lax.ppermute(jnp.concatenate(pieces, axis=0), "leaf", pairs)
        received, row = [], 0
        for piece in pieces:
            received.append(incoming[row : row + piece.shape[0]])
            row += piece.shape[0]
        return received

    for height in range(1, levels + 1):
        stride = 1 << (height - 1)
        pairs = [(index, index ^ stride) for index in range(leaves)]
        pieces = []
        for upper_level in range(height, levels + 1):
            pieces.append(lower_panels[upper_level - 1])
            pieces.extend(blocks_of(upper_panels[upper_level - 1]))
            pieces.append(inverse_panels[upper_level - 1])
        received = exchange(pieces, pairs)
        for upper_level in range(height, levels + 1):
            place = device % (1 << upper_level)
            take = jnp.logical_and(place >= stride, place < 2 * stride)
            width = levels - upper_level
            lower_in = received[0]
            upper_in = jnp.concatenate(received[1 : 1 + width] or [upper_panels[upper_level - 1]], axis=1)
            inverse_in = received[1 + width]
            received = received[2 + width :]
            lower_panels[upper_level - 1] = jnp.where(take, lower_in, lower_panels[upper_level - 1])
            upper_panels[upper_level - 1] = jnp.where(take, upper_in, upper_panels[upper_level - 1])
            inverse_panels[upper_level - 1] = jnp.where(take, inverse_in, inverse_panels[upper_level - 1])

    forward_nodes, adjoint_nodes = [], []
    for height in range(1, levels + 1):
        stride = 1 << (height - 1)
        pairs = [(index, index ^ stride) for index in range(leaves)]
        forward_sums = [mine + theirs for mine, theirs in zip(forward_sums, exchange(forward_sums, pairs))]
        forward_node = -forward_sums[0]
        forward_nodes.append(forward_node)
        forward_sums = forward_sums[1:]
        if forward_sums:
            forward_coupling = blocks_of(across(as_half(forward_node), lower_panels[height - 1]))
            forward_sums = [total + extra for total, extra in zip(forward_sums, forward_coupling)]
        adjoint_sums = [mine + theirs for mine, theirs in zip(adjoint_sums, exchange(adjoint_sums, pairs))]
        adjoint_node = plain_dot(as_half(-adjoint_sums[0]), inverse_panels[height - 1])
        adjoint_nodes.append(adjoint_node)
        adjoint_sums = adjoint_sums[1:]
        if adjoint_sums:
            adjoint_coupling = blocks_of(plain_dot(as_half(adjoint_node), upper_panels[height - 1]))
            adjoint_sums = [total + extra for total, extra in zip(adjoint_sums, adjoint_coupling)]

    forward_above, adjoint_above = [], []
    for height in range(levels, 0, -1):
        right_side = forward_nodes[height - 1]
        adjoint_value = adjoint_nodes[height - 1]
        if forward_above:
            right_side = right_side - across(
                as_half(jnp.concatenate(forward_above, axis=1)), upper_panels[height - 1]
            )
            adjoint_value = adjoint_value - plain_dot(
                as_half(jnp.concatenate(adjoint_above, axis=1)), lower_panels[height - 1]
            )
        forward_above.insert(0, across(as_half(right_side), inverse_panels[height - 1]))
        adjoint_above.insert(0, adjoint_value)
    forward_above = jnp.concatenate(forward_above, axis=1)
    adjoint_above = jnp.concatenate(adjoint_above, axis=1)

    forward_remain = y_leaf - across(as_half(masked(forward_above, base_mask)), anc_upper)
    forward_field = upper_solve(forward_remain, leaf_upper, leaf_inv, block_size, block_count)
    adjoint_remain = z_leaf - plain_dot(as_half(masked(adjoint_above, base_mask)), anc_lower)
    adjoint_field = lower_t_solve(adjoint_remain, leaf_lower, block_size, block_count)
    spread = lax.axis_size("src")
    product_field = (forward_field * adjoint_field).reshape(source_count, spread, cell_count // spread)
    partial_gradient = jnp.sum(product_field, axis=0)
    place = lax.axis_index("src")
    bit = spread // 2
    while bit:
        half = partial_gradient.shape[0] // 2
        upper = (place & bit) != 0
        outgoing = jnp.where(upper, partial_gradient[:half], partial_gradient[half:])
        kept = jnp.where(upper, partial_gradient[half:], partial_gradient[:half])
        pairs = [(index, index ^ bit) for index in range(spread)]
        partial_gradient = kept + lax.ppermute(outgoing, "src", pairs)
        bit //= 2
    gradient = partial_gradient.reshape(-1) * factor
    return (forward_field, adjoint_field, gradient)


def solution(mesh):
    in_specs = (
        P("src"),
        P("leaf"),
        P("src", "leaf"),
        P("leaf", None),
        P("leaf", None),
        P("leaf", None),
        P("leaf", None, None),
        P("leaf", None),
        P("leaf", None),
        P("leaf", None, None),
        P("leaf", None, None),
        P("leaf", None, None),
    )
    out_specs = (P("src", "leaf"), P("src", "leaf"), P(("leaf", "src")))
    return jax.shard_map(shards, mesh=mesh, in_specs=in_specs, out_specs=out_specs, check_vma=False)
```

```python
import math

import jax
import jax.numpy as jnp
from jax import lax
from jax.sharding import PartitionSpec as P


def across(former, latter):
    return lax.dot_general(
        former, latter, (((1,), (1,)), ((), ())), preferred_element_type=jnp.float32
    )


def plain_dot(former, latter):
    return jnp.dot(former, latter, preferred_element_type=jnp.float32)


def as_half(values):
    return values.astype(jnp.bfloat16)


def lower_solve(right_side, lower, block_size, block_count):
    solved = []
    for index in range(block_count):
        segment = right_side[:, index * block_size : (index + 1) * block_size]
        if index:
            earlier = as_half(jnp.concatenate(solved, axis=1))
            segment = segment - across(
                earlier, lower[index * block_size : (index + 1) * block_size, : index * block_size]
            )
        solved.append(segment)
    return jnp.concatenate(solved, axis=1)


def upper_solve(right_side, upper, inverse, block_size, block_count):
    behind = []
    for index in reversed(range(block_count)):
        segment = right_side[:, index * block_size : (index + 1) * block_size]
        if behind:
            segment = segment - across(
                as_half(jnp.concatenate(behind, axis=1)),
                upper[index * block_size : (index + 1) * block_size, (index + 1) * block_size :],
            )
        behind.insert(0, across(as_half(segment), inverse[index]))
    return jnp.concatenate(behind, axis=1)


def upper_t_solve(right_side, upper, inverse, block_size, block_count):
    solved = []
    for index in range(block_count):
        segment = right_side[:, index * block_size : (index + 1) * block_size]
        if index:
            earlier = as_half(jnp.concatenate(solved, axis=1))
            segment = segment - plain_dot(
                earlier, upper[: index * block_size, index * block_size : (index + 1) * block_size]
            )
        solved.append(plain_dot(as_half(segment), inverse[index]))
    return jnp.concatenate(solved, axis=1)


def lower_t_solve(right_side, lower, block_size, block_count):
    behind = []
    for index in reversed(range(block_count)):
        segment = right_side[:, index * block_size : (index + 1) * block_size]
        if behind:
            segment = segment - plain_dot(
                as_half(jnp.concatenate(behind, axis=1)),
                lower[(index + 1) * block_size :, index * block_size : (index + 1) * block_size],
            )
        behind.insert(0, segment)
    return jnp.concatenate(behind, axis=1)


def shards(
    src_cells,
    rec_cells,
    residual,
    pattern,
    leaf_lower,
    leaf_upper,
    leaf_inv,
    anc_lower,
    anc_upper,
    sep_inv,
    sep_lower,
    sep_upper,
):
    leaves = lax.axis_size("leaf")
    levels = leaves.bit_length() - 1
    device = lax.axis_index("leaf")
    block_size = leaf_inv.shape[1]
    block_count = leaf_inv.shape[0]
    cell_count = leaf_lower.shape[1]
    source_count = src_cells.shape[0]
    factor = 1.0 / math.sqrt(source_count * lax.axis_size("src"))
    def level_mask(height):
        level_row = jnp.logical_and(pattern[height] != 0, jnp.arange(1, levels + 1) > height)
        return jnp.repeat(level_row, block_size)

    def masked(values, keep):
        return jnp.where(keep, values, jnp.zeros_like(values))

    def blocks_of(values):
        return [values[:, k * block_size : (k + 1) * block_size] for k in range(values.shape[1] // block_size)]

    columns = lax.broadcasted_iota(jnp.int32, (source_count, cell_count), 1)
    forcing = (src_cells[:, None] - device * cell_count == columns).astype(jnp.float32)
    receiver_hits = (
        rec_cells[:, None] == lax.broadcasted_iota(jnp.int32, (rec_cells.shape[0], cell_count), 1)
    ).astype(jnp.float32)
    adjoint_rhs = jnp.dot(residual, receiver_hits, precision=lax.Precision.HIGHEST)

    base_mask = level_mask(0)
    y_leaf = lower_solve(forcing, leaf_lower, block_size, block_count)
    z_leaf = upper_t_solve(adjoint_rhs, leaf_upper, leaf_inv, block_size, block_count)
    forward_sums = blocks_of(masked(across(as_half(y_leaf), anc_lower), base_mask))
    adjoint_sums = blocks_of(masked(plain_dot(as_half(z_leaf), anc_upper), base_mask))

    lower_panels, upper_panels, inverse_panels = [], [], []
    for height in range(1, levels + 1):
        mask = level_mask(height)[height * block_size :]
        lower_panels.append(masked(sep_lower[height - 1, height * block_size :, :], mask[:, None]))
        upper_panels.append(masked(sep_upper[height - 1, :, height * block_size :], mask[None, :]))
        inverse_panels.append(sep_inv[height - 1])

    def exchange(values, pairs):
        pieces = [piece for piece in values if piece.shape[0]]
        joined = pieces[0] if len(pieces) == 1 else jnp.concatenate(pieces, axis=0)
        incoming = lax.ppermute(joined, "leaf", pairs)
        received, row = [], 0
        for piece in values:
            received.append(incoming[row : row + piece.shape[0]] if piece.shape[0] else piece)
            row += piece.shape[0]
        return received

    for height in range(1, levels + 1):
        stride = 1 << (height - 1)
        pairs = [(index, index ^ stride) for index in range(leaves)]
        pieces = []
        for upper_level in range(height, levels + 1):
            pieces.append(lower_panels[upper_level - 1])
            pieces.extend(blocks_of(upper_panels[upper_level - 1]))
            pieces.append(inverse_panels[upper_level - 1])
        received = exchange(pieces, pairs)
        for upper_level in range(height, levels + 1):
            place = device % (1 << upper_level)
            take = jnp.logical_and(place >= stride, place < 2 * stride)
            width = levels - upper_level
            lower_in = received[0]
            upper_in = jnp.concatenate(received[1 : 1 + width] or [upper_panels[upper_level - 1]], axis=1)
            inverse_in = received[1 + width]
            received = received[2 + width :]
            lower_panels[upper_level - 1] = jnp.where(take, lower_in, lower_panels[upper_level - 1])
            upper_panels[upper_level - 1] = jnp.where(take, upper_in, upper_panels[upper_level - 1])
            inverse_panels[upper_level - 1] = jnp.where(take, inverse_in, inverse_panels[upper_level - 1])

    forward_nodes, adjoint_nodes = [], []
    for height in range(1, levels + 1):
        stride = 1 << (height - 1)
        pairs = [(index, index ^ stride) for index in range(leaves)]
        forward_sums = [mine + theirs for mine, theirs in zip(forward_sums, exchange(forward_sums, pairs))]
        forward_node = -forward_sums[0]
        forward_nodes.append(forward_node)
        forward_sums = forward_sums[1:]
        if forward_sums:
            forward_coupling = blocks_of(across(as_half(forward_node), lower_panels[height - 1]))
            forward_sums = [total + extra for total, extra in zip(forward_sums, forward_coupling)]
        adjoint_sums = [mine + theirs for mine, theirs in zip(adjoint_sums, exchange(adjoint_sums, pairs))]
        adjoint_node = plain_dot(as_half(-adjoint_sums[0]), inverse_panels[height - 1])
        adjoint_nodes.append(adjoint_node)
        adjoint_sums = adjoint_sums[1:]
        if adjoint_sums:
            adjoint_coupling = blocks_of(plain_dot(as_half(adjoint_node), upper_panels[height - 1]))
            adjoint_sums = [total + extra for total, extra in zip(adjoint_sums, adjoint_coupling)]

    forward_above, adjoint_above = [], []
    for height in range(levels, 0, -1):
        right_side = forward_nodes[height - 1]
        adjoint_value = adjoint_nodes[height - 1]
        if forward_above:
            right_side = right_side - across(
                as_half(jnp.concatenate(forward_above, axis=1)), upper_panels[height - 1]
            )
            adjoint_value = adjoint_value - plain_dot(
                as_half(jnp.concatenate(adjoint_above, axis=1)), lower_panels[height - 1]
            )
        forward_above.insert(0, across(as_half(right_side), inverse_panels[height - 1]))
        adjoint_above.insert(0, adjoint_value)
    forward_above = jnp.concatenate(forward_above, axis=1)
    adjoint_above = jnp.concatenate(adjoint_above, axis=1)

    forward_remain = y_leaf - across(as_half(masked(forward_above, base_mask)), anc_upper)
    forward_field = upper_solve(forward_remain, leaf_upper, leaf_inv, block_size, block_count)
    adjoint_remain = z_leaf - plain_dot(as_half(masked(adjoint_above, base_mask)), anc_lower)
    adjoint_field = lower_t_solve(adjoint_remain, leaf_lower, block_size, block_count)
    spread = lax.axis_size("src")
    product_field = (forward_field * adjoint_field).reshape(source_count, spread, cell_count // spread)
    partial_gradient = jnp.sum(product_field, axis=0)
    place = lax.axis_index("src")
    bit = spread // 2
    while bit:
        half = partial_gradient.shape[0] // 2
        upper = (place & bit) != 0
        outgoing = jnp.where(upper, partial_gradient[:half], partial_gradient[half:])
        kept = jnp.where(upper, partial_gradient[half:], partial_gradient[:half])
        pairs = [(index, index ^ bit) for index in range(spread)]
        partial_gradient = kept + lax.ppermute(outgoing, "src", pairs)
        bit //= 2
    gradient = partial_gradient.reshape(-1) * factor
    return (forward_field, adjoint_field, gradient)


def solution(mesh):
    in_specs = (
        P("src"),
        P("leaf"),
        P("src", "leaf"),
        P("leaf", None),
        P("leaf", None),
        P("leaf", None),
        P("leaf", None, None),
        P("leaf", None),
        P("leaf", None),
        P("leaf", None, None),
        P("leaf", None, None),
        P("leaf", None, None),
    )
    out_specs = (P("src", "leaf"), P("src", "leaf"), P(("leaf", "src")))
    return jax.shard_map(shards, mesh=mesh, in_specs=in_specs, out_specs=out_specs, check_vma=False)
```

```python
import math

import jax
import jax.numpy as jnp
from jax import lax
from jax.sharding import PartitionSpec as P


def across(former, latter):
    return lax.dot_general(
        former, latter, (((1,), (1,)), ((), ())), preferred_element_type=jnp.float32
    )


def plain_dot(former, latter):
    return jnp.dot(former, latter, preferred_element_type=jnp.float32)


def as_half(values):
    return values.astype(jnp.bfloat16)


def lower_solve(right_side, lower, block_size, block_count):
    solved = []
    for index in range(block_count):
        segment = right_side[:, index * block_size : (index + 1) * block_size]
        if index:
            earlier = as_half(jnp.concatenate(solved, axis=1))
            segment = segment - across(
                earlier, lower[index * block_size : (index + 1) * block_size, : index * block_size]
            )
        solved.append(segment)
    return jnp.concatenate(solved, axis=1)


def upper_solve(right_side, upper, inverse, block_size, block_count):
    behind = []
    for index in reversed(range(block_count)):
        segment = right_side[:, index * block_size : (index + 1) * block_size]
        if behind:
            segment = segment - across(
                as_half(jnp.concatenate(behind, axis=1)),
                upper[index * block_size : (index + 1) * block_size, (index + 1) * block_size :],
            )
        behind.insert(0, across(as_half(segment), inverse[index]))
    return jnp.concatenate(behind, axis=1)


def upper_t_solve(right_side, upper, inverse, block_size, block_count):
    solved = []
    for index in range(block_count):
        segment = right_side[:, index * block_size : (index + 1) * block_size]
        if index:
            earlier = as_half(jnp.concatenate(solved, axis=1))
            segment = segment - plain_dot(
                earlier, upper[: index * block_size, index * block_size : (index + 1) * block_size]
            )
        solved.append(plain_dot(as_half(segment), inverse[index]))
    return jnp.concatenate(solved, axis=1)


def lower_t_solve(right_side, lower, block_size, block_count):
    behind = []
    for index in reversed(range(block_count)):
        segment = right_side[:, index * block_size : (index + 1) * block_size]
        if behind:
            segment = segment - plain_dot(
                as_half(jnp.concatenate(behind, axis=1)),
                lower[(index + 1) * block_size :, index * block_size : (index + 1) * block_size],
            )
        behind.insert(0, segment)
    return jnp.concatenate(behind, axis=1)


def shards(
    src_cells,
    rec_cells,
    residual,
    pattern,
    leaf_lower,
    leaf_upper,
    leaf_inv,
    anc_lower,
    anc_upper,
    sep_inv,
    sep_lower,
    sep_upper,
):
    leaves = lax.axis_size("leaf")
    levels = leaves.bit_length() - 1
    device = lax.axis_index("leaf")
    block_size = leaf_inv.shape[1]
    block_count = leaf_inv.shape[0]
    cell_count = leaf_lower.shape[1]
    source_count = src_cells.shape[0]
    factor = 1.0 / math.sqrt(source_count * lax.axis_size("src"))
    def level_mask(height):
        level_row = jnp.logical_and(pattern[height] != 0, jnp.arange(1, levels + 1) > height)
        return jnp.repeat(level_row, block_size)

    def masked(values, keep):
        return jnp.where(keep, values, jnp.zeros_like(values))

    def blocks_of(values):
        return [values[:, k * block_size : (k + 1) * block_size] for k in range(values.shape[1] // block_size)]

    columns = lax.broadcasted_iota(jnp.int32, (source_count, cell_count), 1)
    forcing = (src_cells[:, None] - device * cell_count == columns).astype(jnp.float32)
    receiver_hits = (
        rec_cells[:, None] == lax.broadcasted_iota(jnp.int32, (rec_cells.shape[0], cell_count), 1)
    ).astype(jnp.float32)
    adjoint_rhs = jnp.dot(residual, receiver_hits, precision=lax.Precision.HIGHEST)

    base_mask = level_mask(0)
    y_leaf = lower_solve(forcing, leaf_lower, block_size, block_count)
    z_leaf = upper_t_solve(adjoint_rhs, leaf_upper, leaf_inv, block_size, block_count)
    forward_sums = blocks_of(masked(across(as_half(y_leaf), anc_lower), base_mask))
    adjoint_sums = blocks_of(masked(plain_dot(as_half(z_leaf), anc_upper), base_mask))

    lower_panels, upper_panels, inverse_panels = [], [], []
    for height in range(1, levels + 1):
        mask = level_mask(height)[height * block_size :]
        lower_panels.append(masked(sep_lower[height - 1, height * block_size :, :], mask[:, None]))
        upper_panels.append(masked(sep_upper[height - 1, :, height * block_size :], mask[None, :]))
        inverse_panels.append(sep_inv[height - 1])

    def exchange(values, pairs):
        pieces = [piece for piece in values]
        incoming = lax.ppermute(jnp.concatenate(pieces, axis=0), "leaf", pairs)
        received, row = [], 0
        for piece in pieces:
            received.append(incoming[row : row + piece.shape[0]])
            row += piece.shape[0]
        return received

    for height in range(1, levels + 1):
        stride = 1 << (height - 1)
        pairs = [(index, index ^ stride) for index in range(leaves)]
        pieces = []
        for upper_level in range(height, levels + 1):
            pieces.append(lower_panels[upper_level - 1])
            pieces.extend(blocks_of(upper_panels[upper_level - 1]))
            pieces.append(inverse_panels[upper_level - 1])
        received = exchange(pieces, pairs)
        for upper_level in range(height, levels + 1):
            place = device % (1 << upper_level)
            take = jnp.logical_and(place >= stride, place < 2 * stride)
            width = levels - upper_level
            lower_in = received[0]
            upper_in = jnp.concatenate(received[1 : 1 + width] or [upper_panels[upper_level - 1]], axis=1)
            inverse_in = received[1 + width]
            received = received[2 + width :]
            lower_panels[upper_level - 1] = jnp.where(take, lower_in, lower_panels[upper_level - 1])
            upper_panels[upper_level - 1] = jnp.where(take, upper_in, upper_panels[upper_level - 1])
            inverse_panels[upper_level - 1] = jnp.where(take, inverse_in, inverse_panels[upper_level - 1])

    forward_nodes, adjoint_nodes = [], []
    for height in range(1, levels + 1):
        stride = 1 << (height - 1)
        pairs = [(index, index ^ stride) for index in range(leaves)]
        forward_sums = [mine + theirs for mine, theirs in zip(forward_sums, exchange(forward_sums, pairs))]
        forward_node = -forward_sums[0]
        forward_nodes.append(forward_node)
        forward_sums = forward_sums[1:]
        if forward_sums:
            forward_coupling = blocks_of(across(as_half(forward_node), lower_panels[height - 1]))
            forward_sums = [total + extra for total, extra in zip(forward_sums, forward_coupling)]
        adjoint_sums = [mine + theirs for mine, theirs in zip(adjoint_sums, exchange(adjoint_sums, pairs))]
        adjoint_node = plain_dot(as_half(-adjoint_sums[0]), inverse_panels[height - 1])
        adjoint_nodes.append(adjoint_node)
        adjoint_sums = adjoint_sums[1:]
        if adjoint_sums:
            adjoint_coupling = blocks_of(plain_dot(as_half(adjoint_node), upper_panels[height - 1]))
            adjoint_sums = [total + extra for total, extra in zip(adjoint_sums, adjoint_coupling)]

    forward_above, adjoint_above = [], []
    for height in range(levels, 0, -1):
        right_side = forward_nodes[height - 1]
        adjoint_value = adjoint_nodes[height - 1]
        if forward_above:
            right_side = right_side - across(
                as_half(jnp.concatenate(forward_above, axis=1)), upper_panels[height - 1]
            )
            adjoint_value = adjoint_value - plain_dot(
                as_half(jnp.concatenate(adjoint_above, axis=1)), lower_panels[height - 1]
            )
        forward_above.insert(0, across(as_half(right_side), inverse_panels[height - 1]))
        adjoint_above.insert(0, adjoint_value)
    forward_above = jnp.concatenate(forward_above, axis=1)
    adjoint_above = jnp.concatenate(adjoint_above, axis=1)

    forward_remain = y_leaf - across(as_half(masked(forward_above, base_mask)), anc_upper)
    forward_field = upper_solve(forward_remain, leaf_upper, leaf_inv, block_size, block_count)
    adjoint_remain = z_leaf - plain_dot(as_half(masked(adjoint_above, base_mask)), anc_lower)
    adjoint_field = lower_t_solve(adjoint_remain, leaf_lower, block_size, block_count)
    spread = lax.axis_size("src")
    product_field = (forward_field * adjoint_field).reshape(source_count, spread, cell_count // spread)
    partial_gradient = jnp.sum(product_field, axis=0)
    place = lax.axis_index("src")
    bits = [1 << k for k in reversed(range(spread.bit_length() - 1))]
    if len(bits) > 2:
        bits[0], bits[1] = bits[1], bits[0]
    axes = [1 << k for k in reversed(range(spread.bit_length() - 1))]
    partial_gradient = partial_gradient.reshape([2] * len(axes) + [cell_count // spread])
    for bit in bits:
        axis = axes.index(bit)
        upper = (place & bit) != 0
        lower_half = lax.index_in_dim(partial_gradient, 0, axis, keepdims=False)
        upper_half = lax.index_in_dim(partial_gradient, 1, axis, keepdims=False)
        outgoing = jnp.where(upper, lower_half, upper_half)
        kept = jnp.where(upper, upper_half, lower_half)
        pairs = [(index, index ^ bit) for index in range(spread)]
        partial_gradient = kept + lax.ppermute(outgoing, "src", pairs)
        axes.remove(bit)
    gradient = partial_gradient.reshape(-1) * factor
    return (forward_field, adjoint_field, gradient)


def solution(mesh):
    in_specs = (
        P("src"),
        P("leaf"),
        P("src", "leaf"),
        P("leaf", None),
        P("leaf", None),
        P("leaf", None),
        P("leaf", None, None),
        P("leaf", None),
        P("leaf", None),
        P("leaf", None, None),
        P("leaf", None, None),
        P("leaf", None, None),
    )
    out_specs = (P("src", "leaf"), P("src", "leaf"), P(("leaf", "src")))
    return jax.shard_map(shards, mesh=mesh, in_specs=in_specs, out_specs=out_specs, check_vma=False)
```

```python
import math

import jax
import jax.numpy as jnp
from jax import lax
from jax.sharding import PartitionSpec as P


def across(former, latter):
    return lax.dot_general(
        former, latter, (((1,), (1,)), ((), ())), preferred_element_type=jnp.float32
    )


def plain_dot(former, latter):
    return jnp.dot(former, latter, preferred_element_type=jnp.float32)


def as_half(values):
    return values.astype(jnp.bfloat16)


def lower_solve(right_side, lower, block_size, block_count):
    solved = []
    for index in range(block_count):
        segment = right_side[:, index * block_size : (index + 1) * block_size]
        if index:
            earlier = as_half(jnp.concatenate(solved, axis=1))
            segment = segment - across(
                earlier, lower[index * block_size : (index + 1) * block_size, : index * block_size]
            )
        solved.append(segment)
    return jnp.concatenate(solved, axis=1)


def upper_solve(right_side, upper, inverse, block_size, block_count):
    behind = []
    for index in reversed(range(block_count)):
        segment = right_side[:, index * block_size : (index + 1) * block_size]
        if behind:
            segment = segment - across(
                as_half(jnp.concatenate(behind, axis=1)),
                upper[index * block_size : (index + 1) * block_size, (index + 1) * block_size :],
            )
        behind.insert(0, across(as_half(segment), inverse[index]))
    return jnp.concatenate(behind, axis=1)


def upper_t_solve(right_side, upper, inverse, block_size, block_count):
    solved = []
    for index in range(block_count):
        segment = right_side[:, index * block_size : (index + 1) * block_size]
        if index:
            earlier = as_half(jnp.concatenate(solved, axis=1))
            segment = segment - plain_dot(
                earlier, upper[: index * block_size, index * block_size : (index + 1) * block_size]
            )
        solved.append(plain_dot(as_half(segment), inverse[index]))
    return jnp.concatenate(solved, axis=1)


def lower_t_solve(right_side, lower, block_size, block_count):
    behind = []
    for index in reversed(range(block_count)):
        segment = right_side[:, index * block_size : (index + 1) * block_size]
        if behind:
            segment = segment - plain_dot(
                as_half(jnp.concatenate(behind, axis=1)),
                lower[(index + 1) * block_size :, index * block_size : (index + 1) * block_size],
            )
        behind.insert(0, segment)
    return jnp.concatenate(behind, axis=1)


def shards(
    src_cells,
    rec_cells,
    residual,
    pattern,
    leaf_lower,
    leaf_upper,
    leaf_inv,
    anc_lower,
    anc_upper,
    sep_inv,
    sep_lower,
    sep_upper,
):
    leaves = lax.axis_size("leaf")
    levels = leaves.bit_length() - 1
    device = lax.axis_index("leaf")
    block_size = leaf_inv.shape[1]
    block_count = leaf_inv.shape[0]
    cell_count = leaf_lower.shape[1]
    source_count = src_cells.shape[0]
    factor = 1.0 / math.sqrt(source_count * lax.axis_size("src"))
    def level_mask(height):
        level_row = jnp.logical_and(pattern[height] != 0, jnp.arange(1, levels + 1) > height)
        return jnp.repeat(level_row, block_size)

    def masked(values, keep):
        return jnp.where(keep, values, jnp.zeros_like(values))

    def blocks_of(values):
        return [values[:, k * block_size : (k + 1) * block_size] for k in range(values.shape[1] // block_size)]

    columns = lax.broadcasted_iota(jnp.int32, (source_count, cell_count), 1)
    forcing = (src_cells[:, None] - device * cell_count == columns).astype(jnp.float32)
    receiver_hits = (
        rec_cells[:, None] == lax.broadcasted_iota(jnp.int32, (rec_cells.shape[0], cell_count), 1)
    ).astype(jnp.bfloat16)
    leading = residual.astype(jnp.bfloat16)
    rest = residual - leading.astype(jnp.float32)
    middle = rest.astype(jnp.bfloat16)
    trailing = (rest - middle.astype(jnp.float32)).astype(jnp.bfloat16)
    adjoint_rhs = (
        plain_dot(leading, receiver_hits) + plain_dot(middle, receiver_hits)
    ) + plain_dot(trailing, receiver_hits)

    base_mask = level_mask(0)
    y_leaf = lower_solve(forcing, leaf_lower, block_size, block_count)
    z_leaf = upper_t_solve(adjoint_rhs, leaf_upper, leaf_inv, block_size, block_count)
    forward_sums = blocks_of(masked(across(as_half(y_leaf), anc_lower), base_mask))
    adjoint_sums = blocks_of(masked(plain_dot(as_half(z_leaf), anc_upper), base_mask))

    lower_panels, upper_panels, inverse_panels = [], [], []
    for height in range(1, levels + 1):
        mask = level_mask(height)[height * block_size :]
        lower_panels.append(masked(sep_lower[height - 1, height * block_size :, :], mask[:, None]))
        upper_panels.append(masked(sep_upper[height - 1, :, height * block_size :], mask[None, :]))
        inverse_panels.append(sep_inv[height - 1])

    def exchange(values, pairs):
        pieces = [piece for piece in values]
        incoming = lax.ppermute(jnp.concatenate(pieces, axis=0), "leaf", pairs)
        received, row = [], 0
        for piece in pieces:
            received.append(incoming[row : row + piece.shape[0]])
            row += piece.shape[0]
        return received

    for height in range(1, levels + 1):
        stride = 1 << (height - 1)
        pairs = [(index, index ^ stride) for index in range(leaves)]
        pieces = []
        for upper_level in range(height, levels + 1):
            pieces.append(lower_panels[upper_level - 1])
            pieces.extend(blocks_of(upper_panels[upper_level - 1]))
            pieces.append(inverse_panels[upper_level - 1])
        received = exchange(pieces, pairs)
        for upper_level in range(height, levels + 1):
            place = device % (1 << upper_level)
            take = jnp.logical_and(place >= stride, place < 2 * stride)
            width = levels - upper_level
            lower_in = received[0]
            upper_in = jnp.concatenate(received[1 : 1 + width] or [upper_panels[upper_level - 1]], axis=1)
            inverse_in = received[1 + width]
            received = received[2 + width :]
            lower_panels[upper_level - 1] = jnp.where(take, lower_in, lower_panels[upper_level - 1])
            upper_panels[upper_level - 1] = jnp.where(take, upper_in, upper_panels[upper_level - 1])
            inverse_panels[upper_level - 1] = jnp.where(take, inverse_in, inverse_panels[upper_level - 1])

    forward_nodes, adjoint_nodes = [], []
    for height in range(1, levels + 1):
        stride = 1 << (height - 1)
        pairs = [(index, index ^ stride) for index in range(leaves)]
        forward_sums = [mine + theirs for mine, theirs in zip(forward_sums, exchange(forward_sums, pairs))]
        forward_node = -forward_sums[0]
        forward_nodes.append(forward_node)
        forward_sums = forward_sums[1:]
        if forward_sums:
            forward_coupling = blocks_of(across(as_half(forward_node), lower_panels[height - 1]))
            forward_sums = [total + extra for total, extra in zip(forward_sums, forward_coupling)]
        adjoint_sums = [mine + theirs for mine, theirs in zip(adjoint_sums, exchange(adjoint_sums, pairs))]
        adjoint_node = plain_dot(as_half(-adjoint_sums[0]), inverse_panels[height - 1])
        adjoint_nodes.append(adjoint_node)
        adjoint_sums = adjoint_sums[1:]
        if adjoint_sums:
            adjoint_coupling = blocks_of(plain_dot(as_half(adjoint_node), upper_panels[height - 1]))
            adjoint_sums = [total + extra for total, extra in zip(adjoint_sums, adjoint_coupling)]

    forward_above, adjoint_above = [], []
    for height in range(levels, 0, -1):
        right_side = forward_nodes[height - 1]
        adjoint_value = adjoint_nodes[height - 1]
        if forward_above:
            right_side = right_side - across(
                as_half(jnp.concatenate(forward_above, axis=1)), upper_panels[height - 1]
            )
            adjoint_value = adjoint_value - plain_dot(
                as_half(jnp.concatenate(adjoint_above, axis=1)), lower_panels[height - 1]
            )
        forward_above.insert(0, across(as_half(right_side), inverse_panels[height - 1]))
        adjoint_above.insert(0, adjoint_value)
    forward_above = jnp.concatenate(forward_above, axis=1)
    adjoint_above = jnp.concatenate(adjoint_above, axis=1)

    forward_remain = y_leaf - across(as_half(masked(forward_above, base_mask)), anc_upper)
    forward_field = upper_solve(forward_remain, leaf_upper, leaf_inv, block_size, block_count)
    adjoint_remain = z_leaf - plain_dot(as_half(masked(adjoint_above, base_mask)), anc_lower)
    adjoint_field = lower_t_solve(adjoint_remain, leaf_lower, block_size, block_count)
    spread = lax.axis_size("src")
    product_field = (forward_field * adjoint_field).reshape(source_count, spread, cell_count // spread)
    partial_gradient = jnp.sum(product_field, axis=0)
    place = lax.axis_index("src")
    bit = spread // 2
    while bit:
        half = partial_gradient.shape[0] // 2
        upper = (place & bit) != 0
        outgoing = jnp.where(upper, partial_gradient[:half], partial_gradient[half:])
        kept = jnp.where(upper, partial_gradient[half:], partial_gradient[:half])
        pairs = [(index, index ^ bit) for index in range(spread)]
        partial_gradient = kept + lax.ppermute(outgoing, "src", pairs)
        bit //= 2
    gradient = partial_gradient.reshape(-1) * factor
    return (forward_field, adjoint_field, gradient)


def solution(mesh):
    in_specs = (
        P("src"),
        P("leaf"),
        P("src", "leaf"),
        P("leaf", None),
        P("leaf", None),
        P("leaf", None),
        P("leaf", None, None),
        P("leaf", None),
        P("leaf", None),
        P("leaf", None, None),
        P("leaf", None, None),
        P("leaf", None, None),
    )
    out_specs = (P("src", "leaf"), P("src", "leaf"), P(("leaf", "src")))
    return jax.shard_map(shards, mesh=mesh, in_specs=in_specs, out_specs=out_specs, check_vma=False)
```

```python
import math

import jax
import jax.numpy as jnp
from jax import lax
from jax.sharding import PartitionSpec as P


def across(former, latter):
    return lax.dot_general(
        former, latter, (((1,), (1,)), ((), ())), preferred_element_type=jnp.float32
    )


def plain_dot(former, latter):
    return jnp.dot(former, latter, preferred_element_type=jnp.float32)


def as_half(values):
    return values.astype(jnp.bfloat16)


def lower_solve(right_side, lower, block_size, block_count):
    solved = []
    for index in range(block_count):
        segment = right_side[:, index * block_size : (index + 1) * block_size]
        if index:
            earlier = as_half(jnp.concatenate(solved, axis=1))
            segment = segment - across(
                earlier, lower[index * block_size : (index + 1) * block_size, : index * block_size]
            )
        solved.append(segment)
    return jnp.concatenate(solved, axis=1)


def upper_solve(right_side, upper, inverse, block_size, block_count):
    behind = []
    for index in reversed(range(block_count)):
        segment = right_side[:, index * block_size : (index + 1) * block_size]
        if behind:
            segment = segment - across(
                as_half(jnp.concatenate(behind, axis=1)),
                upper[index * block_size : (index + 1) * block_size, (index + 1) * block_size :],
            )
        behind.insert(0, across(as_half(segment), inverse[index]))
    return jnp.concatenate(behind, axis=1)


def upper_t_solve(right_side, upper, inverse, block_size, block_count):
    solved = []
    for index in range(block_count):
        segment = right_side[:, index * block_size : (index + 1) * block_size]
        if index:
            earlier = as_half(jnp.concatenate(solved, axis=1))
            segment = segment - plain_dot(
                earlier, upper[: index * block_size, index * block_size : (index + 1) * block_size]
            )
        solved.append(plain_dot(as_half(segment), inverse[index]))
    return jnp.concatenate(solved, axis=1)


def lower_t_solve(right_side, lower, block_size, block_count):
    behind = []
    for index in reversed(range(block_count)):
        segment = right_side[:, index * block_size : (index + 1) * block_size]
        if behind:
            segment = segment - plain_dot(
                as_half(jnp.concatenate(behind, axis=1)),
                lower[(index + 1) * block_size :, index * block_size : (index + 1) * block_size],
            )
        behind.insert(0, segment)
    return jnp.concatenate(behind, axis=1)


def shards(
    src_cells,
    rec_cells,
    residual,
    pattern,
    leaf_lower,
    leaf_upper,
    leaf_inv,
    anc_lower,
    anc_upper,
    sep_inv,
    sep_lower,
    sep_upper,
):
    leaves = lax.axis_size("leaf")
    levels = leaves.bit_length() - 1
    device = lax.axis_index("leaf")
    block_size = leaf_inv.shape[1]
    block_count = leaf_inv.shape[0]
    cell_count = leaf_lower.shape[1]
    source_count = src_cells.shape[0]
    factor = 1.0 / math.sqrt(source_count * lax.axis_size("src"))
    def level_mask(height):
        level_row = jnp.logical_and(pattern[height] != 0, jnp.arange(1, levels + 1) > height)
        return jnp.repeat(level_row, block_size)

    def masked(values, keep):
        return jnp.where(keep, values, jnp.zeros_like(values))

    def blocks_of(values):
        return [values[:, k * block_size : (k + 1) * block_size] for k in range(values.shape[1] // block_size)]

    columns = lax.broadcasted_iota(jnp.int32, (source_count, cell_count), 1)
    forcing = (src_cells[:, None] - device * cell_count == columns).astype(jnp.float32)
    receiver_hits = (
        rec_cells[:, None] == lax.broadcasted_iota(jnp.int32, (rec_cells.shape[0], cell_count), 1)
    ).astype(jnp.float32)
    adjoint_rhs = jnp.dot(residual, receiver_hits, precision=lax.Precision.HIGHEST)

    base_mask = level_mask(0)
    y_leaf = lower_solve(forcing, leaf_lower, block_size, block_count)
    z_leaf = upper_t_solve(adjoint_rhs, leaf_upper, leaf_inv, block_size, block_count)
    forward_sums = blocks_of(masked(across(as_half(y_leaf), anc_lower), base_mask))
    adjoint_sums = blocks_of(masked(plain_dot(as_half(z_leaf), anc_upper), base_mask))

    lower_panels, upper_panels, inverse_panels = [], [], []
    for height in range(1, levels + 1):
        mask = level_mask(height)[height * block_size :]
        lower_panels.append(masked(sep_lower[height - 1, height * block_size :, :], mask[:, None]))
        upper_panels.append(masked(sep_upper[height - 1, :, height * block_size :], mask[None, :]))
        inverse_panels.append(sep_inv[height - 1])

    def exchange(values, pairs):
        pieces = [piece for piece in values]
        incoming = lax.ppermute(jnp.concatenate(pieces, axis=0), "leaf", pairs)
        received, row = [], 0
        for piece in pieces:
            received.append(incoming[row : row + piece.shape[0]])
            row += piece.shape[0]
        return received

    for height in range(1, levels + 1):
        stride = 1 << (height - 1)
        pairs = [(index, index ^ stride) for index in range(leaves)]
        pieces = []
        for upper_level in range(height, levels + 1):
            pieces.append(lower_panels[upper_level - 1])
            pieces.extend(blocks_of(upper_panels[upper_level - 1]))
            pieces.append(inverse_panels[upper_level - 1])
        received = exchange(pieces, pairs)
        for upper_level in range(height, levels + 1):
            place = device % (1 << upper_level)
            take = jnp.logical_and(place >= stride, place < 2 * stride)
            width = levels - upper_level
            lower_in = received[0]
            upper_in = jnp.concatenate(received[1 : 1 + width] or [upper_panels[upper_level - 1]], axis=1)
            inverse_in = received[1 + width]
            received = received[2 + width :]
            lower_panels[upper_level - 1] = jnp.where(take, lower_in, lower_panels[upper_level - 1])
            upper_panels[upper_level - 1] = jnp.where(take, upper_in, upper_panels[upper_level - 1])
            inverse_panels[upper_level - 1] = jnp.where(take, inverse_in, inverse_panels[upper_level - 1])

    forward_nodes, adjoint_nodes = [], []
    for height in range(1, levels + 1):
        stride = 1 << (height - 1)
        pairs = [(index, index ^ stride) for index in range(leaves)]
        forward_sums = [mine + theirs for mine, theirs in zip(forward_sums, exchange(forward_sums, pairs))]
        forward_node = -forward_sums[0]
        forward_nodes.append(forward_node)
        forward_sums = forward_sums[1:]
        if forward_sums:
            forward_coupling = blocks_of(across(as_half(forward_node), lower_panels[height - 1]))
            forward_sums = [total + extra for total, extra in zip(forward_sums, forward_coupling)]
        adjoint_sums = [mine + theirs for mine, theirs in zip(adjoint_sums, exchange(adjoint_sums, pairs))]
        adjoint_node = plain_dot(as_half(-adjoint_sums[0]), inverse_panels[height - 1])
        adjoint_nodes.append(adjoint_node)
        adjoint_sums = adjoint_sums[1:]
        if adjoint_sums:
            adjoint_coupling = blocks_of(plain_dot(as_half(adjoint_node), upper_panels[height - 1]))
            adjoint_sums = [total + extra for total, extra in zip(adjoint_sums, adjoint_coupling)]

    forward_above, adjoint_above = [], []
    for height in range(levels, 0, -1):
        right_side = forward_nodes[height - 1]
        adjoint_value = adjoint_nodes[height - 1]
        if forward_above:
            right_side = right_side - across(
                as_half(jnp.concatenate(forward_above, axis=1)), upper_panels[height - 1]
            )
            adjoint_value = adjoint_value - plain_dot(
                as_half(jnp.concatenate(adjoint_above, axis=1)), lower_panels[height - 1]
            )
        forward_above.insert(0, across(as_half(right_side), inverse_panels[height - 1]))
        adjoint_above.insert(0, adjoint_value)
    forward_above = jnp.concatenate(forward_above, axis=1)
    adjoint_above = jnp.concatenate(adjoint_above, axis=1)

    forward_remain = y_leaf - across(as_half(masked(forward_above, base_mask)), anc_upper)
    forward_field = upper_solve(forward_remain, leaf_upper, leaf_inv, block_size, block_count)
    adjoint_remain = z_leaf - plain_dot(as_half(masked(adjoint_above, base_mask)), anc_lower)
    adjoint_field = lower_t_solve(adjoint_remain, leaf_lower, block_size, block_count)
    spread = lax.axis_size("src")
    product_field = (forward_field * adjoint_field).reshape(source_count, spread, cell_count // spread)
    partial_gradient = jnp.sum(product_field, axis=0) * factor
    place = lax.axis_index("src")
    bit = spread // 2
    while bit:
        half = partial_gradient.shape[0] // 2
        upper = (place & bit) != 0
        outgoing = jnp.where(upper, partial_gradient[:half], partial_gradient[half:])
        kept = jnp.where(upper, partial_gradient[half:], partial_gradient[:half])
        pairs = [(index, index ^ bit) for index in range(spread)]
        partial_gradient = kept + lax.ppermute(outgoing, "src", pairs)
        bit //= 2
    gradient = partial_gradient.reshape(-1)
    return (forward_field, adjoint_field, gradient)


def solution(mesh):
    in_specs = (
        P("src"),
        P("leaf"),
        P("src", "leaf"),
        P("leaf", None),
        P("leaf", None),
        P("leaf", None),
        P("leaf", None, None),
        P("leaf", None),
        P("leaf", None),
        P("leaf", None, None),
        P("leaf", None, None),
        P("leaf", None, None),
    )
    out_specs = (P("src", "leaf"), P("src", "leaf"), P(("leaf", "src")))
    return jax.shard_map(shards, mesh=mesh, in_specs=in_specs, out_specs=out_specs, check_vma=False)
```

```python
import math

import jax
import jax.numpy as jnp
from jax import lax
from jax.sharding import PartitionSpec as P


def across(former, latter):
    return lax.dot_general(
        former, latter, (((1,), (1,)), ((), ())), preferred_element_type=jnp.float32
    )


def plain_dot(former, latter):
    return jnp.dot(former, latter, preferred_element_type=jnp.float32)


def as_half(values):
    return values.astype(jnp.bfloat16)


def lower_solve(right_side, lower, block_size, block_count):
    solved = []
    for index in range(block_count):
        segment = right_side[:, index * block_size : (index + 1) * block_size]
        if index:
            earlier = as_half(jnp.concatenate(solved, axis=1))
            segment = segment - across(
                earlier, lower[index * block_size : (index + 1) * block_size, : index * block_size]
            )
        solved.append(segment)
    return jnp.concatenate(solved, axis=1)


def upper_solve(right_side, upper, inverse, block_size, block_count):
    behind = []
    for index in reversed(range(block_count)):
        segment = right_side[:, index * block_size : (index + 1) * block_size]
        if behind:
            segment = segment - across(
                as_half(jnp.concatenate(behind, axis=1)),
                upper[index * block_size : (index + 1) * block_size, (index + 1) * block_size :],
            )
        behind.insert(0, across(as_half(segment), inverse[index]))
    return jnp.concatenate(behind, axis=1)


def upper_t_solve(right_side, upper, inverse, block_size, block_count):
    solved = []
    for index in range(block_count):
        segment = right_side[:, index * block_size : (index + 1) * block_size]
        if index:
            earlier = as_half(jnp.concatenate(solved, axis=1))
            segment = segment - plain_dot(
                earlier, upper[: index * block_size, index * block_size : (index + 1) * block_size]
            )
        solved.append(plain_dot(as_half(segment), inverse[index]))
    return jnp.concatenate(solved, axis=1)


def lower_t_solve(right_side, lower, block_size, block_count):
    behind = []
    for index in reversed(range(block_count)):
        segment = right_side[:, index * block_size : (index + 1) * block_size]
        if behind:
            segment = segment - plain_dot(
                as_half(jnp.concatenate(behind, axis=1)),
                lower[(index + 1) * block_size :, index * block_size : (index + 1) * block_size],
            )
        behind.insert(0, segment)
    return jnp.concatenate(behind, axis=1)


def shards(
    src_cells,
    rec_cells,
    residual,
    pattern,
    leaf_lower,
    leaf_upper,
    leaf_inv,
    anc_lower,
    anc_upper,
    sep_inv,
    sep_lower,
    sep_upper,
):
    leaves = lax.axis_size("leaf")
    levels = leaves.bit_length() - 1
    device = lax.axis_index("leaf")
    block_size = leaf_inv.shape[1]
    block_count = leaf_inv.shape[0]
    cell_count = leaf_lower.shape[1]
    source_count = src_cells.shape[0]
    factor = 1.0 / math.sqrt(source_count * lax.axis_size("src"))
    def level_mask(height):
        level_row = jnp.logical_and(pattern[height] != 0, jnp.arange(1, levels + 1) > height)
        return jnp.repeat(level_row, block_size)

    def masked(values, keep):
        return jnp.where(keep, values, jnp.zeros_like(values))

    def blocks_of(values):
        return [values[:, k * block_size : (k + 1) * block_size] for k in range(values.shape[1] // block_size)]

    columns = lax.broadcasted_iota(jnp.int32, (source_count, cell_count), 1)
    forcing = (src_cells[:, None] - device * cell_count == columns).astype(jnp.float32)
    receiver_hits = (
        rec_cells[:, None] == lax.broadcasted_iota(jnp.int32, (rec_cells.shape[0], cell_count), 1)
    ).astype(jnp.float32)
    adjoint_rhs = jnp.dot(residual, receiver_hits, precision=lax.Precision.HIGHEST)

    base_mask = level_mask(0)
    y_leaf = lower_solve(forcing, leaf_lower, block_size, block_count)
    z_leaf = upper_t_solve(adjoint_rhs, leaf_upper, leaf_inv, block_size, block_count)
    forward_sums = blocks_of(masked(across(as_half(y_leaf), anc_lower), base_mask))
    adjoint_sums = blocks_of(masked(plain_dot(as_half(z_leaf), anc_upper), base_mask))

    lower_panels, upper_panels, inverse_panels = [], [], []
    for height in range(1, levels + 1):
        mask = level_mask(height)[height * block_size :]
        lower_panels.append(masked(sep_lower[height - 1, height * block_size :, :], mask[:, None]))
        upper_panels.append(masked(sep_upper[height - 1, :, height * block_size :], mask[None, :]))
        inverse_panels.append(sep_inv[height - 1])

    def exchange(values, pairs):
        pieces = [piece for piece in values]
        incoming = lax.ppermute(jnp.concatenate(pieces, axis=0), "leaf", pairs)
        received, row = [], 0
        for piece in pieces:
            received.append(incoming[row : row + piece.shape[0]])
            row += piece.shape[0]
        return received

    for height in range(1, levels + 1):
        stride = 1 << (height - 1)
        pairs = [(index, index ^ stride) for index in range(leaves)]
        pieces = []
        for upper_level in range(height, levels + 1):
            pieces.append(lower_panels[upper_level - 1])
            pieces.extend(blocks_of(upper_panels[upper_level - 1]))
            pieces.append(inverse_panels[upper_level - 1])
        received = exchange(pieces, pairs)
        for upper_level in range(height, levels + 1):
            place = device % (1 << upper_level)
            take = jnp.logical_and(place >= stride, place < 2 * stride)
            width = levels - upper_level
            lower_in = received[0]
            upper_in = jnp.concatenate(received[1 : 1 + width] or [upper_panels[upper_level - 1]], axis=1)
            inverse_in = received[1 + width]
            received = received[2 + width :]
            lower_panels[upper_level - 1] = jnp.where(take, lower_in, lower_panels[upper_level - 1])
            upper_panels[upper_level - 1] = jnp.where(take, upper_in, upper_panels[upper_level - 1])
            inverse_panels[upper_level - 1] = jnp.where(take, inverse_in, inverse_panels[upper_level - 1])

    forward_nodes, adjoint_nodes = [], []
    for height in range(1, levels + 1):
        stride = 1 << (height - 1)
        pairs = [(index, index ^ stride) for index in range(leaves)]
        forward_sums = [mine + theirs for mine, theirs in zip(forward_sums, exchange(forward_sums, pairs))]
        forward_node = -forward_sums[0]
        forward_nodes.append(forward_node)
        forward_sums = forward_sums[1:]
        if forward_sums:
            forward_coupling = blocks_of(across(as_half(forward_node), lower_panels[height - 1]))
            forward_sums = [total + extra for total, extra in zip(forward_sums, forward_coupling)]
        adjoint_sums = [mine + theirs for mine, theirs in zip(adjoint_sums, exchange(adjoint_sums, pairs))]
        adjoint_node = plain_dot(as_half(-adjoint_sums[0]), inverse_panels[height - 1])
        adjoint_nodes.append(adjoint_node)
        adjoint_sums = adjoint_sums[1:]
        if adjoint_sums:
            adjoint_coupling = blocks_of(plain_dot(as_half(adjoint_node), upper_panels[height - 1]))
            adjoint_sums = [total + extra for total, extra in zip(adjoint_sums, adjoint_coupling)]

    forward_above, adjoint_above = [], []
    for height in range(levels, 0, -1):
        right_side = forward_nodes[height - 1]
        adjoint_value = adjoint_nodes[height - 1]
        if forward_above:
            right_side = right_side - across(
                as_half(jnp.concatenate(forward_above, axis=1)), upper_panels[height - 1]
            )
            adjoint_value = adjoint_value - plain_dot(
                as_half(jnp.concatenate(adjoint_above, axis=1)), lower_panels[height - 1]
            )
        forward_above.insert(0, across(as_half(right_side), inverse_panels[height - 1]))
        adjoint_above.insert(0, adjoint_value)
    forward_above = jnp.concatenate(forward_above, axis=1)
    adjoint_above = jnp.concatenate(adjoint_above, axis=1)

    forward_remain = y_leaf - across(as_half(masked(forward_above, base_mask)), anc_upper)
    forward_field = upper_solve(forward_remain, leaf_upper, leaf_inv, block_size, block_count)
    adjoint_remain = z_leaf - plain_dot(as_half(masked(adjoint_above, base_mask)), anc_lower)
    adjoint_field = lower_t_solve(adjoint_remain, leaf_lower, block_size, block_count)
    spread = lax.axis_size("src")
    product_field = (forward_field * adjoint_field).reshape(source_count, spread, cell_count // spread)
    partial_gradient = jnp.sum(product_field, axis=0)
    place = lax.axis_index("src")
    bits = [1 << k for k in range(spread.bit_length() - 1)]
    axes = [1 << k for k in reversed(range(spread.bit_length() - 1))]
    partial_gradient = partial_gradient.reshape([2] * len(axes) + [cell_count // spread])
    for bit in bits:
        axis = axes.index(bit)
        upper = (place & bit) != 0
        lower_half = lax.index_in_dim(partial_gradient, 0, axis, keepdims=False)
        upper_half = lax.index_in_dim(partial_gradient, 1, axis, keepdims=False)
        outgoing = jnp.where(upper, lower_half, upper_half)
        kept = jnp.where(upper, upper_half, lower_half)
        pairs = [(index, index ^ bit) for index in range(spread)]
        partial_gradient = kept + lax.ppermute(outgoing, "src", pairs)
        axes.remove(bit)
    gradient = partial_gradient.reshape(-1) * factor
    return (forward_field, adjoint_field, gradient)


def solution(mesh):
    in_specs = (
        P("src"),
        P("leaf"),
        P("src", "leaf"),
        P("leaf", None),
        P("leaf", None),
        P("leaf", None),
        P("leaf", None, None),
        P("leaf", None),
        P("leaf", None),
        P("leaf", None, None),
        P("leaf", None, None),
        P("leaf", None, None),
    )
    out_specs = (P("src", "leaf"), P("src", "leaf"), P(("leaf", "src")))
    return jax.shard_map(shards, mesh=mesh, in_specs=in_specs, out_specs=out_specs, check_vma=False)
```

```python
import math

import jax
import jax.numpy as jnp
from jax import lax
from jax.sharding import PartitionSpec as P


def across(former, latter):
    return lax.dot_general(
        former, latter, (((1,), (1,)), ((), ())), preferred_element_type=jnp.float32
    )


def plain_dot(former, latter):
    return jnp.dot(former, latter, preferred_element_type=jnp.float32)


def as_half(values):
    return values.astype(jnp.bfloat16)


def lower_solve(right_side, lower, block_size, block_count):
    solved = []
    for index in range(block_count):
        segment = right_side[:, index * block_size : (index + 1) * block_size]
        if index:
            earlier = as_half(jnp.concatenate(solved, axis=1))
            segment = segment - across(
                earlier, lower[index * block_size : (index + 1) * block_size, : index * block_size]
            )
        solved.append(segment)
    return jnp.concatenate(solved, axis=1)


def upper_solve(right_side, upper, inverse, block_size, block_count):
    behind = []
    for index in reversed(range(block_count)):
        segment = right_side[:, index * block_size : (index + 1) * block_size]
        if behind:
            segment = segment - across(
                as_half(jnp.concatenate(behind, axis=1)),
                upper[index * block_size : (index + 1) * block_size, (index + 1) * block_size :],
            )
        behind.insert(0, across(as_half(segment), inverse[index]))
    return jnp.concatenate(behind, axis=1)


def upper_t_solve(right_side, upper, inverse, block_size, block_count):
    solved = []
    for index in range(block_count):
        segment = right_side[:, index * block_size : (index + 1) * block_size]
        if index:
            earlier = as_half(jnp.concatenate(solved, axis=1))
            segment = segment - plain_dot(
                earlier, upper[: index * block_size, index * block_size : (index + 1) * block_size]
            )
        solved.append(plain_dot(as_half(segment), inverse[index]))
    return jnp.concatenate(solved, axis=1)


def lower_t_solve(right_side, lower, block_size, block_count):
    behind = []
    for index in reversed(range(block_count)):
        segment = right_side[:, index * block_size : (index + 1) * block_size]
        if behind:
            segment = segment - plain_dot(
                as_half(jnp.concatenate(behind, axis=1)),
                lower[(index + 1) * block_size :, index * block_size : (index + 1) * block_size],
            )
        behind.insert(0, segment)
    return jnp.concatenate(behind, axis=1)


def shards(
    src_cells,
    rec_cells,
    residual,
    pattern,
    leaf_lower,
    leaf_upper,
    leaf_inv,
    anc_lower,
    anc_upper,
    sep_inv,
    sep_lower,
    sep_upper,
):
    leaves = lax.axis_size("leaf")
    levels = leaves.bit_length() - 1
    device = lax.axis_index("leaf")
    block_size = leaf_inv.shape[1]
    block_count = leaf_inv.shape[0]
    cell_count = leaf_lower.shape[1]
    source_count = src_cells.shape[0]
    factor = 1.0 / math.sqrt(source_count * lax.axis_size("src"))
    def level_mask(height):
        level_row = jnp.logical_and(pattern[height] != 0, jnp.arange(1, levels + 1) > height)
        return jnp.repeat(level_row, block_size)

    def masked(values, keep):
        return jnp.where(keep, values, jnp.zeros_like(values))

    def blocks_of(values):
        return [values[:, k * block_size : (k + 1) * block_size] for k in range(values.shape[1] // block_size)]

    columns = lax.broadcasted_iota(jnp.int32, (source_count, cell_count), 1)
    forcing = (src_cells[:, None] - device * cell_count == columns).astype(jnp.float32)
    receiver_hits = (
        rec_cells[:, None] == lax.broadcasted_iota(jnp.int32, (rec_cells.shape[0], cell_count), 1)
    ).astype(jnp.float32)
    adjoint_rhs = jnp.dot(residual, receiver_hits, precision=lax.Precision.HIGHEST)

    base_mask = level_mask(0)
    y_leaf = lower_solve(forcing, leaf_lower, block_size, block_count)
    z_leaf = upper_t_solve(adjoint_rhs, leaf_upper, leaf_inv, block_size, block_count)
    forward_sums = blocks_of(masked(across(as_half(y_leaf), anc_lower), base_mask))
    adjoint_sums = blocks_of(masked(plain_dot(as_half(z_leaf), anc_upper), base_mask))

    lower_panels, upper_panels, inverse_panels = [], [], []
    for height in range(1, levels + 1):
        mask = level_mask(height)[height * block_size :]
        lower_panels.append(masked(sep_lower[height - 1, height * block_size :, :], mask[:, None]))
        upper_panels.append(masked(sep_upper[height - 1, :, height * block_size :], mask[None, :]))
        inverse_panels.append(sep_inv[height - 1])

    def exchange(values, pairs):
        pieces = [piece for piece in values]
        incoming = lax.ppermute(jnp.concatenate(pieces, axis=0), "leaf", pairs)
        received, row = [], 0
        for piece in pieces:
            received.append(incoming[row : row + piece.shape[0]])
            row += piece.shape[0]
        return received

    for height in range(1, levels + 1):
        stride = 1 << (height - 1)
        pairs = [(index, index ^ stride) for index in range(leaves)]
        pieces = []
        for upper_level in range(height, levels + 1):
            pieces.append(lower_panels[upper_level - 1])
            pieces.extend(blocks_of(upper_panels[upper_level - 1]))
            pieces.append(inverse_panels[upper_level - 1])
        received = exchange(pieces, pairs)
        for upper_level in range(height, levels + 1):
            place = device % (1 << upper_level)
            take = jnp.logical_and(place >= stride, place < 2 * stride)
            width = levels - upper_level
            lower_in = received[0]
            upper_in = jnp.concatenate(received[1 : 1 + width] or [upper_panels[upper_level - 1]], axis=1)
            inverse_in = received[1 + width]
            received = received[2 + width :]
            lower_panels[upper_level - 1] = jnp.where(take, lower_in, lower_panels[upper_level - 1])
            upper_panels[upper_level - 1] = jnp.where(take, upper_in, upper_panels[upper_level - 1])
            inverse_panels[upper_level - 1] = jnp.where(take, inverse_in, inverse_panels[upper_level - 1])

    forward_nodes, adjoint_nodes = [], []
    for height in range(1, levels + 1):
        stride = 1 << (height - 1)
        pairs = [(index, index ^ stride) for index in range(leaves)]
        forward_sums = [mine + theirs for mine, theirs in zip(forward_sums, exchange(forward_sums, pairs))]
        forward_node = -forward_sums[0]
        forward_nodes.append(forward_node)
        forward_sums = forward_sums[1:]
        if forward_sums:
            forward_coupling = blocks_of(across(as_half(forward_node), lower_panels[height - 1]))
            forward_sums = [total + extra for total, extra in zip(forward_sums, forward_coupling)]
        adjoint_sums = [mine + theirs for mine, theirs in zip(adjoint_sums, exchange(adjoint_sums, pairs))]
        adjoint_node = plain_dot(as_half(-adjoint_sums[0]), inverse_panels[height - 1])
        adjoint_nodes.append(adjoint_node)
        adjoint_sums = adjoint_sums[1:]
        if adjoint_sums:
            adjoint_coupling = blocks_of(plain_dot(as_half(adjoint_node), upper_panels[height - 1]))
            adjoint_sums = [total + extra for total, extra in zip(adjoint_sums, adjoint_coupling)]

    forward_above, adjoint_above = [], []
    for height in range(levels, 0, -1):
        right_side = forward_nodes[height - 1]
        adjoint_value = adjoint_nodes[height - 1]
        if forward_above:
            right_side = right_side - across(
                as_half(jnp.concatenate(forward_above, axis=1)), upper_panels[height - 1]
            )
            adjoint_value = adjoint_value - plain_dot(
                as_half(jnp.concatenate(adjoint_above, axis=1)), lower_panels[height - 1]
            )
        forward_above.insert(0, across(as_half(right_side), inverse_panels[height - 1]))
        adjoint_above.insert(0, adjoint_value)
    forward_above = jnp.concatenate(forward_above, axis=1)
    adjoint_above = jnp.concatenate(adjoint_above, axis=1)

    forward_remain = y_leaf - across(as_half(masked(forward_above, base_mask)), anc_upper)
    forward_field = upper_solve(forward_remain, leaf_upper, leaf_inv, block_size, block_count)
    adjoint_remain = z_leaf - plain_dot(as_half(masked(adjoint_above, base_mask)), anc_lower)
    adjoint_field = lower_t_solve(adjoint_remain, leaf_lower, block_size, block_count)
    spread = lax.axis_size("src")
    product_field = (forward_field * adjoint_field).reshape(source_count, spread, cell_count // spread)
    partial_gradient = jnp.sum(product_field, axis=0)
    place = lax.axis_index("src")
    bits = [1 << k for k in range(spread.bit_length() - 1)]
    bits = bits[:1] + bits[1:][::-1]
    axes = [1 << k for k in reversed(range(spread.bit_length() - 1))]
    partial_gradient = partial_gradient.reshape([2] * len(axes) + [cell_count // spread])
    for bit in bits:
        axis = axes.index(bit)
        upper = (place & bit) != 0
        lower_half = lax.index_in_dim(partial_gradient, 0, axis, keepdims=False)
        upper_half = lax.index_in_dim(partial_gradient, 1, axis, keepdims=False)
        outgoing = jnp.where(upper, lower_half, upper_half)
        kept = jnp.where(upper, upper_half, lower_half)
        pairs = [(index, index ^ bit) for index in range(spread)]
        partial_gradient = kept + lax.ppermute(outgoing, "src", pairs)
        axes.remove(bit)
    gradient = partial_gradient.reshape(-1) * factor
    return (forward_field, adjoint_field, gradient)


def solution(mesh):
    in_specs = (
        P("src"),
        P("leaf"),
        P("src", "leaf"),
        P("leaf", None),
        P("leaf", None),
        P("leaf", None),
        P("leaf", None, None),
        P("leaf", None),
        P("leaf", None),
        P("leaf", None, None),
        P("leaf", None, None),
        P("leaf", None, None),
    )
    out_specs = (P("src", "leaf"), P("src", "leaf"), P(("leaf", "src")))
    return jax.shard_map(shards, mesh=mesh, in_specs=in_specs, out_specs=out_specs, check_vma=False)
```
